32 devices in a mesh: gx: 8 (over z, y), gy: 4 (over x, core).
Axes of the slice: x: 2, y: 2, z: 4, core: 2. Of those that a mesh axis runs over, the one named last changes fastest.
Arguments:
- records: bfloat16 [128, 8, 8192], P('gx', 'gy')
- kept_bins: int32 [1024], replicated, may hold values from 1 to 4095, as said below
- pair_offsets: int32 [128], replicated, may hold values from 1 to 128, as said below
Outputs:
- correlation: bfloat16 [128, 128, 512], P('gy', 'gx')
The draws below stay inside these ranges and needn't reach their ends.
Inputs may be any that keep to these rules, and one draw needn't show every extreme that they name: `kept_bins`: 1024 different bin indices in increasing order, both 1 and 4095 among them. `pair_offsets`: each offset from 1 to 128 exactly once, in any order.
All inputs are finite; a program needn't handle non-finite values.
Results may differ from the reference program's by a relative error of at most 0.0075.
Values may be sent and summed in bfloat16 or wider, within the bound.
No kernel may reach another device: no remote copies, remote signals or barrier semaphores. Data moves between devices by JAX's collectives and lax.ppermute only.
A program may use at most 64 MiB of HBM per device.

```python
import math
import jax
import jax.numpy as jnp
from jax import lax

SAMPLES = 8192
BINS = 1024
OFFSETS = 128
LAGS = 512
CHANNELS = 128
WINDOWS = 8


def draw_records(key, part):
    key_noise, key_tilt, key_scale = jax.random.split(key, 3)
    grid_shape = (CHANNELS, WINDOWS, SAMPLES)
    random_part = jax.random.normal(key_noise, grid_shape, jnp.float32)
    spread = math.log(10.0)
    tilt_coef = jax.random.uniform(key_tilt, (CHANNELS, WINDOWS, 1), jnp.float32, -0.8, 0.8)
    scales = jnp.exp(jax.random.uniform(key_scale, (CHANNELS, WINDOWS, 1), jnp.float32, 0.0, spread))
    return (scales * (random_part + tilt_coef * jnp.roll(random_part, 1, axis=2))).astype(jnp.bfloat16)


def draw_kept_bins(key, part):
    half_count = SAMPLES // 2
    shuffled = jax.random.permutation(key, half_count - 3) + 2
    chosen = jnp.concatenate([jnp.array([1, half_count - 1], jnp.int32), shuffled[:BINS - 2].astype(jnp.int32)])
    return jnp.sort(chosen)


def draw_pair_offsets(key, part):
    return (jax.random.permutation(key, OFFSETS) + 1).astype(jnp.int32)


def setup_inputs(seed: int = 0) -> dict:
    splits = jax.random.split(jax.random.key(seed), 4)
    records = draw_records(jax.random.fold_in(splits[3], 71), 0)
    kept_bins = draw_kept_bins(jax.random.fold_in(splits[3], 71), 0)
    pair_offsets = draw_pair_offsets(jax.random.fold_in(splits[3], 71), 0)
    return {"records": records, "kept_bins": kept_bins, "pair_offsets": pair_offsets}


def forward_table(kept_bins, first_sample, sample_count):
    sample_index = first_sample + jnp.arange(sample_count, dtype=jnp.int32)
    angles = jnp.mod(sample_index[:, None] * kept_bins[None, :], SAMPLES).astype(jnp.float32) * (2.0 * math.pi / SAMPLES)
    return jnp.concatenate([jnp.cos(angles), -jnp.sin(angles)], axis=1).astype(jnp.bfloat16)

def inverse_table(kept_bins):
    lag_index = jnp.arange(LAGS, dtype=jnp.int32) - LAGS // 2
    angles = jnp.mod(kept_bins[:, None] * lag_index[None, :], SAMPLES).astype(jnp.float32) * (2.0 * math.pi / SAMPLES)
    return jnp.stack([jnp.cos(angles), -jnp.sin(angles)], axis=0).astype(jnp.bfloat16)

def whiten(spectra):
    mean_power = lax.optimization_barrier(jnp.mean(spectra * spectra, axis=-1, keepdims=True))
    return (spectra * lax.rsqrt(mean_power + 1e-06)).astype(jnp.bfloat16)

def reference(records, kept_bins, pair_offsets):
    record_rows = records.reshape(CHANNELS * WINDOWS, SAMPLES)
    spectra = jnp.dot(record_rows, forward_table(kept_bins, 0, SAMPLES), preferred_element_type=jnp.float32)
    white = whiten(spectra).reshape(CHANNELS, WINDOWS, 2, BINS)
    padded = jnp.concatenate([white, jnp.zeros((OFFSETS, WINDOWS, 2, BINS), jnp.bfloat16)], axis=0)
    inverse = inverse_table(kept_bins).astype(jnp.float32)
    norm_scale = 0.5 / math.sqrt(WINDOWS * BINS)
    block_rows = math.gcd(CHANNELS, 128)
    index_grid = jnp.arange(block_rows, dtype=jnp.int32)[:, None] + pair_offsets[None, :].astype(jnp.int32)

    def one_block(block_start):
        own_rows = lax.dynamic_slice_in_dim(white, block_start, block_rows, 0).astype(jnp.float32)
        near_rows = lax.dynamic_slice_in_dim(padded, block_start, block_rows + OFFSETS, 0)

        def add_window(running, window):
            own_part = own_rows[:, window]
            theirs = near_rows[:, window][index_grid].astype(jnp.float32)
            real_part = own_part[:, None, 0] * theirs[:, :, 0] + own_part[:, None, 1] * theirs[:, :, 1]
            imag_part = own_part[:, None, 1] * theirs[:, :, 0] - own_part[:, None, 0] * theirs[:, :, 1]
            return (running + jnp.stack([real_part, imag_part], axis=2), None)
        cross_sum, _ = lax.scan(add_window, jnp.zeros((block_rows, OFFSETS, 2, BINS), jnp.float32), jnp.arange(WINDOWS, dtype=jnp.int32))
        cross_sum = cross_sum.astype(jnp.bfloat16).astype(jnp.float32)
        lagged = jnp.einsum('copk,pkl->col', cross_sum, inverse) * norm_scale
        return lagged.astype(jnp.bfloat16)
    starts = jnp.arange(CHANNELS // block_rows, dtype=jnp.int32) * block_rows
    results = lax.map(one_block, starts).reshape(CHANNELS, OFFSETS, LAGS)
    return jnp.transpose(results, (1, 0, 2))
```

```python
import math

import jax
import jax.numpy as jnp
from jax import lax
from jax.sharding import PartitionSpec as P

SAMPLES = 8192
LAGS = 512


def inverse_table(kept_bins):
    lag_index = jnp.arange(LAGS, dtype=jnp.int32) - LAGS // 2
    angles = jnp.mod(kept_bins[:, None] * lag_index[None, :], SAMPLES).astype(jnp.float32) * (
        2.0 * math.pi / SAMPLES
    )
    return jnp.stack([jnp.cos(angles), -jnp.sin(angles)], axis=0).astype(jnp.bfloat16)


def whiten(spectra):
    mean_power = jnp.mean(spectra * spectra, axis=-1, keepdims=True)
    return (spectra * lax.rsqrt(mean_power + 1e-06)).astype(jnp.bfloat16)


def add_cross(running, window_block, my_offsets, own_count):
    group_size = math.gcd(8, my_offsets.shape[0])
    own_part = window_block[:, :own_count].astype(jnp.float32)

    def one_offset(shift_by):
        theirs = lax.dynamic_slice_in_dim(window_block, shift_by, own_count, 1).astype(jnp.float32)
        real_part = jnp.sum(
            own_part[:, :, 0] * theirs[:, :, 0] + own_part[:, :, 1] * theirs[:, :, 1], axis=0
        )
        imag_part = jnp.sum(
            own_part[:, :, 1] * theirs[:, :, 0] - own_part[:, :, 0] * theirs[:, :, 1], axis=0
        )
        return jnp.stack([real_part, imag_part], axis=1)

    def one_group(group_index, carried):
        chosen = lax.dynamic_slice_in_dim(my_offsets, group_index * group_size, group_size)
        update = jax.vmap(one_offset)(chosen)
        current = lax.dynamic_slice_in_dim(carried, group_index * group_size, group_size, 0)
        return lax.dynamic_update_slice_in_dim(
            carried, current + update, group_index * group_size, 0
        )

    return lax.fori_loop(0, my_offsets.shape[0] // group_size, one_group, running)


def small_table(kept_bins, rows):
    fine_count = 1 << ((rows.bit_length() - 1) // 2)
    coarse_count = rows // fine_count

    def angles(step, count):
        index = step * jnp.arange(count, dtype=jnp.int32)
        return jnp.mod(index[:, None] * kept_bins[None, :], SAMPLES).astype(jnp.float32) * (
            2.0 * math.pi / SAMPLES
        )

    fine = angles(1, fine_count)[None, :, :]
    coarse = angles(fine_count, coarse_count)[:, None, :]
    cos_f, sin_f, cos_c, sin_c = jnp.cos(fine), jnp.sin(fine), jnp.cos(coarse), jnp.sin(coarse)
    cos_t = cos_f * cos_c - sin_f * sin_c
    sin_t = sin_f * cos_c + cos_f * sin_c
    table = jnp.concatenate([cos_t, -sin_t], axis=-1)
    return table.reshape(rows, 2 * kept_bins.shape[0]).astype(jnp.bfloat16)


def forward_spectra(record_rows, kept_bins):
    row_count, samples = record_rows.shape
    bin_count = kept_bins.shape[0]
    block_len = math.gcd(samples, 1024)
    block_count = samples // block_len
    x = record_rows.reshape(row_count, block_count, block_len).astype(jnp.float32)
    br = jnp.mod(
        jnp.arange(block_count, dtype=jnp.int32)[:, None] * jnp.arange(block_count, dtype=jnp.int32)[None, :],
        block_count,
    ).astype(jnp.float32) * (2.0 * math.pi / block_count)
    twiddle = jnp.stack([jnp.cos(br), -jnp.sin(br)], axis=0)
    y = jnp.einsum("ubs,pbr->prus", x, twiddle, precision=lax.Precision.HIGHEST)
    y_hi = y.astype(jnp.bfloat16)
    y_lo = (y - y_hi.astype(jnp.float32)).astype(jnp.bfloat16)
    lhs = jnp.stack([y_hi, y_lo], axis=0).reshape(-1, block_len)
    prod = jnp.dot(lhs, small_table(kept_bins, block_len), preferred_element_type=jnp.float32)
    prod = prod.reshape(2, 2, block_count, row_count, 2, bin_count)
    prod = prod[0] + prod[1]
    pick = (
        jnp.mod(kept_bins, block_count)[None, None, :]
        == jnp.arange(block_count, dtype=jnp.int32)[:, None, None]
    ).astype(jnp.float32)
    real_part = jnp.sum(pick * (prod[0, :, :, 0] - prod[1, :, :, 1]), axis=0)
    imag_part = jnp.sum(pick * (prod[0, :, :, 1] + prod[1, :, :, 0]), axis=0)
    return jnp.concatenate([real_part, imag_part], axis=-1)


def local(records, kept_bins, pair_offsets):
    ch_dev, win_dev, samples = records.shape
    bin_count = kept_bins.shape[0]
    band_span = pair_offsets.shape[0]
    record_rows = jnp.transpose(records, (1, 0, 2)).reshape(win_dev * ch_dev, samples)
    spectra = forward_spectra(record_rows, kept_bins)
    white = whiten(spectra).reshape(win_dev, ch_dev, 2, bin_count)
    off_dev = band_span // lax.axis_size("gy")
    my_offsets = lax.dynamic_slice_in_dim(pair_offsets, lax.axis_index("gy") * off_dev, off_dev)
    inverse = inverse_table(kept_bins)
    norm_scale = 0.5 / math.sqrt(win_dev * lax.axis_size("gy") * bin_count)
    freq_white = lax.all_to_all(white, "gx", split_axis=3, concat_axis=1, tiled=True)
    all_channels = freq_white.shape[1]
    empty_sum = jnp.zeros((off_dev, all_channels, 2, freq_white.shape[3]), jnp.float32)
    window_block = lax.all_gather(freq_white, "gy", axis=0, tiled=True)
    widened = jnp.concatenate(
        [
            window_block,
            jnp.zeros(
                (window_block.shape[0], band_span, 2, window_block.shape[3]), window_block.dtype
            ),
        ],
        axis=1,
    )
    cross_sum = add_cross(empty_sum, widened, my_offsets, all_channels).astype(jnp.bfloat16)
    lagged = (
        jnp.einsum(
            "ocpk,pkl->ocl",
            lax.all_to_all(cross_sum, "gx", split_axis=1, concat_axis=3, tiled=True),
            inverse,
            preferred_element_type=jnp.float32,
        )
        * norm_scale
    )
    return lagged.astype(jnp.bfloat16)


def solution(mesh):
    return jax.shard_map(
        local,
        mesh=mesh,
        in_specs=(P("gx", "gy", None), P(), P()),
        out_specs=P("gy", "gx", None),
        check_vma=False,
    )
```

```python
import math

import jax
import jax.numpy as jnp
from jax import lax
from jax.sharding import PartitionSpec as P

SAMPLES = 8192
LAGS = 512


def inverse_table(kept_bins):
    lag_index = jnp.arange(LAGS, dtype=jnp.int32) - LAGS // 2
    angles = jnp.mod(kept_bins[:, None] * lag_index[None, :], SAMPLES).astype(jnp.float32) * (
        2.0 * math.pi / SAMPLES
    )
    return jnp.stack([jnp.cos(angles), -jnp.sin(angles)], axis=0).astype(jnp.bfloat16)


def whiten(spectra):
    mean_power = jnp.mean(spectra * spectra, axis=-1, keepdims=True)
    return (spectra * lax.rsqrt(mean_power + 1e-06)).astype(jnp.bfloat16)


def add_cross(running, window_block, my_offsets, own_count):
    group_size = math.gcd(8, my_offsets.shape[0])
    own_part = window_block[:, :own_count].astype(jnp.float32)

    def one_offset(shift_by):
        theirs = lax.dynamic_slice_in_dim(window_block, shift_by, own_count, 1).astype(jnp.float32)
        real_part = jnp.sum(
            own_part[:, :, 0] * theirs[:, :, 0] + own_part[:, :, 1] * theirs[:, :, 1], axis=0
        )
        imag_part = jnp.sum(
            own_part[:, :, 1] * theirs[:, :, 0] - own_part[:, :, 0] * theirs[:, :, 1], axis=0
        )
        return jnp.stack([real_part, imag_part], axis=1)

    def one_group(group_index, carried):
        chosen = lax.dynamic_slice_in_dim(my_offsets, group_index * group_size, group_size)
        update = jax.vmap(one_offset)(chosen)
        current = lax.dynamic_slice_in_dim(carried, group_index * group_size, group_size, 0)
        return lax.dynamic_update_slice_in_dim(
            carried, current + update, group_index * group_size, 0
        )

    return lax.fori_loop(0, my_offsets.shape[0] // group_size, one_group, running)


def small_table(kept_bins, rows):
    fine_count = 1 << ((rows.bit_length() - 1) // 2)
    coarse_count = rows // fine_count

    def angles(step, count):
        index = step * jnp.arange(count, dtype=jnp.int32)
        return jnp.mod(index[:, None] * kept_bins[None, :], SAMPLES).astype(jnp.float32) * (
            2.0 * math.pi / SAMPLES
        )

    fine = angles(1, fine_count)[None, :, :]
    coarse = angles(fine_count, coarse_count)[:, None, :]
    cos_f, sin_f, cos_c, sin_c = jnp.cos(fine), jnp.sin(fine), jnp.cos(coarse), jnp.sin(coarse)
    cos_t = cos_f * cos_c - sin_f * sin_c
    sin_t = sin_f * cos_c + cos_f * sin_c
    table = jnp.concatenate([cos_t, -sin_t], axis=-1)
    return table.reshape(rows, 2 * kept_bins.shape[0]).astype(jnp.bfloat16)


def forward_spectra(record_rows, kept_bins):
    row_count, samples = record_rows.shape
    bin_count = kept_bins.shape[0]
    block_count = 4
    block_len = samples // block_count
    x = record_rows.reshape(row_count, block_count, block_len).astype(jnp.float32)
    br = jnp.mod(
        jnp.arange(block_count, dtype=jnp.int32)[:, None] * jnp.arange(block_count, dtype=jnp.int32)[None, :],
        block_count,
    ).astype(jnp.float32) * (2.0 * math.pi / block_count)
    twiddle = jnp.round(jnp.stack([jnp.cos(br), -jnp.sin(br)], axis=0))
    y = jnp.einsum("ubs,pbr->prus", x, twiddle, precision=lax.Precision.HIGHEST)
    y_hi = y.astype(jnp.bfloat16)
    y_lo = (y - y_hi.astype(jnp.float32)).astype(jnp.bfloat16)
    lhs = jnp.stack([y_hi, y_lo], axis=0).reshape(-1, block_len)
    prod = jnp.dot(lhs, small_table(kept_bins, block_len), preferred_element_type=jnp.float32)
    prod = prod.reshape(2, 2, block_count, row_count, 2, bin_count)
    prod = prod[0] + prod[1]
    pick = (
        jnp.mod(kept_bins, block_count)[None, None, :]
        == jnp.arange(block_count, dtype=jnp.int32)[:, None, None]
    ).astype(jnp.float32)
    real_part = jnp.sum(pick * (prod[0, :, :, 0] - prod[1, :, :, 1]), axis=0)
    imag_part = jnp.sum(pick * (prod[0, :, :, 1] + prod[1, :, :, 0]), axis=0)
    return jnp.concatenate([real_part, imag_part], axis=-1)


def local(records, kept_bins, pair_offsets):
    ch_dev, win_dev, samples = records.shape
    bin_count = kept_bins.shape[0]
    band_span = pair_offsets.shape[0]
    record_rows = jnp.transpose(records, (1, 0, 2)).reshape(win_dev * ch_dev, samples)
    spectra = forward_spectra(record_rows, kept_bins)
    white = whiten(spectra).reshape(win_dev, ch_dev, 2, bin_count)
    off_dev = band_span // lax.axis_size("gy")
    my_offsets = lax.dynamic_slice_in_dim(pair_offsets, lax.axis_index("gy") * off_dev, off_dev)
    inverse = inverse_table(kept_bins)
    norm_scale = 0.5 / math.sqrt(win_dev * lax.axis_size("gy") * bin_count)
    freq_white = lax.all_to_all(white, "gx", split_axis=3, concat_axis=1, tiled=True)
    all_channels = freq_white.shape[1]
    empty_sum = jnp.zeros((off_dev, all_channels, 2, freq_white.shape[3]), jnp.float32)
    window_block = lax.all_gather(freq_white, "gy", axis=0, tiled=True)
    widened = jnp.concatenate(
        [
            window_block,
            jnp.zeros(
                (window_block.shape[0], band_span, 2, window_block.shape[3]), window_block.dtype
            ),
        ],
        axis=1,
    )
    cross_sum = add_cross(empty_sum, widened, my_offsets, all_channels).astype(jnp.bfloat16)
    lagged = (
        jnp.einsum(
            "ocpk,pkl->ocl",
            lax.all_to_all(cross_sum, "gx", split_axis=1, concat_axis=3, tiled=True),
            inverse,
            preferred_element_type=jnp.float32,
        )
        * norm_scale
    )
    return lagged.astype(jnp.bfloat16)


def solution(mesh):
    return jax.shard_map(
        local,
        mesh=mesh,
        in_specs=(P("gx", "gy", None), P(), P()),
        out_specs=P("gy", "gx", None),
        check_vma=False,
    )
```

```python
import math

import jax
import jax.numpy as jnp
from jax import lax
from jax.sharding import PartitionSpec as P

SAMPLES = 8192
LAGS = 512


def inverse_table(kept_bins):
    lag_index = jnp.arange(LAGS, dtype=jnp.int32) - LAGS // 2
    angles = jnp.mod(kept_bins[:, None] * lag_index[None, :], SAMPLES).astype(jnp.float32) * (
        2.0 * math.pi / SAMPLES
    )
    return jnp.stack([jnp.cos(angles), -jnp.sin(angles)], axis=0).astype(jnp.bfloat16)


def whiten(spectra):
    mean_power = jnp.mean(spectra * spectra, axis=-1, keepdims=True)
    return (spectra * lax.rsqrt(mean_power + 1e-06)).astype(jnp.bfloat16)


def add_cross(running, window_block, my_offsets, own_count):
    group_size = math.gcd(8, my_offsets.shape[0])
    own_part = window_block[:, :own_count].astype(jnp.float32)

    def one_offset(shift_by):
        theirs = lax.dynamic_slice_in_dim(window_block, shift_by, own_count, 1).astype(jnp.float32)
        real_part = jnp.sum(
            own_part[:, :, 0] * theirs[:, :, 0] + own_part[:, :, 1] * theirs[:, :, 1], axis=0
        )
        imag_part = jnp.sum(
            own_part[:, :, 1] * theirs[:, :, 0] - own_part[:, :, 0] * theirs[:, :, 1], axis=0
        )
        return jnp.stack([real_part, imag_part], axis=1)

    def one_group(group_index, carried):
        chosen = lax.dynamic_slice_in_dim(my_offsets, group_index * group_size, group_size)
        update = jax.vmap(one_offset)(chosen)
        current = lax.dynamic_slice_in_dim(carried, group_index * group_size, group_size, 0)
        return lax.dynamic_update_slice_in_dim(
            carried, current + update, group_index * group_size, 0
        )

    return lax.fori_loop(0, my_offsets.shape[0] // group_size, one_group, running)


def small_table(kept_bins, rows):
    fine_count = 1 << ((rows.bit_length() - 1) // 2)
    coarse_count = rows // fine_count

    def angles(step, count):
        index = step * jnp.arange(count, dtype=jnp.int32)
        return jnp.mod(index[:, None] * kept_bins[None, :], SAMPLES).astype(jnp.float32) * (
            2.0 * math.pi / SAMPLES
        )

    fine = angles(1, fine_count)[None, :, :]
    coarse = angles(fine_count, coarse_count)[:, None, :]
    cos_f, sin_f, cos_c, sin_c = jnp.cos(fine), jnp.sin(fine), jnp.cos(coarse), jnp.sin(coarse)
    cos_t = cos_f * cos_c - sin_f * sin_c
    sin_t = sin_f * cos_c + cos_f * sin_c
    table = jnp.concatenate([cos_t, -sin_t], axis=-1)
    return table.reshape(rows, 2 * kept_bins.shape[0]).astype(jnp.bfloat16)


def forward_spectra(record_rows, kept_bins):
    row_count, samples = record_rows.shape
    bin_count = kept_bins.shape[0]
    block_count = 4
    block_len = samples // block_count
    lhs = jnp.transpose(record_rows.reshape(row_count, block_count, block_len), (1, 0, 2))
    prod = jnp.dot(
        lhs.reshape(block_count * row_count, block_len),
        small_table(kept_bins, block_len),
        preferred_element_type=jnp.float32,
    ).reshape(block_count, row_count, 2, bin_count)
    turns = jnp.mod(
        jnp.arange(block_count, dtype=jnp.int32)[:, None] * jnp.mod(kept_bins, block_count)[None, :],
        block_count,
    ).astype(jnp.float32) * (2.0 * math.pi / block_count)
    tw_re = jnp.round(jnp.cos(turns))[:, None, :]
    tw_im = jnp.round(-jnp.sin(turns))[:, None, :]
    p_re, p_im = prod[:, :, 0], prod[:, :, 1]
    real_part = jnp.sum(tw_re * p_re - tw_im * p_im, axis=0)
    imag_part = jnp.sum(tw_re * p_im + tw_im * p_re, axis=0)
    return jnp.concatenate([real_part, imag_part], axis=-1)


def local(records, kept_bins, pair_offsets):
    ch_dev, win_dev, samples = records.shape
    bin_count = kept_bins.shape[0]
    band_span = pair_offsets.shape[0]
    record_rows = jnp.transpose(records, (1, 0, 2)).reshape(win_dev * ch_dev, samples)
    spectra = forward_spectra(record_rows, kept_bins)
    white = whiten(spectra).reshape(win_dev, ch_dev, 2, bin_count)
    off_dev = band_span // lax.axis_size("gy")
    my_offsets = lax.dynamic_slice_in_dim(pair_offsets, lax.axis_index("gy") * off_dev, off_dev)
    inverse = inverse_table(kept_bins)
    norm_scale = 0.5 / math.sqrt(win_dev * lax.axis_size("gy") * bin_count)
    freq_white = lax.all_to_all(white, "gx", split_axis=3, concat_axis=1, tiled=True)
    all_channels = freq_white.shape[1]
    empty_sum = jnp.zeros((off_dev, all_channels, 2, freq_white.shape[3]), jnp.float32)
    window_block = lax.all_gather(freq_white, "gy", axis=0, tiled=True)
    widened = jnp.concatenate(
        [
            window_block,
            jnp.zeros(
                (window_block.shape[0], band_span, 2, window_block.shape[3]), window_block.dtype
            ),
        ],
        axis=1,
    )
    cross_sum = add_cross(empty_sum, widened, my_offsets, all_channels).astype(jnp.bfloat16)
    lagged = (
        jnp.einsum(
            "ocpk,pkl->ocl",
            lax.all_to_all(cross_sum, "gx", split_axis=1, concat_axis=3, tiled=True),
            inverse,
            preferred_element_type=jnp.float32,
        )
        * norm_scale
    )
    return lagged.astype(jnp.bfloat16)


def solution(mesh):
    return jax.shard_map(
        local,
        mesh=mesh,
        in_specs=(P("gx", "gy", None), P(), P()),
        out_specs=P("gy", "gx", None),
        check_vma=False,
    )
```

```python
import functools
import math

import jax
import jax.numpy as jnp
from jax import lax
from jax.experimental import pallas as pl
from jax.experimental.pallas import tpu as pltpu
from jax.sharding import PartitionSpec as P

SAMPLES = 8192
LAGS = 512


def inverse_table(kept_bins):
    lag_index = jnp.arange(LAGS, dtype=jnp.int32) - LAGS // 2
    angles = jnp.mod(kept_bins[:, None] * lag_index[None, :], SAMPLES).astype(jnp.float32) * (
        2.0 * math.pi / SAMPLES
    )
    return jnp.stack([jnp.cos(angles), -jnp.sin(angles)], axis=0).astype(jnp.bfloat16)


def whiten(spectra):
    mean_power = jnp.mean(spectra * spectra, axis=-1, keepdims=True)
    return (spectra * lax.rsqrt(mean_power + 1e-06)).astype(jnp.bfloat16)


def cross_kernel(offsets_ref, base_ref, white_ref, out_ref, *, group, own_count, half):
    step = pl.program_id(0)
    base = base_ref[0]
    own = [white_ref[base + c].astype(jnp.float32) for c in range(own_count)]

    def one_offset(i, carry):
        shift = offsets_ref[step * group + i]
        for c in range(own_count):
            a = own[c]
            b = white_ref[base + c + shift].astype(jnp.float32)
            ar, ai, br, bi = a[:half], a[half:], b[:half], b[half:]
            out_ref[i, 0, pl.ds(c, 1), :] = jnp.sum(ar * br + ai * bi, axis=0, keepdims=True)
            out_ref[i, 1, pl.ds(c, 1), :] = jnp.sum(ai * br - ar * bi, axis=0, keepdims=True)
        return carry

    lax.fori_loop(0, group, one_offset, 0)


def cross_spectra(white_all, pair_offsets, base, own_count):
    rows, bins = white_all.shape[1], white_all.shape[2]
    band_span = pair_offsets.shape[0]
    group = math.gcd(band_span, 8)
    kernel = functools.partial(cross_kernel, group=group, own_count=own_count, half=rows // 2)
    return pl.pallas_call(
        kernel,
        grid_spec=pltpu.PrefetchScalarGridSpec(
            num_scalar_prefetch=2,
            grid=(band_span // group,),
            in_specs=[pl.BlockSpec(white_all.shape, lambda g, offs, b: (0, 0, 0))],
            out_specs=pl.BlockSpec((group, 2, own_count, bins), lambda g, offs, b: (g, 0, 0, 0)),
        ),
        out_shape=jax.ShapeDtypeStruct((band_span, 2, own_count, bins), jnp.float32),
        compiler_params=pltpu.CompilerParams(vmem_limit_bytes=48 * 1024 * 1024),
        cost_estimate=pl.CostEstimate(
            flops=8 * band_span * own_count * rows * bins,
            transcendentals=0,
            bytes_accessed=white_all.size * 2 + band_span * 2 * own_count * bins * 4,
        ),
    )(pair_offsets, base, white_all)


def small_table(kept_bins, rows):
    fine_count = 1 << ((rows.bit_length() - 1) // 2)
    coarse_count = rows // fine_count

    def angles(step, count):
        index = step * jnp.arange(count, dtype=jnp.int32)
        return jnp.mod(index[:, None] * kept_bins[None, :], SAMPLES).astype(jnp.float32) * (
            2.0 * math.pi / SAMPLES
        )

    fine = angles(1, fine_count)[None, :, :]
    coarse = angles(fine_count, coarse_count)[:, None, :]
    cos_f, sin_f, cos_c, sin_c = jnp.cos(fine), jnp.sin(fine), jnp.cos(coarse), jnp.sin(coarse)
    cos_t = cos_f * cos_c - sin_f * sin_c
    sin_t = sin_f * cos_c + cos_f * sin_c
    table = jnp.concatenate([cos_t, -sin_t], axis=-1)
    return table.reshape(rows, 2 * kept_bins.shape[0]).astype(jnp.bfloat16)


def forward_spectra(record_rows, kept_bins):
    row_count, samples = record_rows.shape
    bin_count = kept_bins.shape[0]
    block_count = 4
    block_len = samples // block_count
    lhs = jnp.transpose(record_rows.reshape(row_count, block_count, block_len), (1, 0, 2))
    prod = jnp.dot(
        lhs.reshape(block_count * row_count, block_len),
        small_table(kept_bins, block_len),
        preferred_element_type=jnp.float32,
    ).reshape(block_count, row_count, 2, bin_count)
    turns = jnp.mod(
        jnp.arange(block_count, dtype=jnp.int32)[:, None] * jnp.mod(kept_bins, block_count)[None, :],
        block_count,
    ).astype(jnp.float32) * (2.0 * math.pi / block_count)
    tw_re = jnp.round(jnp.cos(turns))[:, None, :]
    tw_im = jnp.round(-jnp.sin(turns))[:, None, :]
    p_re, p_im = prod[:, :, 0], prod[:, :, 1]
    real_part = jnp.sum(tw_re * p_re - tw_im * p_im, axis=0)
    imag_part = jnp.sum(tw_re * p_im + tw_im * p_re, axis=0)
    return jnp.concatenate([real_part, imag_part], axis=-1)


def local(records, kept_bins, pair_offsets):
    ch_dev, win_dev, samples = records.shape
    bin_count = kept_bins.shape[0]
    band_span = pair_offsets.shape[0]
    record_rows = jnp.transpose(records, (1, 0, 2)).reshape(win_dev * ch_dev, samples)
    spectra = forward_spectra(record_rows, kept_bins)
    white = whiten(spectra).reshape(win_dev, ch_dev, 2, bin_count)
    freq_white = lax.all_to_all(white, "gy", split_axis=3, concat_axis=0, tiled=True)
    windows = freq_white.shape[0]
    shard_bins = freq_white.shape[3]
    rows_white = jnp.transpose(freq_white, (1, 2, 0, 3)).reshape(ch_dev, 2 * windows, shard_bins)
    all_white = lax.all_gather(rows_white, "gx", axis=0, tiled=True)
    padded = jnp.concatenate(
        [all_white, jnp.zeros((band_span,) + all_white.shape[1:], all_white.dtype)], axis=0
    )
    base = (lax.axis_index("gx") * ch_dev).astype(jnp.int32).reshape(1)
    cross = cross_spectra(padded, pair_offsets.astype(jnp.int32), base, ch_dev).astype(jnp.bfloat16)
    cross = lax.all_to_all(cross, "gy", split_axis=0, concat_axis=3, tiled=True)
    inverse = inverse_table(kept_bins)
    norm_scale = 0.5 / math.sqrt(windows * bin_count)
    lagged = (
        jnp.einsum("opck,pkl->ocl", cross, inverse, preferred_element_type=jnp.float32) * norm_scale
    )
    return lagged.astype(jnp.bfloat16)


def solution(mesh):
    return jax.shard_map(
        local,
        mesh=mesh,
        in_specs=(P("gx", "gy", None), P(), P()),
        out_specs=P("gy", "gx", None),
        check_vma=False,
    )
```

```python
import functools
import math

import jax
import jax.numpy as jnp
from jax import lax
from jax.experimental import pallas as pl
from jax.experimental.pallas import tpu as pltpu
from jax.sharding import PartitionSpec as P

SAMPLES = 8192
LAGS = 512


def inverse_table(kept_bins):
    fine_count = 32
    coarse_count = LAGS // fine_count

    def angles(index):
        return jnp.mod(kept_bins[:, None] * index[None, :], SAMPLES).astype(jnp.float32) * (
            2.0 * math.pi / SAMPLES
        )

    fine = angles(jnp.arange(fine_count, dtype=jnp.int32))[:, None, :]
    coarse = angles(fine_count * jnp.arange(coarse_count, dtype=jnp.int32) - LAGS // 2)[:, :, None]
    cos_f, sin_f, cos_c, sin_c = jnp.cos(fine), jnp.sin(fine), jnp.cos(coarse), jnp.sin(coarse)
    cos_t = (cos_f * cos_c - sin_f * sin_c).reshape(kept_bins.shape[0], LAGS)
    sin_t = (sin_f * cos_c + cos_f * sin_c).reshape(kept_bins.shape[0], LAGS)
    return jnp.stack([cos_t, -sin_t], axis=0).astype(jnp.bfloat16)


def whiten(spectra):
    mean_power = jnp.mean(spectra * spectra, axis=-1, keepdims=True)
    return (spectra * lax.rsqrt(mean_power + 1e-06)).astype(jnp.bfloat16)


def cross_kernel(offsets_ref, base_ref, white_ref, out_ref, *, group, own_count, half):
    step = pl.program_id(0)
    base = base_ref[0]
    own = [white_ref[base + c].astype(jnp.float32) for c in range(own_count)]

    def one_offset(i, carry):
        shift = offsets_ref[step * group + i]
        for c in range(own_count):
            a = own[c]
            b = white_ref[base + c + shift].astype(jnp.float32)
            ar, ai, br, bi = a[:half], a[half:], b[:half], b[half:]
            out_ref[i, 0, pl.ds(c, 1), :] = jnp.sum(ar * br + ai * bi, axis=0, keepdims=True)
            out_ref[i, 1, pl.ds(c, 1), :] = jnp.sum(ai * br - ar * bi, axis=0, keepdims=True)
        return carry

    lax.fori_loop(0, group, one_offset, 0)


def cross_spectra(white_all, pair_offsets, base, own_count):
    rows, bins = white_all.shape[1], white_all.shape[2]
    band_span = pair_offsets.shape[0]
    group = math.gcd(band_span, 8)
    kernel = functools.partial(cross_kernel, group=group, own_count=own_count, half=rows // 2)
    return pl.pallas_call(
        kernel,
        grid_spec=pltpu.PrefetchScalarGridSpec(
            num_scalar_prefetch=2,
            grid=(band_span // group,),
            in_specs=[pl.BlockSpec(white_all.shape, lambda g, offs, b: (0, 0, 0))],
            out_specs=pl.BlockSpec((group, 2, own_count, bins), lambda g, offs, b: (g, 0, 0, 0)),
        ),
        out_shape=jax.ShapeDtypeStruct((band_span, 2, own_count, bins), jnp.float32),
        compiler_params=pltpu.CompilerParams(vmem_limit_bytes=48 * 1024 * 1024),
        cost_estimate=pl.CostEstimate(
            flops=8 * band_span * own_count * rows * bins,
            transcendentals=0,
            bytes_accessed=white_all.size * 2 + band_span * 2 * own_count * bins * 4,
        ),
    )(pair_offsets, base, white_all)


def small_table(kept_bins, rows):
    fine_count = 1 << ((rows.bit_length() - 1) // 2)
    coarse_count = rows // fine_count

    def angles(step, count):
        index = step * jnp.arange(count, dtype=jnp.int32)
        return jnp.mod(index[:, None] * kept_bins[None, :], SAMPLES).astype(jnp.float32) * (
            2.0 * math.pi / SAMPLES
        )

    fine = angles(1, fine_count)[None, :, :]
    coarse = angles(fine_count, coarse_count)[:, None, :]
    cos_f, sin_f, cos_c, sin_c = jnp.cos(fine), jnp.sin(fine), jnp.cos(coarse), jnp.sin(coarse)
    cos_t = cos_f * cos_c - sin_f * sin_c
    sin_t = sin_f * cos_c + cos_f * sin_c
    table = jnp.concatenate([cos_t, -sin_t], axis=-1)
    return table.reshape(rows, 2 * kept_bins.shape[0]).astype(jnp.bfloat16)


def forward_spectra(record_rows, kept_bins):
    row_count, samples = record_rows.shape
    bin_count = kept_bins.shape[0]
    block_count = 4
    block_len = samples // block_count
    lhs = jnp.transpose(record_rows.reshape(row_count, block_count, block_len), (1, 0, 2))
    prod = jnp.dot(
        lhs.reshape(block_count * row_count, block_len),
        small_table(kept_bins, block_len),
        preferred_element_type=jnp.float32,
    ).reshape(block_count, row_count, 2, bin_count)
    turns = jnp.mod(
        jnp.arange(block_count, dtype=jnp.int32)[:, None] * jnp.mod(kept_bins, block_count)[None, :],
        block_count,
    ).astype(jnp.float32) * (2.0 * math.pi / block_count)
    tw_re = jnp.round(jnp.cos(turns))[:, None, :]
    tw_im = jnp.round(-jnp.sin(turns))[:, None, :]
    p_re, p_im = prod[:, :, 0], prod[:, :, 1]
    real_part = jnp.sum(tw_re * p_re - tw_im * p_im, axis=0)
    imag_part = jnp.sum(tw_re * p_im + tw_im * p_re, axis=0)
    return jnp.concatenate([real_part, imag_part], axis=-1)


def local(records, kept_bins, pair_offsets):
    ch_dev, win_dev, samples = records.shape
    bin_count = kept_bins.shape[0]
    band_span = pair_offsets.shape[0]
    record_rows = jnp.transpose(records, (1, 0, 2)).reshape(win_dev * ch_dev, samples)
    spectra = forward_spectra(record_rows, kept_bins)
    white = whiten(spectra).reshape(win_dev, ch_dev, 2, bin_count)
    freq_white = lax.all_to_all(white, "gy", split_axis=3, concat_axis=0, tiled=True)
    windows = freq_white.shape[0]
    shard_bins = freq_white.shape[3]
    rows_white = jnp.transpose(freq_white, (1, 2, 0, 3)).reshape(ch_dev, 2 * windows, shard_bins)
    all_white = lax.all_gather(rows_white, "gx", axis=0, tiled=True)
    padded = jnp.concatenate(
        [all_white, jnp.zeros((band_span,) + all_white.shape[1:], all_white.dtype)], axis=0
    )
    base = (lax.axis_index("gx") * ch_dev).astype(jnp.int32).reshape(1)
    gy_count = lax.axis_size("gy")
    halves = pair_offsets.astype(jnp.int32).reshape(gy_count, 2, band_span // (2 * gy_count))
    parts = []
    for h in range(2):
        part = cross_spectra(padded, halves[:, h].reshape(-1), base, ch_dev).astype(jnp.bfloat16)
        parts.append(lax.all_to_all(part, "gy", split_axis=0, concat_axis=3, tiled=True))
    cross = jnp.concatenate(parts, axis=0)
    inverse = inverse_table(kept_bins)
    norm_scale = 0.5 / math.sqrt(windows * bin_count)
    lagged = (
        jnp.einsum("opck,pkl->ocl", cross, inverse, preferred_element_type=jnp.float32) * norm_scale
    )
    return lagged.astype(jnp.bfloat16)


def solution(mesh):
    return jax.shard_map(
        local,
        mesh=mesh,
        in_specs=(P("gx", "gy", None), P(), P()),
        out_specs=P("gy", "gx", None),
        check_vma=False,
    )
```

```python
import functools
import math

import jax
import jax.numpy as jnp
from jax import lax
from jax.experimental import pallas as pl
from jax.experimental.pallas import tpu as pltpu
from jax.sharding import PartitionSpec as P

SAMPLES = 8192
LAGS = 512


def inverse_table(kept_bins):
    fine_count = 32
    coarse_count = LAGS // fine_count

    def angles(index):
        return jnp.mod(kept_bins[:, None] * index[None, :], SAMPLES).astype(jnp.float32) * (
            2.0 * math.pi / SAMPLES
        )

    fine = angles(jnp.arange(fine_count, dtype=jnp.int32))[:, None, :]
    coarse = angles(fine_count * jnp.arange(coarse_count, dtype=jnp.int32) - LAGS // 2)[:, :, None]
    cos_f, sin_f, cos_c, sin_c = jnp.cos(fine), jnp.sin(fine), jnp.cos(coarse), jnp.sin(coarse)
    cos_t = (cos_f * cos_c - sin_f * sin_c).reshape(kept_bins.shape[0], LAGS)
    sin_t = (sin_f * cos_c + cos_f * sin_c).reshape(kept_bins.shape[0], LAGS)
    return jnp.stack([cos_t, -sin_t], axis=0).astype(jnp.bfloat16)


def whiten(spectra):
    mean_power = jnp.mean(spectra * spectra, axis=-1, keepdims=True)
    return (spectra * lax.rsqrt(mean_power + 1e-06)).astype(jnp.bfloat16)


def cross_kernel(offsets_ref, base_ref, white_ref, out_ref, *, group, own_count, half):
    step = pl.program_id(0)
    base = base_ref[0]
    own = [white_ref[base + c].astype(jnp.float32) for c in range(own_count)]

    def one_offset(i, carry):
        shift = offsets_ref[step * group + i]
        for c in range(own_count):
            a = own[c]
            b = white_ref[base + c + shift].astype(jnp.float32)
            ar, ai, br, bi = a[:half], a[half:], b[:half], b[half:]
            out_ref[i, 0, pl.ds(c, 1), :] = jnp.sum(ar * br + ai * bi, axis=0, keepdims=True)
            out_ref[i, 1, pl.ds(c, 1), :] = jnp.sum(ai * br - ar * bi, axis=0, keepdims=True)
        return carry

    lax.fori_loop(0, group, one_offset, 0)


def cross_spectra(white_all, pair_offsets, base, own_count):
    rows, bins = white_all.shape[1], white_all.shape[2]
    band_span = pair_offsets.shape[0]
    group = math.gcd(band_span, 8)
    kernel = functools.partial(cross_kernel, group=group, own_count=own_count, half=rows // 2)
    return pl.pallas_call(
        kernel,
        grid_spec=pltpu.PrefetchScalarGridSpec(
            num_scalar_prefetch=2,
            grid=(band_span // group,),
            in_specs=[pl.BlockSpec(white_all.shape, lambda g, offs, b: (0, 0, 0))],
            out_specs=pl.BlockSpec((group, 2, own_count, bins), lambda g, offs, b: (g, 0, 0, 0)),
        ),
        out_shape=jax.ShapeDtypeStruct((band_span, 2, own_count, bins), jnp.float32),
        compiler_params=pltpu.CompilerParams(vmem_limit_bytes=48 * 1024 * 1024),
        cost_estimate=pl.CostEstimate(
            flops=8 * band_span * own_count * rows * bins,
            transcendentals=0,
            bytes_accessed=white_all.size * 2 + band_span * 2 * own_count * bins * 4,
        ),
    )(pair_offsets, base, white_all)


def small_table(kept_bins, rows):
    fine_count = 1 << ((rows.bit_length() - 1) // 2)
    coarse_count = rows // fine_count

    def angles(step, count):
        index = step * jnp.arange(count, dtype=jnp.int32)
        return jnp.mod(index[:, None] * kept_bins[None, :], SAMPLES).astype(jnp.float32) * (
            2.0 * math.pi / SAMPLES
        )

    fine = angles(1, fine_count)[None, :, :]
    coarse = angles(fine_count, coarse_count)[:, None, :]
    cos_f, sin_f, cos_c, sin_c = jnp.cos(fine), jnp.sin(fine), jnp.cos(coarse), jnp.sin(coarse)
    cos_t = cos_f * cos_c - sin_f * sin_c
    sin_t = sin_f * cos_c + cos_f * sin_c
    table = jnp.concatenate([cos_t, -sin_t], axis=-1)
    return table.reshape(rows, 2 * kept_bins.shape[0]).astype(jnp.bfloat16)


def forward_spectra(record_rows, kept_bins):
    row_count, samples = record_rows.shape
    bin_count = kept_bins.shape[0]
    block_count = 4
    block_len = samples // block_count
    lhs = jnp.transpose(record_rows.reshape(row_count, block_count, block_len), (1, 0, 2))
    prod = jnp.dot(
        lhs.reshape(block_count * row_count, block_len),
        small_table(kept_bins, block_len),
        preferred_element_type=jnp.float32,
    ).reshape(block_count, row_count, 2, bin_count)
    turns = jnp.mod(
        jnp.arange(block_count, dtype=jnp.int32)[:, None] * jnp.mod(kept_bins, block_count)[None, :],
        block_count,
    ).astype(jnp.float32) * (2.0 * math.pi / block_count)
    tw_re = jnp.round(jnp.cos(turns))[:, None, :]
    tw_im = jnp.round(-jnp.sin(turns))[:, None, :]
    p_re, p_im = prod[:, :, 0], prod[:, :, 1]
    real_part = jnp.sum(tw_re * p_re - tw_im * p_im, axis=0)
    imag_part = jnp.sum(tw_re * p_im + tw_im * p_re, axis=0)
    return jnp.concatenate([real_part, imag_part], axis=-1)


def local(records, kept_bins, pair_offsets):
    ch_dev, win_dev, samples = records.shape
    bin_count = kept_bins.shape[0]
    band_span = pair_offsets.shape[0]
    record_rows = jnp.transpose(records, (1, 0, 2)).reshape(win_dev * ch_dev, samples)
    spectra = forward_spectra(record_rows, kept_bins)
    white = whiten(spectra).reshape(win_dev, ch_dev, 2, bin_count)
    freq_white = lax.all_to_all(white, "gy", split_axis=3, concat_axis=0, tiled=True)
    windows = freq_white.shape[0]
    shard_bins = freq_white.shape[3]
    rows_white = jnp.transpose(freq_white, (1, 2, 0, 3)).reshape(ch_dev, 2 * windows, shard_bins)
    base = (lax.axis_index("gx") * ch_dev).astype(jnp.int32).reshape(1)
    half_bins = shard_bins // 2
    parts = []
    for h in range(2):
        own_half = rows_white[:, :, h * half_bins:(h + 1) * half_bins]
        all_white = lax.all_gather(own_half, "gx", axis=0, tiled=True)
        padded = jnp.concatenate(
            [all_white, jnp.zeros((band_span,) + all_white.shape[1:], all_white.dtype)], axis=0
        )
        part = cross_spectra(padded, pair_offsets.astype(jnp.int32), base, ch_dev).astype(jnp.bfloat16)
        parts.append(lax.all_to_all(part, "gy", split_axis=0, concat_axis=3, tiled=True))
    cross = jnp.concatenate(parts, axis=3)
    bin_order = jnp.transpose(kept_bins.reshape(-1, 2, half_bins), (1, 0, 2)).reshape(-1)
    inverse = inverse_table(bin_order)
    norm_scale = 0.5 / math.sqrt(windows * bin_count)
    lagged = (
        jnp.einsum("opck,pkl->ocl", cross, inverse, preferred_element_type=jnp.float32) * norm_scale
    )
    return lagged.astype(jnp.bfloat16)


def solution(mesh):
    return jax.shard_map(
        local,
        mesh=mesh,
        in_specs=(P("gx", "gy", None), P(), P()),
        out_specs=P("gy", "gx", None),
        check_vma=False,
    )
```

```python
import functools
import math

import jax
import jax.numpy as jnp
from jax import lax
from jax.experimental import pallas as pl
from jax.experimental.pallas import tpu as pltpu
from jax.sharding import PartitionSpec as P

SAMPLES = 8192
LAGS = 512


def inverse_table(kept_bins):
    fine_count = 32
    coarse_count = LAGS // fine_count

    def angles(index):
        return jnp.mod(kept_bins[:, None] * index[None, :], SAMPLES).astype(jnp.float32) * (
            2.0 * math.pi / SAMPLES
        )

    fine = angles(jnp.arange(fine_count, dtype=jnp.int32))[:, None, :]
    coarse = angles(fine_count * jnp.arange(coarse_count, dtype=jnp.int32) - LAGS // 2)[:, :, None]
    cos_f, sin_f, cos_c, sin_c = jnp.cos(fine), jnp.sin(fine), jnp.cos(coarse), jnp.sin(coarse)
    cos_t = (cos_f * cos_c - sin_f * sin_c).reshape(kept_bins.shape[0], LAGS)
    sin_t = (sin_f * cos_c + cos_f * sin_c).reshape(kept_bins.shape[0], LAGS)
    return jnp.stack([cos_t, -sin_t], axis=0).astype(jnp.bfloat16)


def whiten(spectra):
    mean_power = jnp.mean(spectra * spectra, axis=-1, keepdims=True)
    return (spectra * lax.rsqrt(mean_power + 1e-06)).astype(jnp.bfloat16)


def cross_kernel(offsets_ref, base_ref, white_ref, out_ref, *, group, own_count, half):
    step = pl.program_id(0)
    base = base_ref[0]
    own = [white_ref[base + c].astype(jnp.float32) for c in range(own_count)]

    def one_offset(i, carry):
        shift = offsets_ref[step * group + i]
        for c in range(own_count):
            a = own[c]
            b = white_ref[base + c + shift].astype(jnp.float32)
            ar, ai, br, bi = a[:half], a[half:], b[:half], b[half:]
            out_ref[i, 0, pl.ds(c, 1), :] = jnp.sum(ar * br + ai * bi, axis=0, keepdims=True)
            out_ref[i, 1, pl.ds(c, 1), :] = jnp.sum(ai * br - ar * bi, axis=0, keepdims=True)
        return carry

    lax.fori_loop(0, group, one_offset, 0)


def cross_spectra(white_all, pair_offsets, base, own_count):
    rows, bins = white_all.shape[1], white_all.shape[2]
    band_span = pair_offsets.shape[0]
    group = math.gcd(band_span, 8)
    kernel = functools.partial(cross_kernel, group=group, own_count=own_count, half=rows // 2)
    return pl.pallas_call(
        kernel,
        grid_spec=pltpu.PrefetchScalarGridSpec(
            num_scalar_prefetch=2,
            grid=(band_span // group,),
            in_specs=[pl.BlockSpec(white_all.shape, lambda g, offs, b: (0, 0, 0))],
            out_specs=pl.BlockSpec((group, 2, own_count, bins), lambda g, offs, b: (g, 0, 0, 0)),
        ),
        out_shape=jax.ShapeDtypeStruct((band_span, 2, own_count, bins), jnp.float32),
        compiler_params=pltpu.CompilerParams(vmem_limit_bytes=48 * 1024 * 1024),
        cost_estimate=pl.CostEstimate(
            flops=8 * band_span * own_count * rows * bins,
            transcendentals=0,
            bytes_accessed=white_all.size * 2 + band_span * 2 * own_count * bins * 4,
        ),
    )(pair_offsets, base, white_all)


def small_table(kept_bins, rows):
    fine_count = 1 << ((rows.bit_length() - 1) // 2)
    coarse_count = rows // fine_count

    def angles(step, count):
        index = step * jnp.arange(count, dtype=jnp.int32)
        return jnp.mod(index[:, None] * kept_bins[None, :], SAMPLES).astype(jnp.float32) * (
            2.0 * math.pi / SAMPLES
        )

    fine = angles(1, fine_count)[None, :, :]
    coarse = angles(fine_count, coarse_count)[:, None, :]
    cos_f, sin_f, cos_c, sin_c = jnp.cos(fine), jnp.sin(fine), jnp.cos(coarse), jnp.sin(coarse)
    cos_t = cos_f * cos_c - sin_f * sin_c
    sin_t = sin_f * cos_c + cos_f * sin_c
    table = jnp.concatenate([cos_t, -sin_t], axis=-1)
    return table.reshape(rows, 2 * kept_bins.shape[0]).astype(jnp.bfloat16)


def forward_spectra(record_rows, kept_bins):
    row_count, samples = record_rows.shape
    bin_count = kept_bins.shape[0]
    block_count = 4
    block_len = samples // block_count
    lhs = jnp.transpose(record_rows.reshape(row_count, block_count, block_len), (1, 0, 2))
    prod = jnp.dot(
        lhs.reshape(block_count * row_count, block_len),
        small_table(kept_bins, block_len),
        preferred_element_type=jnp.float32,
    ).reshape(block_count, row_count, 2, bin_count)
    turns = jnp.mod(
        jnp.arange(block_count, dtype=jnp.int32)[:, None] * jnp.mod(kept_bins, block_count)[None, :],
        block_count,
    ).astype(jnp.float32) * (2.0 * math.pi / block_count)
    tw_re = jnp.round(jnp.cos(turns))[:, None, :]
    tw_im = jnp.round(-jnp.sin(turns))[:, None, :]
    p_re, p_im = prod[:, :, 0], prod[:, :, 1]
    real_part = jnp.sum(tw_re * p_re - tw_im * p_im, axis=0)
    imag_part = jnp.sum(tw_re * p_im + tw_im * p_re, axis=0)
    return jnp.concatenate([real_part, imag_part], axis=-1)


def local(records, kept_bins, pair_offsets):
    ch_dev, win_dev, samples = records.shape
    bin_count = kept_bins.shape[0]
    band_span = pair_offsets.shape[0]
    record_rows = jnp.transpose(records, (1, 0, 2)).reshape(win_dev * ch_dev, samples)
    spectra = forward_spectra(record_rows, kept_bins)
    white = whiten(spectra).reshape(win_dev, ch_dev, 2, bin_count)
    freq_white = lax.all_to_all(white, "gy", split_axis=3, concat_axis=0, tiled=True)
    windows = freq_white.shape[0]
    shard_bins = freq_white.shape[3]
    rows_white = jnp.transpose(freq_white, (1, 2, 0, 3)).reshape(ch_dev, 2 * windows, shard_bins)
    gx_count = lax.axis_size("gx")
    needed = -(-band_span // ch_dev)
    blocks = [rows_white]
    for shift in range(1, min(needed, gx_count - 1) + 1):
        pairs = [(src, src - shift) for src in range(shift, gx_count)]
        blocks.append(lax.ppermute(rows_white, "gx", perm=pairs))
    missing = needed + 1 - len(blocks)
    if missing > 0:
        blocks.append(jnp.zeros((missing * ch_dev,) + rows_white.shape[1:], rows_white.dtype))
    padded = jnp.concatenate(blocks, axis=0)
    base = jnp.zeros((1,), jnp.int32)
    gy_count = lax.axis_size("gy")
    halves = pair_offsets.astype(jnp.int32).reshape(gy_count, 2, band_span // (2 * gy_count))
    parts = []
    for h in range(2):
        part = cross_spectra(padded, halves[:, h].reshape(-1), base, ch_dev).astype(jnp.bfloat16)
        parts.append(lax.all_to_all(part, "gy", split_axis=0, concat_axis=3, tiled=True))
    cross = jnp.concatenate(parts, axis=0)
    inverse = inverse_table(kept_bins)
    norm_scale = 0.5 / math.sqrt(windows * bin_count)
    lagged = (
        jnp.einsum("opck,pkl->ocl", cross, inverse, preferred_element_type=jnp.float32) * norm_scale
    )
    return lagged.astype(jnp.bfloat16)


def solution(mesh):
    return jax.shard_map(
        local,
        mesh=mesh,
        in_specs=(P("gx", "gy", None), P(), P()),
        out_specs=P("gy", "gx", None),
        check_vma=False,
    )
```

```python
import functools
import math

import jax
import jax.numpy as jnp
from jax import lax
from jax.experimental import pallas as pl
from jax.experimental.pallas import tpu as pltpu
from jax.sharding import PartitionSpec as P

SAMPLES = 8192
LAGS = 512


def inverse_table(kept_bins):
    fine_count = 32
    coarse_count = LAGS // fine_count

    def angles(index):
        return jnp.mod(kept_bins[:, None] * index[None, :], SAMPLES).astype(jnp.float32) * (
            2.0 * math.pi / SAMPLES
        )

    fine = angles(jnp.arange(fine_count, dtype=jnp.int32))[:, None, :]
    coarse = angles(fine_count * jnp.arange(coarse_count, dtype=jnp.int32) - LAGS // 2)[:, :, None]
    cos_f, sin_f, cos_c, sin_c = jnp.cos(fine), jnp.sin(fine), jnp.cos(coarse), jnp.sin(coarse)
    cos_t = (cos_f * cos_c - sin_f * sin_c).reshape(kept_bins.shape[0], LAGS)
    sin_t = (sin_f * cos_c + cos_f * sin_c).reshape(kept_bins.shape[0], LAGS)
    return jnp.stack([cos_t, -sin_t], axis=0).astype(jnp.bfloat16)


def whiten(spectra):
    mean_power = jnp.mean(spectra * spectra, axis=-1, keepdims=True)
    return (spectra * lax.rsqrt(mean_power + 1e-06)).astype(jnp.bfloat16)


def cross_kernel(offsets_ref, white_ref, out_ref, *, group, own_count, windows):
    step = pl.program_id(0)
    bins = white_ref.shape[2]

    span = own_count + 16

    def one_offset(i, carry):
        shift = offsets_ref[step * group + i]
        start = pl.multiple_of((shift // 8) * 8, 8)
        turn = (span - shift % 8) % span
        real_sum = jnp.zeros((own_count, bins), jnp.float32)
        imag_sum = jnp.zeros((own_count, bins), jnp.float32)
        for w in range(windows):
            ar = white_ref[w, pl.ds(0, own_count), :]
            ai = white_ref[windows + w, pl.ds(0, own_count), :]
            br = pltpu.roll(white_ref[w, pl.ds(start, span), :], turn, 0)[:own_count]
            bi = pltpu.roll(white_ref[windows + w, pl.ds(start, span), :], turn, 0)[:own_count]
            real_sum = real_sum + (ar * br + ai * bi)
            imag_sum = imag_sum + (ai * br - ar * bi)
        out_ref[i, 0] = real_sum
        out_ref[i, 1] = imag_sum
        return carry

    lax.fori_loop(0, group, one_offset, 0)


def cross_spectra(white_rows, pair_offsets, own_count):
    rows, channels, bins = white_rows.shape
    band_span = pair_offsets.shape[0]
    group = math.gcd(band_span, 8)
    kernel = functools.partial(cross_kernel, group=group, own_count=own_count, windows=rows // 2)
    return pl.pallas_call(
        kernel,
        grid_spec=pltpu.PrefetchScalarGridSpec(
            num_scalar_prefetch=1,
            grid=(band_span // group,),
            in_specs=[pl.BlockSpec(white_rows.shape, lambda g, offs: (0, 0, 0))],
            out_specs=pl.BlockSpec((group, 2, own_count, bins), lambda g, offs: (g, 0, 0, 0)),
        ),
        out_shape=jax.ShapeDtypeStruct((band_span, 2, own_count, bins), jnp.float32),
        compiler_params=pltpu.CompilerParams(vmem_limit_bytes=48 * 1024 * 1024),
        cost_estimate=pl.CostEstimate(
            flops=8 * band_span * own_count * rows * bins,
            transcendentals=0,
            bytes_accessed=white_rows.size * 4 + band_span * 2 * own_count * bins * 4,
        ),
    )(pair_offsets, white_rows)


def small_table(kept_bins, rows):
    fine_count = 1 << ((rows.bit_length() - 1) // 2)
    coarse_count = rows // fine_count

    def angles(step, count):
        index = step * jnp.arange(count, dtype=jnp.int32)
        return jnp.mod(index[:, None] * kept_bins[None, :], SAMPLES).astype(jnp.float32) * (
            2.0 * math.pi / SAMPLES
        )

    fine = angles(1, fine_count)[None, :, :]
    coarse = angles(fine_count, coarse_count)[:, None, :]
    cos_f, sin_f, cos_c, sin_c = jnp.cos(fine), jnp.sin(fine), jnp.cos(coarse), jnp.sin(coarse)
    cos_t = cos_f * cos_c - sin_f * sin_c
    sin_t = sin_f * cos_c + cos_f * sin_c
    table = jnp.concatenate([cos_t, -sin_t], axis=-1)
    return table.reshape(rows, 2 * kept_bins.shape[0]).astype(jnp.bfloat16)


def forward_spectra(record_rows, kept_bins):
    row_count, samples = record_rows.shape
    bin_count = kept_bins.shape[0]
    block_count = 4
    block_len = samples // block_count
    lhs = jnp.transpose(record_rows.reshape(row_count, block_count, block_len), (1, 0, 2))
    prod = jnp.dot(
        lhs.reshape(block_count * row_count, block_len),
        small_table(kept_bins, block_len),
        preferred_element_type=jnp.float32,
    ).reshape(block_count, row_count, 2, bin_count)
    turns = jnp.mod(
        jnp.arange(block_count, dtype=jnp.int32)[:, None] * jnp.mod(kept_bins, block_count)[None, :],
        block_count,
    ).astype(jnp.float32) * (2.0 * math.pi / block_count)
    tw_re = jnp.round(jnp.cos(turns))[:, None, :]
    tw_im = jnp.round(-jnp.sin(turns))[:, None, :]
    p_re, p_im = prod[:, :, 0], prod[:, :, 1]
    real_part = jnp.sum(tw_re * p_re - tw_im * p_im, axis=0)
    imag_part = jnp.sum(tw_re * p_im + tw_im * p_re, axis=0)
    return jnp.concatenate([real_part, imag_part], axis=-1)


def local(records, kept_bins, pair_offsets):
    ch_dev, win_dev, samples = records.shape
    bin_count = kept_bins.shape[0]
    band_span = pair_offsets.shape[0]
    record_rows = jnp.transpose(records, (1, 0, 2)).reshape(win_dev * ch_dev, samples)
    spectra = forward_spectra(record_rows, kept_bins)
    white = whiten(spectra).reshape(win_dev, ch_dev, 2, bin_count)
    freq_white = lax.all_to_all(white, "gy", split_axis=3, concat_axis=0, tiled=True)
    windows = freq_white.shape[0]
    shard_bins = freq_white.shape[3]
    rows_white = jnp.transpose(freq_white, (1, 2, 0, 3)).reshape(ch_dev, 2 * windows, shard_bins)
    gx_count = lax.axis_size("gx")
    needed = -(-band_span // ch_dev)
    blocks = [rows_white]
    for shift in range(1, min(needed, gx_count - 1) + 1):
        pairs = [(src, src - shift) for src in range(shift, gx_count)]
        blocks.append(lax.ppermute(rows_white, "gx", perm=pairs))
    missing = needed + 2 - len(blocks)
    if missing > 0:
        blocks.append(jnp.zeros((missing * ch_dev,) + rows_white.shape[1:], rows_white.dtype))
    padded = jnp.transpose(jnp.concatenate(blocks, axis=0), (1, 0, 2)).astype(jnp.float32)
    gy_count = lax.axis_size("gy")
    halves = pair_offsets.astype(jnp.int32).reshape(gy_count, 2, band_span // (2 * gy_count))
    parts = []
    for h in range(2):
        part = cross_spectra(padded, halves[:, h].reshape(-1), ch_dev).astype(jnp.bfloat16)
        parts.append(lax.all_to_all(part, "gy", split_axis=0, concat_axis=3, tiled=True))
    cross = jnp.concatenate(parts, axis=0)
    inverse = inverse_table(kept_bins)
    norm_scale = 0.5 / math.sqrt(windows * bin_count)
    lagged = (
        jnp.einsum("opck,pkl->ocl", cross, inverse, preferred_element_type=jnp.float32) * norm_scale
    )
    return lagged.astype(jnp.bfloat16)


def solution(mesh):
    return jax.shard_map(
        local,
        mesh=mesh,
        in_specs=(P("gx", "gy", None), P(), P()),
        out_specs=P("gy", "gx", None),
        check_vma=False,
    )
```

```python
import functools
import math

import jax
import jax.numpy as jnp
from jax import lax
from jax.experimental import pallas as pl
from jax.experimental.pallas import tpu as pltpu
from jax.sharding import PartitionSpec as P

SAMPLES = 8192
LAGS = 512


def inverse_table(kept_bins):
    fine_count = 32
    coarse_count = LAGS // fine_count

    def angles(index):
        return jnp.mod(kept_bins[:, None] * index[None, :], SAMPLES).astype(jnp.float32) * (
            2.0 * math.pi / SAMPLES
        )

    fine = angles(jnp.arange(fine_count, dtype=jnp.int32))[:, None, :]
    coarse = angles(fine_count * jnp.arange(coarse_count, dtype=jnp.int32) - LAGS // 2)[:, :, None]
    cos_f, sin_f, cos_c, sin_c = jnp.cos(fine), jnp.sin(fine), jnp.cos(coarse), jnp.sin(coarse)
    cos_t = (cos_f * cos_c - sin_f * sin_c).reshape(kept_bins.shape[0], LAGS)
    sin_t = (sin_f * cos_c + cos_f * sin_c).reshape(kept_bins.shape[0], LAGS)
    return jnp.stack([cos_t, -sin_t], axis=0).astype(jnp.bfloat16)


def whiten(spectra):
    mean_power = jnp.mean(spectra * spectra, axis=-1, keepdims=True)
    return (spectra * lax.rsqrt(mean_power + 1e-06)).astype(jnp.bfloat16)


def cross_kernel(offsets_ref, base_ref, white_ref, out_ref, *, group, own_count, half):
    step = pl.program_id(0)
    base = base_ref[0]
    own = [white_ref[base + c].astype(jnp.float32) for c in range(own_count)]

    def one_offset(i, carry):
        shift = offsets_ref[step * group + i]
        for c in range(own_count):
            a = own[c]
            b = white_ref[base + c + shift].astype(jnp.float32)
            ar, ai, br, bi = a[:half], a[half:], b[:half], b[half:]
            out_ref[i, 0, pl.ds(c, 1), :] = jnp.sum(ar * br + ai * bi, axis=0, keepdims=True)
            out_ref[i, 1, pl.ds(c, 1), :] = jnp.sum(ai * br - ar * bi, axis=0, keepdims=True)
        return carry

    lax.fori_loop(0, group, one_offset, 0)


def cross_spectra(white_all, pair_offsets, base, own_count):
    rows, bins = white_all.shape[1], white_all.shape[2]
    band_span = pair_offsets.shape[0]
    group = math.gcd(band_span, 8)
    kernel = functools.partial(cross_kernel, group=group, own_count=own_count, half=rows // 2)
    return pl.pallas_call(
        kernel,
        grid_spec=pltpu.PrefetchScalarGridSpec(
            num_scalar_prefetch=2,
            grid=(band_span // group,),
            in_specs=[pl.BlockSpec(white_all.shape, lambda g, offs, b: (0, 0, 0))],
            out_specs=pl.BlockSpec((group, 2, own_count, bins), lambda g, offs, b: (g, 0, 0, 0)),
        ),
        out_shape=jax.ShapeDtypeStruct((band_span, 2, own_count, bins), jnp.float32),
        compiler_params=pltpu.CompilerParams(vmem_limit_bytes=48 * 1024 * 1024),
        cost_estimate=pl.CostEstimate(
            flops=8 * band_span * own_count * rows * bins,
            transcendentals=0,
            bytes_accessed=white_all.size * 2 + band_span * 2 * own_count * bins * 4,
        ),
    )(pair_offsets, base, white_all)


def small_table(kept_bins, rows):
    fine_count = 1 << ((rows.bit_length() - 1) // 2)
    coarse_count = rows // fine_count

    def angles(step, count):
        index = step * jnp.arange(count, dtype=jnp.int32)
        return jnp.mod(index[:, None] * kept_bins[None, :], SAMPLES).astype(jnp.float32) * (
            2.0 * math.pi / SAMPLES
        )

    fine = angles(1, fine_count)[None, :, :]
    coarse = angles(fine_count, coarse_count)[:, None, :]
    cos_f, sin_f, cos_c, sin_c = jnp.cos(fine), jnp.sin(fine), jnp.cos(coarse), jnp.sin(coarse)
    cos_t = cos_f * cos_c - sin_f * sin_c
    sin_t = sin_f * cos_c + cos_f * sin_c
    table = jnp.concatenate([cos_t, -sin_t], axis=-1)
    return table.reshape(rows, 2 * kept_bins.shape[0]).astype(jnp.bfloat16)


def forward_spectra(record_rows, kept_bins):
    row_count, samples = record_rows.shape
    bin_count = kept_bins.shape[0]
    block_count = 4
    block_len = samples // block_count
    lhs = jnp.transpose(record_rows.reshape(row_count, block_count, block_len), (1, 0, 2))
    prod = jnp.dot(
        lhs.reshape(block_count * row_count, block_len),
        small_table(kept_bins, block_len),
        preferred_element_type=jnp.float32,
    ).reshape(block_count, row_count, 2, bin_count)
    turns = jnp.mod(
        jnp.arange(block_count, dtype=jnp.int32)[:, None] * jnp.mod(kept_bins, block_count)[None, :],
        block_count,
    ).astype(jnp.float32) * (2.0 * math.pi / block_count)
    tw_re = jnp.round(jnp.cos(turns))[:, None, :]
    tw_im = jnp.round(-jnp.sin(turns))[:, None, :]
    p_re, p_im = prod[:, :, 0], prod[:, :, 1]
    real_part = jnp.sum(tw_re * p_re - tw_im * p_im, axis=0)
    imag_part = jnp.sum(tw_re * p_im + tw_im * p_re, axis=0)
    return jnp.concatenate([real_part, imag_part], axis=-1)


def local(records, kept_bins, pair_offsets):
    ch_dev, win_dev, samples = records.shape
    bin_count = kept_bins.shape[0]
    band_span = pair_offsets.shape[0]
    record_rows = jnp.transpose(records, (1, 0, 2)).reshape(win_dev * ch_dev, samples)
    spectra = forward_spectra(record_rows, kept_bins)
    white = whiten(spectra).reshape(win_dev, ch_dev, 2, bin_count)
    freq_white = lax.all_to_all(white, "gy", split_axis=3, concat_axis=0, tiled=True)
    windows = freq_white.shape[0]
    shard_bins = freq_white.shape[3]
    rows_white = jnp.transpose(freq_white, (1, 2, 0, 3)).reshape(ch_dev, 2 * windows, shard_bins)
    gx_count = lax.axis_size("gx")
    needed = -(-band_span // ch_dev)
    blocks = [rows_white]
    for shift in range(1, min(needed, gx_count - 1) + 1):
        pairs = [(src, src - shift) for src in range(shift, gx_count)]
        blocks.append(lax.ppermute(rows_white, "gx", perm=pairs))
    missing = needed + 1 - len(blocks)
    if missing > 0:
        blocks.append(jnp.zeros((missing * ch_dev,) + rows_white.shape[1:], rows_white.dtype))
    padded = jnp.concatenate(blocks, axis=0)
    base = jnp.zeros((1,), jnp.int32)
    gy_count = lax.axis_size("gy")
    part_count = 4
    halves = pair_offsets.astype(jnp.int32).reshape(gy_count, part_count, band_span // (part_count * gy_count))
    parts = []
    for h in range(part_count):
        part = cross_spectra(padded, halves[:, h].reshape(-1), base, ch_dev).astype(jnp.bfloat16)
        parts.append(lax.all_to_all(part, "gy", split_axis=0, concat_axis=3, tiled=True))
    cross = jnp.concatenate(parts, axis=0)
    inverse = inverse_table(kept_bins)
    norm_scale = 0.5 / math.sqrt(windows * bin_count)
    lagged = (
        jnp.einsum("opck,pkl->ocl", cross, inverse, preferred_element_type=jnp.float32) * norm_scale
    )
    return lagged.astype(jnp.bfloat16)


def solution(mesh):
    return jax.shard_map(
        local,
        mesh=mesh,
        in_specs=(P("gx", "gy", None), P(), P()),
        out_specs=P("gy", "gx", None),
        check_vma=False,
    )
```

```python
import functools
import math

import jax
import jax.numpy as jnp
from jax import lax
from jax.experimental import pallas as pl
from jax.experimental.pallas import tpu as pltpu
from jax.sharding import PartitionSpec as P

SAMPLES = 8192
LAGS = 512


def inverse_table(kept_bins):
    fine_count = 32
    coarse_count = LAGS // fine_count

    def angles(index):
        return jnp.mod(kept_bins[:, None] * index[None, :], SAMPLES).astype(jnp.float32) * (
            2.0 * math.pi / SAMPLES
        )

    fine = angles(jnp.arange(fine_count, dtype=jnp.int32))[:, None, :]
    coarse = angles(fine_count * jnp.arange(coarse_count, dtype=jnp.int32) - LAGS // 2)[:, :, None]
    cos_f, sin_f, cos_c, sin_c = jnp.cos(fine), jnp.sin(fine), jnp.cos(coarse), jnp.sin(coarse)
    cos_t = (cos_f * cos_c - sin_f * sin_c).reshape(kept_bins.shape[0], LAGS)
    sin_t = (sin_f * cos_c + cos_f * sin_c).reshape(kept_bins.shape[0], LAGS)
    return jnp.stack([cos_t, -sin_t], axis=0).astype(jnp.bfloat16)


def whiten(spectra):
    mean_power = jnp.mean(spectra * spectra, axis=-1, keepdims=True)
    return (spectra * lax.rsqrt(mean_power + 1e-06)).astype(jnp.bfloat16)


def cross_kernel(offsets_ref, base_ref, white_ref, out_ref, *, group, own_count, half):
    step = pl.program_id(0)
    base = base_ref[0]
    own = [white_ref[base + c].astype(jnp.float32) for c in range(own_count)]

    def one_offset(i, carry):
        shift = offsets_ref[step * group + i]
        for c in range(own_count):
            a = own[c]
            b = white_ref[base + c + shift].astype(jnp.float32)
            ar, ai, br, bi = a[:half], a[half:], b[:half], b[half:]
            out_ref[i, 0, pl.ds(c, 1), :] = jnp.sum(ar * br + ai * bi, axis=0, keepdims=True)
            out_ref[i, 1, pl.ds(c, 1), :] = jnp.sum(ai * br - ar * bi, axis=0, keepdims=True)
        return carry

    lax.fori_loop(0, group, one_offset, 0)


def cross_spectra(white_all, pair_offsets, base, own_count):
    rows, bins = white_all.shape[1], white_all.shape[2]
    band_span = pair_offsets.shape[0]
    group = math.gcd(band_span, 8)
    kernel = functools.partial(cross_kernel, group=group, own_count=own_count, half=rows // 2)
    return pl.pallas_call(
        kernel,
        grid_spec=pltpu.PrefetchScalarGridSpec(
            num_scalar_prefetch=2,
            grid=(band_span // group,),
            in_specs=[pl.BlockSpec(white_all.shape, lambda g, offs, b: (0, 0, 0))],
            out_specs=pl.BlockSpec((group, 2, own_count, bins), lambda g, offs, b: (g, 0, 0, 0)),
        ),
        out_shape=jax.ShapeDtypeStruct((band_span, 2, own_count, bins), jnp.float32),
        compiler_params=pltpu.CompilerParams(vmem_limit_bytes=48 * 1024 * 1024),
        cost_estimate=pl.CostEstimate(
            flops=8 * band_span * own_count * rows * bins,
            transcendentals=0,
            bytes_accessed=white_all.size * 2 + band_span * 2 * own_count * bins * 4,
        ),
    )(pair_offsets, base, white_all)


def small_table(kept_bins, rows):
    fine_count = 1 << ((rows.bit_length() - 1) // 2)
    coarse_count = rows // fine_count

    def angles(step, count):
        index = step * jnp.arange(count, dtype=jnp.int32)
        return jnp.mod(index[:, None] * kept_bins[None, :], SAMPLES).astype(jnp.float32) * (
            2.0 * math.pi / SAMPLES
        )

    fine = angles(1, fine_count)[None, :, :]
    coarse = angles(fine_count, coarse_count)[:, None, :]
    cos_f, sin_f, cos_c, sin_c = jnp.cos(fine), jnp.sin(fine), jnp.cos(coarse), jnp.sin(coarse)
    cos_t = cos_f * cos_c - sin_f * sin_c
    sin_t = sin_f * cos_c + cos_f * sin_c
    table = jnp.concatenate([cos_t, -sin_t], axis=-1)
    return table.reshape(rows, 2 * kept_bins.shape[0]).astype(jnp.bfloat16)


def forward_spectra(record_rows, kept_bins):
    row_count, samples = record_rows.shape
    bin_count = kept_bins.shape[0]
    block_count = 4
    block_len = samples // block_count
    lhs = jnp.transpose(record_rows.reshape(row_count, block_count, block_len), (1, 0, 2))
    prod = jnp.dot(
        lhs.reshape(block_count * row_count, block_len),
        small_table(kept_bins, block_len),
        preferred_element_type=jnp.float32,
    ).reshape(block_count, row_count, 2, bin_count)
    turns = jnp.mod(
        jnp.arange(block_count, dtype=jnp.int32)[:, None] * jnp.mod(kept_bins, block_count)[None, :],
        block_count,
    ).astype(jnp.float32) * (2.0 * math.pi / block_count)
    tw_re = jnp.round(jnp.cos(turns))[:, None, :]
    tw_im = jnp.round(-jnp.sin(turns))[:, None, :]
    p_re, p_im = prod[:, :, 0], prod[:, :, 1]
    real_part = jnp.sum(tw_re * p_re - tw_im * p_im, axis=0)
    imag_part = jnp.sum(tw_re * p_im + tw_im * p_re, axis=0)
    return jnp.concatenate([real_part, imag_part], axis=-1)


def local(records, kept_bins, pair_offsets):
    ch_dev, win_dev, samples = records.shape
    bin_count = kept_bins.shape[0]
    band_span = pair_offsets.shape[0]
    record_rows = jnp.transpose(records, (1, 0, 2)).reshape(win_dev * ch_dev, samples)
    spectra = forward_spectra(record_rows, kept_bins)
    white = whiten(spectra).reshape(win_dev, ch_dev, 2, bin_count)
    freq_white = lax.all_to_all(white, "gy", split_axis=3, concat_axis=0, tiled=True)
    windows = freq_white.shape[0]
    shard_bins = freq_white.shape[3]
    rows_white = jnp.transpose(freq_white, (1, 2, 0, 3)).reshape(ch_dev, 2 * windows, shard_bins)
    gx_count = lax.axis_size("gx")
    needed = -(-band_span // ch_dev)
    blocks = [rows_white]
    for shift in range(1, min(needed, gx_count - 1) + 1):
        pairs = [(src, src - shift) for src in range(shift, gx_count)]
        blocks.append(lax.ppermute(rows_white, "gx", perm=pairs))
    missing = needed + 1 - len(blocks)
    if missing > 0:
        blocks.append(jnp.zeros((missing * ch_dev,) + rows_white.shape[1:], rows_white.dtype))
    padded = jnp.concatenate(blocks, axis=0)
    base = jnp.zeros((1,), jnp.int32)
    gy_count = lax.axis_size("gy")
    off_dev = band_span // gy_count
    me = lax.axis_index("gy")
    offsets = pair_offsets.astype(jnp.int32)
    inverse = inverse_table(kept_bins)
    norm_scale = 0.5 / math.sqrt(windows * bin_count)
    lagged = None
    for shift in list(range(1, gy_count)) + [0]:
        dest = lax.rem(me + shift, gy_count)
        part = cross_spectra(
            padded, lax.dynamic_slice_in_dim(offsets, dest * off_dev, off_dev), base, ch_dev
        ).astype(jnp.bfloat16)
        if shift:
            pairs = [(src, (src + shift) % gy_count) for src in range(gy_count)]
            part = lax.ppermute(part, "gy", perm=pairs)
        origin = lax.rem(me + gy_count - shift, gy_count)
        rows = lax.dynamic_slice_in_dim(inverse, origin * shard_bins, shard_bins, 1)
        term = jnp.einsum("opck,pkl->ocl", part, rows, preferred_element_type=jnp.float32)
        lagged = term if lagged is None else lagged + term
    lagged = lagged * norm_scale
    return lagged.astype(jnp.bfloat16)


def solution(mesh):
    return jax.shard_map(
        local,
        mesh=mesh,
        in_specs=(P("gx", "gy", None), P(), P()),
        out_specs=P("gy", "gx", None),
        check_vma=False,
    )
```

```python
import functools
import math

import jax
import jax.numpy as jnp
from jax import lax
from jax.experimental import pallas as pl
from jax.experimental.pallas import tpu as pltpu
from jax.sharding import PartitionSpec as P

SAMPLES = 8192
LAGS = 512


def inverse_table(kept_bins):
    fine_count = 32
    coarse_count = LAGS // fine_count

    def angles(index):
        return jnp.mod(kept_bins[:, None] * index[None, :], SAMPLES).astype(jnp.float32) * (
            2.0 * math.pi / SAMPLES
        )

    fine = angles(jnp.arange(fine_count, dtype=jnp.int32))[:, None, :]
    coarse = angles(fine_count * jnp.arange(coarse_count, dtype=jnp.int32) - LAGS // 2)[:, :, None]
    cos_f, sin_f, cos_c, sin_c = jnp.cos(fine), jnp.sin(fine), jnp.cos(coarse), jnp.sin(coarse)
    cos_t = (cos_f * cos_c - sin_f * sin_c).reshape(kept_bins.shape[0], LAGS)
    sin_t = (sin_f * cos_c + cos_f * sin_c).reshape(kept_bins.shape[0], LAGS)
    return jnp.stack([cos_t, -sin_t], axis=0).astype(jnp.bfloat16)


def whiten(spectra):
    mean_power = jnp.mean(spectra * spectra, axis=-1, keepdims=True)
    return (spectra * lax.rsqrt(mean_power + 1e-06)).astype(jnp.bfloat16)


def cross_kernel(offsets_ref, base_ref, white_ref, out_ref, *, group, own_count, half):
    step = pl.program_id(0)
    base = base_ref[0]
    own = [white_ref[base + c].astype(jnp.float32) for c in range(own_count)]

    def one_offset(i, carry):
        shift = offsets_ref[step * group + i]
        for c in range(own_count):
            a = own[c]
            b = white_ref[base + c + shift].astype(jnp.float32)
            ar, ai, br, bi = a[:half], a[half:], b[:half], b[half:]
            out_ref[i, 0, pl.ds(c, 1), :] = jnp.sum(ar * br + ai * bi, axis=0, keepdims=True)
            out_ref[i, 1, pl.ds(c, 1), :] = jnp.sum(ai * br - ar * bi, axis=0, keepdims=True)
        return carry

    lax.fori_loop(0, group, one_offset, 0)


def cross_spectra(white_all, pair_offsets, base, own_count):
    rows, bins = white_all.shape[1], white_all.shape[2]
    band_span = pair_offsets.shape[0]
    group = math.gcd(band_span, 8)
    kernel = functools.partial(cross_kernel, group=group, own_count=own_count, half=rows // 2)
    return pl.pallas_call(
        kernel,
        grid_spec=pltpu.PrefetchScalarGridSpec(
            num_scalar_prefetch=2,
            grid=(band_span // group,),
            in_specs=[pl.BlockSpec(white_all.shape, lambda g, offs, b: (0, 0, 0))],
            out_specs=pl.BlockSpec((group, 2, own_count, bins), lambda g, offs, b: (g, 0, 0, 0)),
        ),
        out_shape=jax.ShapeDtypeStruct((band_span, 2, own_count, bins), jnp.float32),
        compiler_params=pltpu.CompilerParams(vmem_limit_bytes=48 * 1024 * 1024),
        cost_estimate=pl.CostEstimate(
            flops=8 * band_span * own_count * rows * bins,
            transcendentals=0,
            bytes_accessed=white_all.size * 2 + band_span * 2 * own_count * bins * 4,
        ),
    )(pair_offsets, base, white_all)


def small_table(kept_bins, rows):
    fine_count = 1 << ((rows.bit_length() - 1) // 2)
    coarse_count = rows // fine_count

    def angles(step, count):
        index = step * jnp.arange(count, dtype=jnp.int32)
        return jnp.mod(index[:, None] * kept_bins[None, :], SAMPLES).astype(jnp.float32) * (
            2.0 * math.pi / SAMPLES
        )

    fine = angles(1, fine_count)[None, :, :]
    coarse = angles(fine_count, coarse_count)[:, None, :]
    cos_f, sin_f, cos_c, sin_c = jnp.cos(fine), jnp.sin(fine), jnp.cos(coarse), jnp.sin(coarse)
    cos_t = cos_f * cos_c - sin_f * sin_c
    sin_t = sin_f * cos_c + cos_f * sin_c
    table = jnp.concatenate([cos_t, -sin_t], axis=-1)
    return table.reshape(rows, 2 * kept_bins.shape[0]).astype(jnp.bfloat16)


def forward_spectra(record_rows, kept_bins):
    row_count, samples = record_rows.shape
    bin_count = kept_bins.shape[0]
    block_count = 4
    block_len = samples // block_count
    lhs = jnp.transpose(record_rows.reshape(row_count, block_count, block_len), (1, 0, 2))
    prod = jnp.dot(
        lhs.reshape(block_count * row_count, block_len),
        small_table(kept_bins, block_len),
        preferred_element_type=jnp.float32,
    ).reshape(block_count, row_count, 2, bin_count)
    turns = jnp.mod(
        jnp.arange(block_count, dtype=jnp.int32)[:, None] * jnp.mod(kept_bins, block_count)[None, :],
        block_count,
    ).astype(jnp.float32) * (2.0 * math.pi / block_count)
    tw_re = jnp.round(jnp.cos(turns))[:, None, :]
    tw_im = jnp.round(-jnp.sin(turns))[:, None, :]
    p_re, p_im = prod[:, :, 0], prod[:, :, 1]
    real_part = jnp.sum(tw_re * p_re - tw_im * p_im, axis=0)
    imag_part = jnp.sum(tw_re * p_im + tw_im * p_re, axis=0)
    return jnp.concatenate([real_part, imag_part], axis=-1)


def local(records, kept_bins, pair_offsets):
    ch_dev, win_dev, samples = records.shape
    bin_count = kept_bins.shape[0]
    band_span = pair_offsets.shape[0]
    record_rows = jnp.transpose(records, (1, 0, 2)).reshape(win_dev * ch_dev, samples)
    spectra = forward_spectra(record_rows, kept_bins)
    white = whiten(spectra).reshape(win_dev, ch_dev, 2, bin_count)
    freq_white = lax.all_to_all(white, "gy", split_axis=3, concat_axis=0, tiled=True)
    windows = freq_white.shape[0]
    shard_bins = freq_white.shape[3]
    rows_white = jnp.transpose(freq_white, (1, 2, 0, 3)).reshape(ch_dev, 2 * windows, shard_bins)
    gx_count = lax.axis_size("gx")
    gy_count = lax.axis_size("gy")
    needed = -(-band_span // ch_dev)
    off_dev = band_span // gy_count
    me = lax.axis_index("gy")
    offsets = pair_offsets.astype(jnp.int32)
    inverse = inverse_table(kept_bins)
    norm_scale = 0.5 / math.sqrt(windows * bin_count)
    base = jnp.zeros((1,), jnp.int32)
    half_bins = shard_bins // 2

    def gather_above(own_rows):
        blocks = [own_rows]
        for shift in range(1, min(needed, gx_count - 1) + 1):
            pairs = [(src, src - shift) for src in range(shift, gx_count)]
            blocks.append(lax.ppermute(own_rows, "gx", perm=pairs))
        missing = needed + 1 - len(blocks)
        if missing > 0:
            blocks.append(jnp.zeros((missing * ch_dev,) + own_rows.shape[1:], own_rows.dtype))
        return jnp.concatenate(blocks, axis=0)

    first_half = gather_above(rows_white[:, :, :half_bins])
    second_own, first_half = lax.optimization_barrier((rows_white[:, :, half_bins:], first_half))
    second_half = gather_above(second_own)
    lagged = None
    for h, padded in enumerate([first_half, second_half]):
        for shift in list(range(1, gy_count)) + [0]:
            dest = lax.rem(me + shift, gy_count)
            part = cross_spectra(
                padded, lax.dynamic_slice_in_dim(offsets, dest * off_dev, off_dev), base, ch_dev
            ).astype(jnp.bfloat16)
            if shift:
                pairs = [(src, (src + shift) % gy_count) for src in range(gy_count)]
                part = lax.ppermute(part, "gy", perm=pairs)
            origin = lax.rem(me + gy_count - shift, gy_count)
            rows = lax.dynamic_slice_in_dim(inverse, origin * shard_bins + h * half_bins, half_bins, 1)
            term = jnp.einsum("opck,pkl->ocl", part, rows, preferred_element_type=jnp.float32)
            lagged = term if lagged is None else lagged + term
    lagged = lagged * norm_scale
    return lagged.astype(jnp.bfloat16)


def solution(mesh):
    return jax.shard_map(
        local,
        mesh=mesh,
        in_specs=(P("gx", "gy", None), P(), P()),
        out_specs=P("gy", "gx", None),
        check_vma=False,
    )
```

```python
import functools
import math

import jax
import jax.numpy as jnp
from jax import lax
from jax.experimental import pallas as pl
from jax.experimental.pallas import tpu as pltpu
from jax.sharding import PartitionSpec as P

SAMPLES = 8192
LAGS = 512


def inverse_table(kept_bins):
    fine_count = 32
    coarse_count = LAGS // fine_count

    def angles(index):
        return jnp.mod(kept_bins[:, None] * index[None, :], SAMPLES).astype(jnp.float32) * (
            2.0 * math.pi / SAMPLES
        )

    fine = angles(jnp.arange(fine_count, dtype=jnp.int32))[:, None, :]
    coarse = angles(fine_count * jnp.arange(coarse_count, dtype=jnp.int32) - LAGS // 2)[:, :, None]
    cos_f, sin_f, cos_c, sin_c = jnp.cos(fine), jnp.sin(fine), jnp.cos(coarse), jnp.sin(coarse)
    cos_t = (cos_f * cos_c - sin_f * sin_c).reshape(kept_bins.shape[0], LAGS)
    sin_t = (sin_f * cos_c + cos_f * sin_c).reshape(kept_bins.shape[0], LAGS)
    return jnp.stack([cos_t, -sin_t], axis=0).astype(jnp.bfloat16)


def whiten(spectra):
    mean_power = jnp.mean(spectra * spectra, axis=-1, keepdims=True)
    return (spectra * lax.rsqrt(mean_power + 1e-06)).astype(jnp.bfloat16)


def cross_kernel(offsets_ref, white_ref, *rest, group, own_count, half, first_row, end_row):
    if len(rest) == 2:
        earlier_ref, out_ref = rest
    else:
        earlier_ref, (out_ref,) = None, rest
    step = pl.program_id(0)
    own = [white_ref[c].astype(jnp.float32) for c in range(own_count)]

    def one_offset(i, carry):
        shift = offsets_ref[step * group + i]
        meets = jnp.logical_and(shift + own_count > first_row, shift < end_row)

        @pl.when(meets)
        def _():
            for c in range(own_count):
                a = own[c]
                b = white_ref[c + shift].astype(jnp.float32)
                ar, ai, br, bi = a[:half], a[half:], b[:half], b[half:]
                real_part = jnp.sum(ar * br + ai * bi, axis=0, keepdims=True)
                imag_part = jnp.sum(ai * br - ar * bi, axis=0, keepdims=True)
                if earlier_ref is not None:
                    real_part = real_part + earlier_ref[i, 0, pl.ds(c, 1), :]
                    imag_part = imag_part + earlier_ref[i, 1, pl.ds(c, 1), :]
                out_ref[i, 0, pl.ds(c, 1), :] = real_part
                out_ref[i, 1, pl.ds(c, 1), :] = imag_part

        @pl.when(jnp.logical_not(meets))
        def _():
            if earlier_ref is None:
                out_ref[i] = jnp.zeros(out_ref.shape[1:], out_ref.dtype)
            else:
                out_ref[i] = earlier_ref[i]

        return carry

    lax.fori_loop(0, group, one_offset, 0)


def cross_spectra(white_all, pair_offsets, own_count, first_row, end_row, earlier=None):
    rows, bins = white_all.shape[1], white_all.shape[2]
    band_span = pair_offsets.shape[0]
    group = math.gcd(band_span, 8)
    kernel = functools.partial(
        cross_kernel, group=group, own_count=own_count, half=rows // 2, first_row=first_row, end_row=end_row
    )
    block = pl.BlockSpec((group, 2, own_count, bins), lambda g, offs: (g, 0, 0, 0))
    operands = [pair_offsets, white_all] + ([] if earlier is None else [earlier])
    return pl.pallas_call(
        kernel,
        grid_spec=pltpu.PrefetchScalarGridSpec(
            num_scalar_prefetch=1,
            grid=(band_span // group,),
            in_specs=[pl.BlockSpec(white_all.shape, lambda g, offs: (0, 0, 0))]
            + ([] if earlier is None else [block]),
            out_specs=block,
        ),
        out_shape=jax.ShapeDtypeStruct((band_span, 2, own_count, bins), jnp.float32),
        compiler_params=pltpu.CompilerParams(vmem_limit_bytes=48 * 1024 * 1024),
        cost_estimate=pl.CostEstimate(
            flops=1024 * band_span * own_count * rows * bins,
            transcendentals=0,
            bytes_accessed=white_all.size * 2 + band_span * 2 * own_count * bins * 8,
        ),
    )(*operands)


def small_table(kept_bins, rows):
    fine_count = 1 << ((rows.bit_length() - 1) // 2)
    coarse_count = rows // fine_count

    def angles(step, count):
        index = step * jnp.arange(count, dtype=jnp.int32)
        return jnp.mod(index[:, None] * kept_bins[None, :], SAMPLES).astype(jnp.float32) * (
            2.0 * math.pi / SAMPLES
        )

    fine = angles(1, fine_count)[None, :, :]
    coarse = angles(fine_count, coarse_count)[:, None, :]
    cos_f, sin_f, cos_c, sin_c = jnp.cos(fine), jnp.sin(fine), jnp.cos(coarse), jnp.sin(coarse)
    cos_t = cos_f * cos_c - sin_f * sin_c
    sin_t = sin_f * cos_c + cos_f * sin_c
    table = jnp.concatenate([cos_t, -sin_t], axis=-1)
    return table.reshape(rows, 2 * kept_bins.shape[0]).astype(jnp.bfloat16)


def forward_spectra(record_rows, kept_bins):
    row_count, samples = record_rows.shape
    bin_count = kept_bins.shape[0]
    block_count = 4
    block_len = samples // block_count
    lhs = jnp.transpose(record_rows.reshape(row_count, block_count, block_len), (1, 0, 2))
    prod = jnp.dot(
        lhs.reshape(block_count * row_count, block_len),
        small_table(kept_bins, block_len),
        preferred_element_type=jnp.float32,
    ).reshape(block_count, row_count, 2, bin_count)
    turns = jnp.mod(
        jnp.arange(block_count, dtype=jnp.int32)[:, None] * jnp.mod(kept_bins, block_count)[None, :],
        block_count,
    ).astype(jnp.float32) * (2.0 * math.pi / block_count)
    tw_re = jnp.round(jnp.cos(turns))[:, None, :]
    tw_im = jnp.round(-jnp.sin(turns))[:, None, :]
    p_re, p_im = prod[:, :, 0], prod[:, :, 1]
    real_part = jnp.sum(tw_re * p_re - tw_im * p_im, axis=0)
    imag_part = jnp.sum(tw_re * p_im + tw_im * p_re, axis=0)
    return jnp.concatenate([real_part, imag_part], axis=-1)


def local(records, kept_bins, pair_offsets):
    ch_dev, win_dev, samples = records.shape
    bin_count = kept_bins.shape[0]
    band_span = pair_offsets.shape[0]
    record_rows = jnp.transpose(records, (1, 0, 2)).reshape(win_dev * ch_dev, samples)
    spectra = forward_spectra(record_rows, kept_bins)
    white = whiten(spectra).reshape(win_dev, ch_dev, 2, bin_count)
    freq_white = lax.all_to_all(white, "gy", split_axis=3, concat_axis=0, tiled=True)
    windows = freq_white.shape[0]
    shard_bins = freq_white.shape[3]
    rows_white = jnp.transpose(freq_white, (1, 2, 0, 3)).reshape(ch_dev, 2 * windows, shard_bins)
    gx_count = lax.axis_size("gx")
    needed = -(-band_span // ch_dev)
    real_count = min(needed, gx_count - 1) + 1
    near_count = min(4, real_count)
    blocks = [rows_white]
    source = rows_white
    for shift in range(1, real_count):
        if shift == near_count:
            source, _ = lax.optimization_barrier((rows_white, blocks))
        pairs = [(src, src - shift) for src in range(shift, gx_count)]
        blocks.append(lax.ppermute(source, "gx", perm=pairs))
    zero_block = jnp.zeros_like(rows_white)
    blocks += [zero_block] * (needed + 1 - len(blocks))
    near = jnp.concatenate(blocks[:near_count] + [zero_block] * (len(blocks) - near_count), axis=0)
    far = jnp.concatenate([rows_white] + [zero_block] * (near_count - 1) + blocks[near_count:], axis=0)
    split_row = near_count * ch_dev
    end_row = len(blocks) * ch_dev
    gy_count = lax.axis_size("gy")
    off_dev = band_span // gy_count
    me = lax.axis_index("gy")
    offsets = pair_offsets.astype(jnp.int32)
    inverse = inverse_table(kept_bins)
    norm_scale = 0.5 / math.sqrt(windows * bin_count)
    shifts = list(range(1, gy_count)) + [0]
    dest_offsets = [
        lax.dynamic_slice_in_dim(offsets, lax.rem(me + shift, gy_count) * off_dev, off_dev) for shift in shifts
    ]
    near_parts = [cross_spectra(near, offs, ch_dev, 0, split_row) for offs in dest_offsets]
    lagged = None
    for shift, offs, near_part in zip(shifts, dest_offsets, near_parts):
        part = cross_spectra(far, offs, ch_dev, split_row, end_row, near_part).astype(jnp.bfloat16)
        if shift:
            pairs = [(src, (src + shift) % gy_count) for src in range(gy_count)]
            part = lax.ppermute(part, "gy", perm=pairs)
        origin = lax.rem(me + gy_count - shift, gy_count)
        rows = lax.dynamic_slice_in_dim(inverse, origin * shard_bins, shard_bins, 1)
        term = jnp.einsum("opck,pkl->ocl", part, rows, preferred_element_type=jnp.float32)
        lagged = term if lagged is None else lagged + term
    lagged = lagged * norm_scale
    return lagged.astype(jnp.bfloat16)


def solution(mesh):
    return jax.shard_map(
        local,
        mesh=mesh,
        in_specs=(P("gx", "gy", None), P(), P()),
        out_specs=P("gy", "gx", None),
        check_vma=False,
    )
```

```python
import functools
import math

import jax
import jax.numpy as jnp
from jax import lax
from jax.experimental import pallas as pl
from jax.experimental.pallas import tpu as pltpu
from jax.sharding import PartitionSpec as P

SAMPLES = 8192
LAGS = 512


def inverse_table(kept_bins):
    fine_count = 32
    coarse_count = LAGS // fine_count

    def angles(index):
        return jnp.mod(kept_bins[:, None] * index[None, :], SAMPLES).astype(jnp.float32) * (
            2.0 * math.pi / SAMPLES
        )

    fine = angles(jnp.arange(fine_count, dtype=jnp.int32))[:, None, :]
    coarse = angles(fine_count * jnp.arange(coarse_count, dtype=jnp.int32) - LAGS // 2)[:, :, None]
    cos_f, sin_f, cos_c, sin_c = jnp.cos(fine), jnp.sin(fine), jnp.cos(coarse), jnp.sin(coarse)
    cos_t = (cos_f * cos_c - sin_f * sin_c).reshape(kept_bins.shape[0], LAGS)
    sin_t = (sin_f * cos_c + cos_f * sin_c).reshape(kept_bins.shape[0], LAGS)
    return jnp.stack([cos_t, -sin_t], axis=0).astype(jnp.bfloat16)


def whiten(spectra):
    mean_power = jnp.mean(spectra * spectra, axis=-1, keepdims=True)
    return (spectra * lax.rsqrt(mean_power + 1e-06)).astype(jnp.bfloat16)


def cross_kernel(offsets_ref, base_ref, white_ref, out_ref, *, group, own_count, half):
    step = pl.program_id(0)
    base = base_ref[0]
    bins = white_ref.shape[2]
    row_of = lax.broadcasted_iota(jnp.int32, (own_count, own_count * half), 1) // half
    pick = (row_of == lax.broadcasted_iota(jnp.int32, (own_count, own_count * half), 0)).astype(jnp.float32)

    def window_sum(products):
        return jnp.dot(
            pick,
            products.reshape(own_count * half, bins),
            precision=lax.Precision.HIGHEST,
            preferred_element_type=jnp.float32,
        )

    def one_offset(i, carry):
        shift = offsets_ref[step * group + i]
        a = white_ref[pl.ds(base, own_count)].astype(jnp.float32)
        b = white_ref[pl.ds(base + shift, own_count)].astype(jnp.float32)
        ar, ai, br, bi = a[:, :half], a[:, half:], b[:, :half], b[:, half:]
        out_ref[i, 0] = window_sum(ar * br + ai * bi)
        out_ref[i, 1] = window_sum(ai * br - ar * bi)
        return carry

    lax.fori_loop(0, group, one_offset, 0)


def cross_spectra(white_all, pair_offsets, base, own_count):
    rows, bins = white_all.shape[1], white_all.shape[2]
    band_span = pair_offsets.shape[0]
    group = math.gcd(band_span, 8)
    kernel = functools.partial(cross_kernel, group=group, own_count=own_count, half=rows // 2)
    return pl.pallas_call(
        kernel,
        grid_spec=pltpu.PrefetchScalarGridSpec(
            num_scalar_prefetch=2,
            grid=(band_span // group,),
            in_specs=[pl.BlockSpec(white_all.shape, lambda g, offs, b: (0, 0, 0))],
            out_specs=pl.BlockSpec((group, 2, own_count, bins), lambda g, offs, b: (g, 0, 0, 0)),
        ),
        out_shape=jax.ShapeDtypeStruct((band_span, 2, own_count, bins), jnp.float32),
        compiler_params=pltpu.CompilerParams(vmem_limit_bytes=48 * 1024 * 1024),
        cost_estimate=pl.CostEstimate(
            flops=8 * band_span * own_count * rows * bins,
            transcendentals=0,
            bytes_accessed=white_all.size * 2 + band_span * 2 * own_count * bins * 4,
        ),
    )(pair_offsets, base, white_all)


def small_table(kept_bins, rows):
    fine_count = 1 << ((rows.bit_length() - 1) // 2)
    coarse_count = rows // fine_count

    def angles(step, count):
        index = step * jnp.arange(count, dtype=jnp.int32)
        return jnp.mod(index[:, None] * kept_bins[None, :], SAMPLES).astype(jnp.float32) * (
            2.0 * math.pi / SAMPLES
        )

    fine = angles(1, fine_count)[None, :, :]
    coarse = angles(fine_count, coarse_count)[:, None, :]
    cos_f, sin_f, cos_c, sin_c = jnp.cos(fine), jnp.sin(fine), jnp.cos(coarse), jnp.sin(coarse)
    cos_t = cos_f * cos_c - sin_f * sin_c
    sin_t = sin_f * cos_c + cos_f * sin_c
    table = jnp.concatenate([cos_t, -sin_t], axis=-1)
    return table.reshape(rows, 2 * kept_bins.shape[0]).astype(jnp.bfloat16)


def forward_spectra(record_rows, kept_bins):
    row_count, samples = record_rows.shape
    bin_count = kept_bins.shape[0]
    block_count = 4
    block_len = samples // block_count
    lhs = jnp.transpose(record_rows.reshape(row_count, block_count, block_len), (1, 0, 2))
    prod = jnp.dot(
        lhs.reshape(block_count * row_count, block_len),
        small_table(kept_bins, block_len),
        preferred_element_type=jnp.float32,
    ).reshape(block_count, row_count, 2, bin_count)
    turns = jnp.mod(
        jnp.arange(block_count, dtype=jnp.int32)[:, None] * jnp.mod(kept_bins, block_count)[None, :],
        block_count,
    ).astype(jnp.float32) * (2.0 * math.pi / block_count)
    tw_re = jnp.round(jnp.cos(turns))[:, None, :]
    tw_im = jnp.round(-jnp.sin(turns))[:, None, :]
    p_re, p_im = prod[:, :, 0], prod[:, :, 1]
    real_part = jnp.sum(tw_re * p_re - tw_im * p_im, axis=0)
    imag_part = jnp.sum(tw_re * p_im + tw_im * p_re, axis=0)
    return jnp.concatenate([real_part, imag_part], axis=-1)


def local(records, kept_bins, pair_offsets):
    ch_dev, win_dev, samples = records.shape
    bin_count = kept_bins.shape[0]
    band_span = pair_offsets.shape[0]
    record_rows = jnp.transpose(records, (1, 0, 2)).reshape(win_dev * ch_dev, samples)
    spectra = forward_spectra(record_rows, kept_bins)
    white = whiten(spectra).reshape(win_dev, ch_dev, 2, bin_count)
    freq_white = lax.all_to_all(white, "gy", split_axis=3, concat_axis=0, tiled=True)
    windows = freq_white.shape[0]
    shard_bins = freq_white.shape[3]
    rows_white = jnp.transpose(freq_white, (1, 2, 0, 3)).reshape(ch_dev, 2 * windows, shard_bins)
    gx_count = lax.axis_size("gx")
    needed = -(-band_span // ch_dev)
    blocks = [rows_white]
    for shift in range(1, min(needed, gx_count - 1) + 1):
        pairs = [(src, src - shift) for src in range(shift, gx_count)]
        blocks.append(lax.ppermute(rows_white, "gx", perm=pairs))
    missing = needed + 1 - len(blocks)
    if missing > 0:
        blocks.append(jnp.zeros((missing * ch_dev,) + rows_white.shape[1:], rows_white.dtype))
    padded = jnp.concatenate(blocks, axis=0)
    base = jnp.zeros((1,), jnp.int32)
    gy_count = lax.axis_size("gy")
    off_dev = band_span // gy_count
    me = lax.axis_index("gy")
    offsets = pair_offsets.astype(jnp.int32)
    inverse = inverse_table(kept_bins)
    norm_scale = 0.5 / math.sqrt(windows * bin_count)
    lagged = None
    for shift in list(range(1, gy_count)) + [0]:
        dest = lax.rem(me + shift, gy_count)
        part = cross_spectra(
            padded, lax.dynamic_slice_in_dim(offsets, dest * off_dev, off_dev), base, ch_dev
        ).astype(jnp.bfloat16)
        if shift:
            pairs = [(src, (src + shift) % gy_count) for src in range(gy_count)]
            part = lax.ppermute(part, "gy", perm=pairs)
        origin = lax.rem(me + gy_count - shift, gy_count)
        rows = lax.dynamic_slice_in_dim(inverse, origin * shard_bins, shard_bins, 1)
        term = jnp.einsum("opck,pkl->ocl", part, rows, preferred_element_type=jnp.float32)
        lagged = term if lagged is None else lagged + term
    lagged = lagged * norm_scale
    return lagged.astype(jnp.bfloat16)


def solution(mesh):
    return jax.shard_map(
        local,
        mesh=mesh,
        in_specs=(P("gx", "gy", None), P(), P()),
        out_specs=P("gy", "gx", None),
        check_vma=False,
    )
```

```python
import functools
import math

import jax
import jax.numpy as jnp
from jax import lax
from jax.experimental import pallas as pl
from jax.experimental.pallas import tpu as pltpu
from jax.sharding import PartitionSpec as P

SAMPLES = 8192
LAGS = 512


def inverse_table(kept_bins):
    fine_count = 32
    coarse_count = LAGS // fine_count

    def angles(index):
        return jnp.mod(kept_bins[:, None] * index[None, :], SAMPLES).astype(jnp.float32) * (
            2.0 * math.pi / SAMPLES
        )

    fine = angles(jnp.arange(fine_count, dtype=jnp.int32))[:, None, :]
    coarse = angles(fine_count * jnp.arange(coarse_count, dtype=jnp.int32) - LAGS // 2)[:, :, None]
    cos_f, sin_f, cos_c, sin_c = jnp.cos(fine), jnp.sin(fine), jnp.cos(coarse), jnp.sin(coarse)
    cos_t = (cos_f * cos_c - sin_f * sin_c).reshape(kept_bins.shape[0], LAGS)
    sin_t = (sin_f * cos_c + cos_f * sin_c).reshape(kept_bins.shape[0], LAGS)
    return jnp.stack([cos_t, -sin_t], axis=0).astype(jnp.bfloat16)


def whiten(spectra):
    mean_power = jnp.mean(spectra * spectra, axis=-1, keepdims=True)
    return (spectra * lax.rsqrt(mean_power + 1e-06)).astype(jnp.bfloat16)


def cross_kernel(offsets_ref, base_ref, white_ref, out_ref, *, group, own_count, half):
    step = pl.program_id(0)
    base = base_ref[0]
    own = [white_ref[base + c].astype(jnp.float32) for c in range(own_count)]

    def one_offset(i, carry):
        shift = offsets_ref[step * group + i]
        for c in range(own_count):
            a = own[c]
            b = white_ref[base + c + shift].astype(jnp.float32)
            ar, ai, br, bi = a[:half], a[half:], b[:half], b[half:]
            out_ref[i, 0, pl.ds(c, 1), :] = jnp.sum(ar * br + ai * bi, axis=0, keepdims=True)
            out_ref[i, 1, pl.ds(c, 1), :] = jnp.sum(ai * br - ar * bi, axis=0, keepdims=True)
        return carry

    lax.fori_loop(0, group, one_offset, 0)


def cross_spectra(white_all, pair_offsets, base, own_count):
    rows, bins = white_all.shape[1], white_all.shape[2]
    band_span = pair_offsets.shape[0]
    group = math.gcd(band_span, 8)
    kernel = functools.partial(cross_kernel, group=group, own_count=own_count, half=rows // 2)
    return pl.pallas_call(
        kernel,
        grid_spec=pltpu.PrefetchScalarGridSpec(
            num_scalar_prefetch=2,
            grid=(band_span // group,),
            in_specs=[pl.BlockSpec(white_all.shape, lambda g, offs, b: (0, 0, 0))],
            out_specs=pl.BlockSpec((group, 2, own_count, bins), lambda g, offs, b: (g, 0, 0, 0)),
        ),
        out_shape=jax.ShapeDtypeStruct((band_span, 2, own_count, bins), jnp.float32),
        compiler_params=pltpu.CompilerParams(vmem_limit_bytes=48 * 1024 * 1024),
        cost_estimate=pl.CostEstimate(
            flops=8 * band_span * own_count * rows * bins,
            transcendentals=0,
            bytes_accessed=white_all.size * 2 + band_span * 2 * own_count * bins * 4,
        ),
    )(pair_offsets, base, white_all)


def small_table(kept_bins, rows):
    fine_count = 1 << ((rows.bit_length() - 1) // 2)
    coarse_count = rows // fine_count

    def angles(step, count):
        index = step * jnp.arange(count, dtype=jnp.int32)
        return jnp.mod(index[:, None] * kept_bins[None, :], SAMPLES).astype(jnp.float32) * (
            2.0 * math.pi / SAMPLES
        )

    fine = angles(1, fine_count)[None, :, :]
    coarse = angles(fine_count, coarse_count)[:, None, :]
    cos_f, sin_f, cos_c, sin_c = jnp.cos(fine), jnp.sin(fine), jnp.cos(coarse), jnp.sin(coarse)
    cos_t = cos_f * cos_c - sin_f * sin_c
    sin_t = sin_f * cos_c + cos_f * sin_c
    table = jnp.concatenate([cos_t, -sin_t], axis=-1)
    return table.reshape(rows, 2 * kept_bins.shape[0]).astype(jnp.bfloat16)


def forward_spectra(record_rows, kept_bins):
    row_count, samples = record_rows.shape
    bin_count = kept_bins.shape[0]
    block_count = 4
    block_len = samples // block_count
    prod = jnp.dot(
        record_rows.reshape(row_count * block_count, block_len),
        small_table(kept_bins, block_len),
        preferred_element_type=jnp.float32,
    ).reshape(row_count, block_count, 2, bin_count)
    turns = jnp.mod(
        jnp.arange(block_count, dtype=jnp.int32)[:, None] * jnp.mod(kept_bins, block_count)[None, :],
        block_count,
    ).astype(jnp.float32) * (2.0 * math.pi / block_count)
    tw_re = jnp.round(jnp.cos(turns))[None]
    tw_im = jnp.round(-jnp.sin(turns))[None]
    p_re, p_im = prod[:, :, 0], prod[:, :, 1]
    real_part = jnp.sum(tw_re * p_re - tw_im * p_im, axis=1)
    imag_part = jnp.sum(tw_re * p_im + tw_im * p_re, axis=1)
    return jnp.concatenate([real_part, imag_part], axis=-1)


def local(records, kept_bins, pair_offsets):
    ch_dev, win_dev, samples = records.shape
    bin_count = kept_bins.shape[0]
    band_span = pair_offsets.shape[0]
    spectra = forward_spectra(records.reshape(ch_dev * win_dev, samples), kept_bins)
    white = whiten(spectra).reshape(ch_dev, win_dev, 2, bin_count)
    freq_white = lax.all_to_all(white, "gy", split_axis=3, concat_axis=1, tiled=True)
    windows = freq_white.shape[1]
    shard_bins = freq_white.shape[3]
    rows_white = jnp.transpose(freq_white, (0, 2, 1, 3)).reshape(ch_dev, 2 * windows, shard_bins)
    gx_count = lax.axis_size("gx")
    needed = -(-band_span // ch_dev)
    blocks = [rows_white]
    for shift in range(1, min(needed, gx_count - 1) + 1):
        pairs = [(src, src - shift) for src in range(shift, gx_count)]
        blocks.append(lax.ppermute(rows_white, "gx", perm=pairs))
    missing = needed + 1 - len(blocks)
    if missing > 0:
        blocks.append(jnp.zeros((missing * ch_dev,) + rows_white.shape[1:], rows_white.dtype))
    padded = jnp.concatenate(blocks, axis=0)
    base = jnp.zeros((1,), jnp.int32)
    gy_count = lax.axis_size("gy")
    off_dev = band_span // gy_count
    me = lax.axis_index("gy")
    offsets = pair_offsets.astype(jnp.int32)
    inverse = inverse_table(kept_bins)
    norm_scale = 0.5 / math.sqrt(windows * bin_count)
    lagged = None
    for shift in list(range(1, gy_count)) + [0]:
        dest = lax.rem(me + shift, gy_count)
        part = cross_spectra(
            padded, lax.dynamic_slice_in_dim(offsets, dest * off_dev, off_dev), base, ch_dev
        ).astype(jnp.bfloat16)
        if shift:
            pairs = [(src, (src + shift) % gy_count) for src in range(gy_count)]
            part = lax.ppermute(part, "gy", perm=pairs)
        origin = lax.rem(me + gy_count - shift, gy_count)
        rows = lax.dynamic_slice_in_dim(inverse, origin * shard_bins, shard_bins, 1)
        term = jnp.einsum("opck,pkl->ocl", part, rows, preferred_element_type=jnp.float32)
        lagged = term if lagged is None else lagged + term
    lagged = lagged * norm_scale
    return lagged.astype(jnp.bfloat16)


def solution(mesh):
    return jax.shard_map(
        local,
        mesh=mesh,
        in_specs=(P("gx", "gy", None), P(), P()),
        out_specs=P("gy", "gx", None),
        check_vma=False,
    )
```

```python
import functools
import math

import jax
import jax.numpy as jnp
from jax import lax
from jax.experimental import pallas as pl
from jax.experimental.pallas import tpu as pltpu
from jax.sharding import PartitionSpec as P

SAMPLES = 8192
LAGS = 512


def inverse_table(kept_bins):
    fine_count = 32
    coarse_count = LAGS // fine_count

    def angles(index):
        return jnp.mod(kept_bins[:, None] * index[None, :], SAMPLES).astype(jnp.float32) * (
            2.0 * math.pi / SAMPLES
        )

    fine = angles(jnp.arange(fine_count, dtype=jnp.int32))[:, None, :]
    coarse = angles(fine_count * jnp.arange(coarse_count, dtype=jnp.int32) - LAGS // 2)[:, :, None]
    cos_f, sin_f, cos_c, sin_c = jnp.cos(fine), jnp.sin(fine), jnp.cos(coarse), jnp.sin(coarse)
    cos_t = (cos_f * cos_c - sin_f * sin_c).reshape(kept_bins.shape[0], LAGS)
    sin_t = (sin_f * cos_c + cos_f * sin_c).reshape(kept_bins.shape[0], LAGS)
    return jnp.stack([cos_t, -sin_t], axis=0).astype(jnp.bfloat16)


def whiten(spectra):
    mean_power = jnp.mean(spectra * spectra, axis=-1, keepdims=True)
    return (spectra * lax.rsqrt(mean_power + 1e-06)).astype(jnp.bfloat16)


def cross_kernel(offsets_ref, base_ref, white_ref, out_ref, *, group, own_count, half):
    step = pl.program_id(0)
    base = base_ref[0]
    own = [white_ref[base + c].astype(jnp.float32) for c in range(own_count)]

    def one_offset(i, carry):
        shift = offsets_ref[step * group + i]
        for c in range(own_count):
            a = own[c]
            b = white_ref[base + c + shift].astype(jnp.float32)
            ar, ai, br, bi = a[:half], a[half:], b[:half], b[half:]
            out_ref[i, 0, pl.ds(c, 1), :] = jnp.sum(ar * br + ai * bi, axis=0, keepdims=True)
            out_ref[i, 1, pl.ds(c, 1), :] = jnp.sum(ai * br - ar * bi, axis=0, keepdims=True)
        return carry

    lax.fori_loop(0, group, one_offset, 0)


def cross_spectra(white_all, pair_offsets, base, own_count):
    rows, bins = white_all.shape[1], white_all.shape[2]
    band_span = pair_offsets.shape[0]
    group = math.gcd(band_span, 8)
    kernel = functools.partial(cross_kernel, group=group, own_count=own_count, half=rows // 2)
    return pl.pallas_call(
        kernel,
        grid_spec=pltpu.PrefetchScalarGridSpec(
            num_scalar_prefetch=2,
            grid=(band_span // group,),
            in_specs=[pl.BlockSpec(white_all.shape, lambda g, offs, b: (0, 0, 0))],
            out_specs=pl.BlockSpec((group, 2, own_count, bins), lambda g, offs, b: (g, 0, 0, 0)),
        ),
        out_shape=jax.ShapeDtypeStruct((band_span, 2, own_count, bins), jnp.float32),
        compiler_params=pltpu.CompilerParams(vmem_limit_bytes=48 * 1024 * 1024),
        cost_estimate=pl.CostEstimate(
            flops=8 * band_span * own_count * rows * bins,
            transcendentals=0,
            bytes_accessed=white_all.size * 2 + band_span * 2 * own_count * bins * 4,
        ),
    )(pair_offsets, base, white_all)


def small_table(kept_bins, rows):
    fine_count = 1 << ((rows.bit_length() - 1) // 2)
    coarse_count = rows // fine_count

    def angles(step, count):
        index = step * jnp.arange(count, dtype=jnp.int32)
        return jnp.mod(index[:, None] * kept_bins[None, :], SAMPLES).astype(jnp.float32) * (
            2.0 * math.pi / SAMPLES
        )

    fine = angles(1, fine_count)[None, :, :]
    coarse = angles(fine_count, coarse_count)[:, None, :]
    cos_f, sin_f, cos_c, sin_c = jnp.cos(fine), jnp.sin(fine), jnp.cos(coarse), jnp.sin(coarse)
    cos_t = cos_f * cos_c - sin_f * sin_c
    sin_t = sin_f * cos_c + cos_f * sin_c
    table = jnp.concatenate([cos_t, -sin_t], axis=-1)
    return table.reshape(rows, 2 * kept_bins.shape[0]).astype(jnp.bfloat16)


def forward_spectra(record_rows, kept_bins):
    row_count, samples = record_rows.shape
    bin_count = kept_bins.shape[0]
    block_count = 4
    block_len = samples // block_count
    prod = jnp.dot(
        record_rows.reshape(row_count * block_count, block_len),
        small_table(kept_bins, block_len),
        preferred_element_type=jnp.float32,
    ).reshape(row_count, block_count, 2, bin_count)
    turns = jnp.mod(
        jnp.arange(block_count, dtype=jnp.int32)[:, None] * jnp.mod(kept_bins, block_count)[None, :],
        block_count,
    ).astype(jnp.float32) * (2.0 * math.pi / block_count)
    tw_re = jnp.round(jnp.cos(turns))[None]
    tw_im = jnp.round(-jnp.sin(turns))[None]
    p_re, p_im = prod[:, :, 0], prod[:, :, 1]
    real_part = jnp.sum(tw_re * p_re - tw_im * p_im, axis=1)
    imag_part = jnp.sum(tw_re * p_im + tw_im * p_re, axis=1)
    return jnp.concatenate([real_part, imag_part], axis=-1)


def local(records, kept_bins, pair_offsets):
    ch_dev, win_dev, samples = records.shape
    bin_count = kept_bins.shape[0]
    band_span = pair_offsets.shape[0]
    spectra = forward_spectra(records.reshape(ch_dev * win_dev, samples), kept_bins)
    white = whiten(spectra).reshape(ch_dev, win_dev, 2, bin_count)
    freq_white = lax.all_to_all(white, "gy", split_axis=3, concat_axis=1, tiled=True)
    windows = freq_white.shape[1]
    shard_bins = freq_white.shape[3]
    rows_white = jnp.transpose(freq_white, (0, 2, 1, 3)).reshape(ch_dev, 2 * windows, shard_bins)
    gx_count = lax.axis_size("gx")
    needed = -(-band_span // ch_dev)
    hop = 4
    top = min(needed, gx_count - 1)
    blocks = [rows_white]
    relayed = None
    for shift in range(1, top + 1):
        if shift < hop:
            pairs = [(src, src - shift) for src in range(shift, gx_count)]
            blocks.append(lax.ppermute(rows_white, "gx", perm=pairs))
        elif shift == hop:
            pairs = [(src, src - hop) for src in range(hop, gx_count)]
            relayed = lax.ppermute(rows_white, "gx", perm=pairs)
            blocks.append(relayed)
        else:
            step = shift - hop
            pairs = [(src, src - step) for src in range(step, gx_count - hop)]
            blocks.append(lax.ppermute(relayed, "gx", perm=pairs))
    missing = needed + 1 - len(blocks)
    if missing > 0:
        blocks.append(jnp.zeros((missing * ch_dev,) + rows_white.shape[1:], rows_white.dtype))
    padded = jnp.concatenate(blocks, axis=0)
    base = jnp.zeros((1,), jnp.int32)
    gy_count = lax.axis_size("gy")
    off_dev = band_span // gy_count
    me = lax.axis_index("gy")
    offsets = pair_offsets.astype(jnp.int32)
    inverse = inverse_table(kept_bins)
    norm_scale = 0.5 / math.sqrt(windows * bin_count)
    lagged = None
    for shift in list(range(1, gy_count)) + [0]:
        dest = lax.rem(me + shift, gy_count)
        part = cross_spectra(
            padded, lax.dynamic_slice_in_dim(offsets, dest * off_dev, off_dev), base, ch_dev
        ).astype(jnp.bfloat16)
        if shift:
            pairs = [(src, (src + shift) % gy_count) for src in range(gy_count)]
            part = lax.ppermute(part, "gy", perm=pairs)
        origin = lax.rem(me + gy_count - shift, gy_count)
        rows = lax.dynamic_slice_in_dim(inverse, origin * shard_bins, shard_bins, 1)
        term = jnp.einsum("opck,pkl->ocl", part, rows, preferred_element_type=jnp.float32)
        lagged = term if lagged is None else lagged + term
    lagged = lagged * norm_scale
    return lagged.astype(jnp.bfloat16)


def solution(mesh):
    return jax.shard_map(
        local,
        mesh=mesh,
        in_specs=(P("gx", "gy", None), P(), P()),
        out_specs=P("gy", "gx", None),
        check_vma=False,
    )
```

```python
import functools
import math

import jax
import jax.numpy as jnp
from jax import lax
from jax.experimental import pallas as pl
from jax.experimental.pallas import tpu as pltpu
from jax.sharding import PartitionSpec as P

SAMPLES = 8192
LAGS = 512


def inverse_table(kept_bins):
    fine_count = 32
    coarse_count = LAGS // fine_count

    def angles(index):
        return jnp.mod(kept_bins[:, None] * index[None, :], SAMPLES).astype(jnp.float32) * (
            2.0 * math.pi / SAMPLES
        )

    fine = angles(jnp.arange(fine_count, dtype=jnp.int32))[:, None, :]
    coarse = angles(fine_count * jnp.arange(coarse_count, dtype=jnp.int32) - LAGS // 2)[:, :, None]
    cos_f, sin_f, cos_c, sin_c = jnp.cos(fine), jnp.sin(fine), jnp.cos(coarse), jnp.sin(coarse)
    cos_t = (cos_f * cos_c - sin_f * sin_c).reshape(kept_bins.shape[0], LAGS)
    sin_t = (sin_f * cos_c + cos_f * sin_c).reshape(kept_bins.shape[0], LAGS)
    return jnp.stack([cos_t, -sin_t], axis=0).astype(jnp.bfloat16)


def whiten(spectra):
    mean_power = jnp.mean(spectra * spectra, axis=-1, keepdims=True)
    return (spectra * lax.rsqrt(mean_power + 1e-06)).astype(jnp.bfloat16)


def cross_kernel(offsets_ref, white_ref, *rest, group, own_count, half, first_row, end_row):
    if len(rest) == 2:
        earlier_ref, out_ref = rest
    else:
        earlier_ref, (out_ref,) = None, rest
    step = pl.program_id(0)
    own = [white_ref[c].astype(jnp.float32) for c in range(own_count)]

    def one_offset(i, carry):
        shift = offsets_ref[step * group + i]
        meets = jnp.logical_and(shift + own_count > first_row, shift < end_row)

        @pl.when(meets)
        def _():
            for c in range(own_count):
                a = own[c]
                b = white_ref[c + shift].astype(jnp.float32)
                ar, ai, br, bi = a[:half], a[half:], b[:half], b[half:]
                real_part = jnp.sum(ar * br + ai * bi, axis=0, keepdims=True)
                imag_part = jnp.sum(ai * br - ar * bi, axis=0, keepdims=True)
                if earlier_ref is not None:
                    real_part = real_part + earlier_ref[i, 0, pl.ds(c, 1), :]
                    imag_part = imag_part + earlier_ref[i, 1, pl.ds(c, 1), :]
                out_ref[i, 0, pl.ds(c, 1), :] = real_part
                out_ref[i, 1, pl.ds(c, 1), :] = imag_part

        @pl.when(jnp.logical_not(meets))
        def _():
            if earlier_ref is None:
                out_ref[i] = jnp.zeros(out_ref.shape[1:], out_ref.dtype)
            else:
                out_ref[i] = earlier_ref[i]

        return carry

    lax.fori_loop(0, group, one_offset, 0)


def cross_spectra(white_all, pair_offsets, own_count, first_row, end_row, earlier=None):
    rows, bins = white_all.shape[1], white_all.shape[2]
    band_span = pair_offsets.shape[0]
    group = math.gcd(band_span, 8)
    kernel = functools.partial(
        cross_kernel, group=group, own_count=own_count, half=rows // 2, first_row=first_row, end_row=end_row
    )
    block = pl.BlockSpec((group, 2, own_count, bins), lambda g, offs: (g, 0, 0, 0))
    operands = [pair_offsets, white_all] + ([] if earlier is None else [earlier])
    return pl.pallas_call(
        kernel,
        grid_spec=pltpu.PrefetchScalarGridSpec(
            num_scalar_prefetch=1,
            grid=(band_span // group,),
            in_specs=[pl.BlockSpec(white_all.shape, lambda g, offs: (0, 0, 0))]
            + ([] if earlier is None else [block]),
            out_specs=block,
        ),
        out_shape=jax.ShapeDtypeStruct((band_span, 2, own_count, bins), jnp.float32),
        compiler_params=pltpu.CompilerParams(vmem_limit_bytes=48 * 1024 * 1024),
        cost_estimate=pl.CostEstimate(
            flops=1024 * band_span * own_count * rows * bins,
            transcendentals=0,
            bytes_accessed=white_all.size * 2 + band_span * 2 * own_count * bins * 8,
        ),
    )(*operands)


def small_table(kept_bins, rows):
    fine_count = 1 << ((rows.bit_length() - 1) // 2)
    coarse_count = rows // fine_count

    def angles(step, count):
        index = step * jnp.arange(count, dtype=jnp.int32)
        return jnp.mod(index[:, None] * kept_bins[None, :], SAMPLES).astype(jnp.float32) * (
            2.0 * math.pi / SAMPLES
        )

    fine = angles(1, fine_count)[None, :, :]
    coarse = angles(fine_count, coarse_count)[:, None, :]
    cos_f, sin_f, cos_c, sin_c = jnp.cos(fine), jnp.sin(fine), jnp.cos(coarse), jnp.sin(coarse)
    cos_t = cos_f * cos_c - sin_f * sin_c
    sin_t = sin_f * cos_c + cos_f * sin_c
    table = jnp.concatenate([cos_t, -sin_t], axis=-1)
    return table.reshape(rows, 2 * kept_bins.shape[0]).astype(jnp.bfloat16)


def forward_spectra(record_rows, kept_bins):
    row_count, samples = record_rows.shape
    bin_count = kept_bins.shape[0]
    block_count = 4
    block_len = samples // block_count
    lhs = jnp.transpose(record_rows.reshape(row_count, block_count, block_len), (1, 0, 2))
    prod = jnp.dot(
        lhs.reshape(block_count * row_count, block_len),
        small_table(kept_bins, block_len),
        preferred_element_type=jnp.float32,
    ).reshape(block_count, row_count, 2, bin_count)
    turns = jnp.mod(
        jnp.arange(block_count, dtype=jnp.int32)[:, None] * jnp.mod(kept_bins, block_count)[None, :],
        block_count,
    ).astype(jnp.float32) * (2.0 * math.pi / block_count)
    tw_re = jnp.round(jnp.cos(turns))[:, None, :]
    tw_im = jnp.round(-jnp.sin(turns))[:, None, :]
    p_re, p_im = prod[:, :, 0], prod[:, :, 1]
    real_part = jnp.sum(tw_re * p_re - tw_im * p_im, axis=0)
    imag_part = jnp.sum(tw_re * p_im + tw_im * p_re, axis=0)
    return jnp.concatenate([real_part, imag_part], axis=-1)


def local(records, kept_bins, pair_offsets):
    ch_dev, win_dev, samples = records.shape
    bin_count = kept_bins.shape[0]
    band_span = pair_offsets.shape[0]
    record_rows = jnp.transpose(records, (1, 0, 2)).reshape(win_dev * ch_dev, samples)
    spectra = forward_spectra(record_rows, kept_bins)
    white = whiten(spectra).reshape(win_dev, ch_dev, 2, bin_count)
    freq_white = lax.all_to_all(white, "gy", split_axis=3, concat_axis=0, tiled=True)
    windows = freq_white.shape[0]
    shard_bins = freq_white.shape[3]
    rows_white = jnp.transpose(freq_white, (1, 2, 0, 3)).reshape(ch_dev, 2 * windows, shard_bins)
    gx_count = lax.axis_size("gx")
    needed = -(-band_span // ch_dev)
    real_count = min(needed, gx_count - 1) + 1
    near_count = min(4, real_count)
    blocks = [rows_white]
    source = rows_white
    for shift in range(1, real_count):
        pairs = [(src, src - shift) for src in range(shift, gx_count)]
        blocks.append(lax.ppermute(source, "gx", perm=pairs))
    zero_block = jnp.zeros_like(rows_white)
    blocks += [zero_block] * (needed + 1 - len(blocks))
    near = jnp.concatenate(blocks[:near_count] + [zero_block] * (len(blocks) - near_count), axis=0)
    split_row = near_count * ch_dev
    end_row = len(blocks) * ch_dev
    gy_count = lax.axis_size("gy")
    off_dev = band_span // gy_count
    me = lax.axis_index("gy")
    offsets = pair_offsets.astype(jnp.int32)
    inverse = inverse_table(kept_bins)
    norm_scale = 0.5 / math.sqrt(windows * bin_count)
    shifts = list(range(1, gy_count)) + [0]
    dest_offsets = [
        lax.dynamic_slice_in_dim(offsets, lax.rem(me + shift, gy_count) * off_dev, off_dev) for shift in shifts
    ]
    near_parts = [cross_spectra(near, offs, ch_dev, 0, split_row) for offs in dest_offsets]
    far_blocks, near_parts = lax.optimization_barrier((blocks[near_count:], near_parts))
    far = jnp.concatenate([rows_white] + [zero_block] * (near_count - 1) + list(far_blocks), axis=0)
    lagged = None
    for shift, offs, near_part in zip(shifts, dest_offsets, near_parts):
        part = cross_spectra(far, offs, ch_dev, split_row, end_row, near_part).astype(jnp.bfloat16)
        if shift:
            pairs = [(src, (src + shift) % gy_count) for src in range(gy_count)]
            part = lax.ppermute(part, "gy", perm=pairs)
        origin = lax.rem(me + gy_count - shift, gy_count)
        rows = lax.dynamic_slice_in_dim(inverse, origin * shard_bins, shard_bins, 1)
        term = jnp.einsum("opck,pkl->ocl", part, rows, preferred_element_type=jnp.float32)
        lagged = term if lagged is None else lagged + term
    lagged = lagged * norm_scale
    return lagged.astype(jnp.bfloat16)


def solution(mesh):
    return jax.shard_map(
        local,
        mesh=mesh,
        in_specs=(P("gx", "gy", None), P(), P()),
        out_specs=P("gy", "gx", None),
        check_vma=False,
    )
```

```python
import functools
import math

import jax
import jax.numpy as jnp
from jax import lax
from jax.experimental import pallas as pl
from jax.experimental.pallas import tpu as pltpu
from jax.sharding import PartitionSpec as P

SAMPLES = 8192
LAGS = 512


def inverse_table(kept_bins):
    fine_count = 32
    coarse_count = LAGS // fine_count

    def angles(index):
        return jnp.mod(kept_bins[:, None] * index[None, :], SAMPLES).astype(jnp.float32) * (
            2.0 * math.pi / SAMPLES
        )

    fine = angles(jnp.arange(fine_count, dtype=jnp.int32))[:, None, :]
    coarse = angles(fine_count * jnp.arange(coarse_count, dtype=jnp.int32) - LAGS // 2)[:, :, None]
    cos_f, sin_f, cos_c, sin_c = jnp.cos(fine), jnp.sin(fine), jnp.cos(coarse), jnp.sin(coarse)
    cos_t = (cos_f * cos_c - sin_f * sin_c).reshape(kept_bins.shape[0], LAGS)
    sin_t = (sin_f * cos_c + cos_f * sin_c).reshape(kept_bins.shape[0], LAGS)
    return jnp.stack([cos_t, -sin_t], axis=0).astype(jnp.bfloat16)


def whiten(spectra):
    mean_power = jnp.mean(spectra * spectra, axis=-1, keepdims=True)
    return (spectra * lax.rsqrt(mean_power + 1e-06)).astype(jnp.bfloat16)


def cross_kernel(offsets_ref, base_ref, white_ref, out_ref, *, group, own_count, half):
    step = pl.program_id(0)
    base = base_ref[0]
    own = [white_ref[base + c].astype(jnp.float32) for c in range(own_count)]

    def one_offset(i, carry):
        shift = offsets_ref[step * group + i]
        for c in range(own_count):
            a = own[c]
            b = white_ref[base + c + shift].astype(jnp.float32)
            ar, ai, br, bi = a[:half], a[half:], b[:half], b[half:]
            out_ref[i, 0, pl.ds(c, 1), :] = jnp.sum(ar * br + ai * bi, axis=0, keepdims=True)
            out_ref[i, 1, pl.ds(c, 1), :] = jnp.sum(ai * br - ar * bi, axis=0, keepdims=True)
        return carry

    lax.fori_loop(0, group, one_offset, 0)


def cross_spectra(white_all, pair_offsets, base, own_count):
    rows, bins = white_all.shape[1], white_all.shape[2]
    band_span = pair_offsets.shape[0]
    group = math.gcd(band_span, 8)
    kernel = functools.partial(cross_kernel, group=group, own_count=own_count, half=rows // 2)
    return pl.pallas_call(
        kernel,
        grid_spec=pltpu.PrefetchScalarGridSpec(
            num_scalar_prefetch=2,
            grid=(band_span // group,),
            in_specs=[pl.BlockSpec(white_all.shape, lambda g, offs, b: (0, 0, 0))],
            out_specs=pl.BlockSpec((group, 2, own_count, bins), lambda g, offs, b: (g, 0, 0, 0)),
        ),
        out_shape=jax.ShapeDtypeStruct((band_span, 2, own_count, bins), jnp.float32),
        compiler_params=pltpu.CompilerParams(vmem_limit_bytes=48 * 1024 * 1024),
        cost_estimate=pl.CostEstimate(
            flops=8 * band_span * own_count * rows * bins,
            transcendentals=0,
            bytes_accessed=white_all.size * 2 + band_span * 2 * own_count * bins * 4,
        ),
    )(pair_offsets, base, white_all)


def small_table(kept_bins, rows):
    fine_count = 1 << ((rows.bit_length() - 1) // 2)
    coarse_count = rows // fine_count

    def angles(step, count):
        index = step * jnp.arange(count, dtype=jnp.int32)
        return jnp.mod(index[:, None] * kept_bins[None, :], SAMPLES).astype(jnp.float32) * (
            2.0 * math.pi / SAMPLES
        )

    fine = angles(1, fine_count)[None, :, :]
    coarse = angles(fine_count, coarse_count)[:, None, :]
    cos_f, sin_f, cos_c, sin_c = jnp.cos(fine), jnp.sin(fine), jnp.cos(coarse), jnp.sin(coarse)
    cos_t = cos_f * cos_c - sin_f * sin_c
    sin_t = sin_f * cos_c + cos_f * sin_c
    table = jnp.concatenate([cos_t, -sin_t], axis=-1)
    return table.reshape(rows, 2 * kept_bins.shape[0]).astype(jnp.bfloat16)


def forward_spectra(record_rows, kept_bins):
    row_count, samples = record_rows.shape
    bin_count = kept_bins.shape[0]
    block_count = 4
    block_len = samples // block_count
    prod = jnp.dot(
        record_rows.reshape(row_count * block_count, block_len),
        small_table(kept_bins, block_len),
        preferred_element_type=jnp.float32,
    ).reshape(row_count, block_count, 2, bin_count)
    turns = jnp.mod(
        jnp.arange(block_count, dtype=jnp.int32)[:, None] * jnp.mod(kept_bins, block_count)[None, :],
        block_count,
    ).astype(jnp.float32) * (2.0 * math.pi / block_count)
    tw_re = jnp.round(jnp.cos(turns))[None]
    tw_im = jnp.round(-jnp.sin(turns))[None]
    p_re, p_im = prod[:, :, 0], prod[:, :, 1]
    real_part = jnp.sum(tw_re * p_re - tw_im * p_im, axis=1)
    imag_part = jnp.sum(tw_re * p_im + tw_im * p_re, axis=1)
    return jnp.concatenate([real_part, imag_part], axis=-1)


def local(records, kept_bins, pair_offsets):
    ch_dev, win_dev, samples = records.shape
    bin_count = kept_bins.shape[0]
    band_span = pair_offsets.shape[0]
    spectra = forward_spectra(records.reshape(ch_dev * win_dev, samples), kept_bins)
    white = whiten(spectra).reshape(ch_dev, win_dev, 2, bin_count)
    gy_count = lax.axis_size("gy")
    shard_bins = bin_count // gy_count
    me = lax.axis_index("gy")
    slots = []
    for shift in range(gy_count):
        dest = lax.rem(me + shift, gy_count)
        piece = lax.dynamic_slice_in_dim(white, dest * shard_bins, shard_bins, 3)
        if shift:
            piece = lax.ppermute(piece, "gy", perm=[(src, (src + shift) % gy_count) for src in range(gy_count)])
        slots.append(piece)
    freq_white = jnp.concatenate(slots, axis=1)
    windows = freq_white.shape[1]
    rows_white = jnp.transpose(freq_white, (0, 2, 1, 3)).reshape(ch_dev, 2 * windows, shard_bins)
    gx_count = lax.axis_size("gx")
    needed = -(-band_span // ch_dev)
    blocks = [rows_white]
    for shift in range(1, min(needed, gx_count - 1) + 1):
        pairs = [(src, src - shift) for src in range(shift, gx_count)]
        blocks.append(lax.ppermute(rows_white, "gx", perm=pairs))
    missing = needed + 1 - len(blocks)
    if missing > 0:
        blocks.append(jnp.zeros((missing * ch_dev,) + rows_white.shape[1:], rows_white.dtype))
    padded = jnp.concatenate(blocks, axis=0)
    base = jnp.zeros((1,), jnp.int32)
    gy_count = lax.axis_size("gy")
    off_dev = band_span // gy_count
    me = lax.axis_index("gy")
    offsets = pair_offsets.astype(jnp.int32)
    inverse = inverse_table(kept_bins)
    norm_scale = 0.5 / math.sqrt(windows * bin_count)
    lagged = None
    for shift in list(range(1, gy_count)) + [0]:
        dest = lax.rem(me + shift, gy_count)
        part = cross_spectra(
            padded, lax.dynamic_slice_in_dim(offsets, dest * off_dev, off_dev), base, ch_dev
        ).astype(jnp.bfloat16)
        if shift:
            pairs = [(src, (src + shift) % gy_count) for src in range(gy_count)]
            part = lax.ppermute(part, "gy", perm=pairs)
        origin = lax.rem(me + gy_count - shift, gy_count)
        rows = lax.dynamic_slice_in_dim(inverse, origin * shard_bins, shard_bins, 1)
        term = jnp.einsum("opck,pkl->ocl", part, rows, preferred_element_type=jnp.float32)
        lagged = term if lagged is None else lagged + term
    lagged = lagged * norm_scale
    return lagged.astype(jnp.bfloat16)


def solution(mesh):
    return jax.shard_map(
        local,
        mesh=mesh,
        in_specs=(P("gx", "gy", None), P(), P()),
        out_specs=P("gy", "gx", None),
        check_vma=False,
    )
```

```python
import functools
import math

import jax
import jax.numpy as jnp
from jax import lax
from jax.experimental import pallas as pl
from jax.experimental.pallas import tpu as pltpu
from jax.sharding import PartitionSpec as P

SAMPLES = 8192
LAGS = 512


def inverse_table(kept_bins):
    fine_count = 32
    coarse_count = LAGS // fine_count

    def angles(index):
        return jnp.mod(kept_bins[:, None] * index[None, :], SAMPLES).astype(jnp.float32) * (
            2.0 * math.pi / SAMPLES
        )

    fine = angles(jnp.arange(fine_count, dtype=jnp.int32))[:, None, :]
    coarse = angles(fine_count * jnp.arange(coarse_count, dtype=jnp.int32) - LAGS // 2)[:, :, None]
    cos_f, sin_f, cos_c, sin_c = jnp.cos(fine), jnp.sin(fine), jnp.cos(coarse), jnp.sin(coarse)
    cos_t = (cos_f * cos_c - sin_f * sin_c).reshape(kept_bins.shape[0], LAGS)
    sin_t = (sin_f * cos_c + cos_f * sin_c).reshape(kept_bins.shape[0], LAGS)
    return jnp.stack([cos_t, -sin_t], axis=0).astype(jnp.bfloat16)


def whiten(spectra):
    mean_power = jnp.mean(spectra * spectra, axis=-1, keepdims=True)
    return (spectra * lax.rsqrt(mean_power + 1e-06)).astype(jnp.bfloat16)


def cross_kernel(offsets_ref, base_ref, white_ref, out_ref, *, group, own_count, half):
    step = pl.program_id(0)
    base = base_ref[0]
    own = [white_ref[base + c].astype(jnp.float32) for c in range(own_count)]

    def one_offset(i, carry):
        shift = offsets_ref[step * group + i]
        for c in range(own_count):
            a = own[c]
            b = white_ref[base + c + shift].astype(jnp.float32)
            ar, ai, br, bi = a[:half], a[half:], b[:half], b[half:]
            out_ref[i, 0, pl.ds(c, 1), :] = jnp.sum(ar * br + ai * bi, axis=0, keepdims=True)
            out_ref[i, 1, pl.ds(c, 1), :] = jnp.sum(ai * br - ar * bi, axis=0, keepdims=True)
        return carry

    lax.fori_loop(0, group, one_offset, 0)


def cross_spectra(white_all, pair_offsets, base, own_count):
    rows, bins = white_all.shape[1], white_all.shape[2]
    band_span = pair_offsets.shape[0]
    group = math.gcd(band_span, 8)
    kernel = functools.partial(cross_kernel, group=group, own_count=own_count, half=rows // 2)
    return pl.pallas_call(
        kernel,
        grid_spec=pltpu.PrefetchScalarGridSpec(
            num_scalar_prefetch=2,
            grid=(band_span // group,),
            in_specs=[pl.BlockSpec(white_all.shape, lambda g, offs, b: (0, 0, 0))],
            out_specs=pl.BlockSpec((group, 2, own_count, bins), lambda g, offs, b: (g, 0, 0, 0)),
        ),
        out_shape=jax.ShapeDtypeStruct((band_span, 2, own_count, bins), jnp.float32),
        compiler_params=pltpu.CompilerParams(vmem_limit_bytes=48 * 1024 * 1024),
        cost_estimate=pl.CostEstimate(
            flops=8 * band_span * own_count * rows * bins,
            transcendentals=0,
            bytes_accessed=white_all.size * 2 + band_span * 2 * own_count * bins * 4,
        ),
    )(pair_offsets, base, white_all)


def small_table(kept_bins, rows):
    fine_count = 1 << ((rows.bit_length() - 1) // 2)
    coarse_count = rows // fine_count

    def angles(step, count):
        index = step * jnp.arange(count, dtype=jnp.int32)
        return jnp.mod(index[:, None] * kept_bins[None, :], SAMPLES).astype(jnp.float32) * (
            2.0 * math.pi / SAMPLES
        )

    fine = angles(1, fine_count)[None, :, :]
    coarse = angles(fine_count, coarse_count)[:, None, :]
    cos_f, sin_f, cos_c, sin_c = jnp.cos(fine), jnp.sin(fine), jnp.cos(coarse), jnp.sin(coarse)
    cos_t = cos_f * cos_c - sin_f * sin_c
    sin_t = sin_f * cos_c + cos_f * sin_c
    table = jnp.concatenate([cos_t, -sin_t], axis=-1)
    return table.reshape(rows, 2 * kept_bins.shape[0]).astype(jnp.bfloat16)


def forward_spectra(record_rows, kept_bins):
    row_count, samples = record_rows.shape
    bin_count = kept_bins.shape[0]
    block_count = 4
    block_len = samples // block_count
    prod = jnp.dot(
        record_rows.reshape(row_count * block_count, block_len),
        small_table(kept_bins, block_len),
        preferred_element_type=jnp.float32,
    ).reshape(row_count, block_count, 2, bin_count)
    turns = jnp.mod(
        jnp.arange(block_count, dtype=jnp.int32)[:, None] * jnp.mod(kept_bins, block_count)[None, :],
        block_count,
    ).astype(jnp.float32) * (2.0 * math.pi / block_count)
    tw_re = jnp.round(jnp.cos(turns))[None]
    tw_im = jnp.round(-jnp.sin(turns))[None]
    p_re, p_im = prod[:, :, 0], prod[:, :, 1]
    real_part = jnp.sum(tw_re * p_re - tw_im * p_im, axis=1)
    imag_part = jnp.sum(tw_re * p_im + tw_im * p_re, axis=1)
    return jnp.concatenate([real_part, imag_part], axis=-1)


def local(records, kept_bins, pair_offsets):
    ch_dev, win_dev, samples = records.shape
    bin_count = kept_bins.shape[0]
    band_span = pair_offsets.shape[0]
    spectra = forward_spectra(records.reshape(ch_dev * win_dev, samples), kept_bins)
    white = whiten(spectra).reshape(ch_dev, win_dev, 2, bin_count)
    gy_count = lax.axis_size("gy")
    shard_bins = bin_count // gy_count
    me = lax.axis_index("gy")
    slots = []
    for shift in range(gy_count):
        dest = lax.rem(me + shift, gy_count)
        piece = lax.dynamic_slice_in_dim(white, dest * shard_bins, shard_bins, 3)
        if shift:
            piece = lax.ppermute(piece, "gy", perm=[(src, (src + shift) % gy_count) for src in range(gy_count)])
        slots.append(piece)
    freq_white = jnp.concatenate(slots, axis=1)
    windows = freq_white.shape[1]
    rows_white = jnp.transpose(freq_white, (0, 2, 1, 3)).reshape(ch_dev, 2 * windows, shard_bins)
    gx_count = lax.axis_size("gx")
    needed = -(-band_span // ch_dev)
    blocks = [rows_white]
    for shift in range(1, min(needed, gx_count - 1) + 1):
        pairs = [(src, src - shift) for src in range(shift, gx_count)]
        blocks.append(lax.ppermute(rows_white, "gx", perm=pairs))
    missing = needed + 1 - len(blocks)
    if missing > 0:
        blocks.append(jnp.zeros((missing * ch_dev,) + rows_white.shape[1:], rows_white.dtype))
    padded = jnp.concatenate(blocks, axis=0)
    base = jnp.zeros((1,), jnp.int32)
    gy_count = lax.axis_size("gy")
    off_dev = band_span // gy_count
    me = lax.axis_index("gy")
    offsets = pair_offsets.astype(jnp.int32)
    norm_scale = 0.5 / math.sqrt(windows * bin_count)
    lagged = None
    for shift in list(range(1, gy_count)) + [0]:
        dest = lax.rem(me + shift, gy_count)
        part = cross_spectra(
            padded, lax.dynamic_slice_in_dim(offsets, dest * off_dev, off_dev), base, ch_dev
        ).astype(jnp.bfloat16)
        if shift:
            pairs = [(src, (src + shift) % gy_count) for src in range(gy_count)]
            part = lax.ppermute(part, "gy", perm=pairs)
        origin = lax.rem(me + gy_count - shift, gy_count)
        rows = inverse_table(lax.dynamic_slice_in_dim(kept_bins, origin * shard_bins, shard_bins))
        term = jnp.einsum("opck,pkl->ocl", part, rows, preferred_element_type=jnp.float32)
        lagged = term if lagged is None else lagged + term
    lagged = lagged * norm_scale
    return lagged.astype(jnp.bfloat16)


def solution(mesh):
    return jax.shard_map(
        local,
        mesh=mesh,
        in_specs=(P("gx", "gy", None), P(), P()),
        out_specs=P("gy", "gx", None),
        check_vma=False,
    )
```

```python
import functools
import math

import jax
import jax.numpy as jnp
from jax import lax
from jax.experimental import pallas as pl
from jax.experimental.pallas import tpu as pltpu
from jax.sharding import PartitionSpec as P

SAMPLES = 8192
LAGS = 512


def inverse_table(kept_bins):
    fine_count = 32
    coarse_count = LAGS // fine_count

    def angles(index):
        return jnp.mod(kept_bins[:, None] * index[None, :], SAMPLES).astype(jnp.float32) * (
            2.0 * math.pi / SAMPLES
        )

    fine = angles(jnp.arange(fine_count, dtype=jnp.int32))[:, None, :]
    coarse = angles(fine_count * jnp.arange(coarse_count, dtype=jnp.int32) - LAGS // 2)[:, :, None]
    cos_f, sin_f, cos_c, sin_c = jnp.cos(fine), jnp.sin(fine), jnp.cos(coarse), jnp.sin(coarse)
    cos_t = (cos_f * cos_c - sin_f * sin_c).reshape(kept_bins.shape[0], LAGS)
    sin_t = (sin_f * cos_c + cos_f * sin_c).reshape(kept_bins.shape[0], LAGS)
    return jnp.stack([cos_t, -sin_t], axis=0).astype(jnp.bfloat16)


def whiten(spectra):
    mean_power = jnp.mean(spectra * spectra, axis=-1, keepdims=True)
    return (spectra * lax.rsqrt(mean_power + 1e-06)).astype(jnp.bfloat16)


def cross_kernel(offsets_ref, base_ref, white_ref, out_ref, *, group, own_count, half):
    step = pl.program_id(0)
    base = base_ref[0]
    own = [white_ref[base + c].astype(jnp.float32) for c in range(own_count)]

    def one_offset(i, carry):
        shift = offsets_ref[step * group + i]
        for c in range(own_count):
            a = own[c]
            b = white_ref[base + c + shift].astype(jnp.float32)
            ar, ai, br, bi = a[:half], a[half:], b[:half], b[half:]
            out_ref[i, 0, pl.ds(c, 1), :] = jnp.sum(ar * br + ai * bi, axis=0, keepdims=True)
            out_ref[i, 1, pl.ds(c, 1), :] = jnp.sum(ai * br - ar * bi, axis=0, keepdims=True)
        return carry

    lax.fori_loop(0, group, one_offset, 0)


def cross_spectra(white_all, pair_offsets, base, own_count):
    rows, bins = white_all.shape[1], white_all.shape[2]
    band_span = pair_offsets.shape[0]
    group = math.gcd(band_span, 8)
    kernel = functools.partial(cross_kernel, group=group, own_count=own_count, half=rows // 2)
    return pl.pallas_call(
        kernel,
        grid_spec=pltpu.PrefetchScalarGridSpec(
            num_scalar_prefetch=2,
            grid=(band_span // group,),
            in_specs=[pl.BlockSpec(white_all.shape, lambda g, offs, b: (0, 0, 0))],
            out_specs=pl.BlockSpec((group, 2, own_count, bins), lambda g, offs, b: (g, 0, 0, 0)),
        ),
        out_shape=jax.ShapeDtypeStruct((band_span, 2, own_count, bins), jnp.float32),
        compiler_params=pltpu.CompilerParams(vmem_limit_bytes=48 * 1024 * 1024),
        cost_estimate=pl.CostEstimate(
            flops=8 * band_span * own_count * rows * bins,
            transcendentals=0,
            bytes_accessed=white_all.size * 4 + band_span * 2 * own_count * bins * 4,
        ),
    )(pair_offsets, base, white_all)


def small_table(kept_bins, rows):
    fine_count = 1 << ((rows.bit_length() - 1) // 2)
    coarse_count = rows // fine_count

    def angles(step, count):
        index = step * jnp.arange(count, dtype=jnp.int32)
        return jnp.mod(index[:, None] * kept_bins[None, :], SAMPLES).astype(jnp.float32) * (
            2.0 * math.pi / SAMPLES
        )

    fine = angles(1, fine_count)[None, :, :]
    coarse = angles(fine_count, coarse_count)[:, None, :]
    cos_f, sin_f, cos_c, sin_c = jnp.cos(fine), jnp.sin(fine), jnp.cos(coarse), jnp.sin(coarse)
    cos_t = cos_f * cos_c - sin_f * sin_c
    sin_t = sin_f * cos_c + cos_f * sin_c
    table = jnp.concatenate([cos_t, -sin_t], axis=-1)
    return table.reshape(rows, 2 * kept_bins.shape[0]).astype(jnp.bfloat16)


def forward_spectra(record_rows, kept_bins):
    row_count, samples = record_rows.shape
    bin_count = kept_bins.shape[0]
    block_count = 4
    block_len = samples // block_count
    prod = jnp.dot(
        record_rows.reshape(row_count * block_count, block_len),
        small_table(kept_bins, block_len),
        preferred_element_type=jnp.float32,
    ).reshape(row_count, block_count, 2, bin_count)
    turns = jnp.mod(
        jnp.arange(block_count, dtype=jnp.int32)[:, None] * jnp.mod(kept_bins, block_count)[None, :],
        block_count,
    ).astype(jnp.float32) * (2.0 * math.pi / block_count)
    tw_re = jnp.round(jnp.cos(turns))[None]
    tw_im = jnp.round(-jnp.sin(turns))[None]
    p_re, p_im = prod[:, :, 0], prod[:, :, 1]
    real_part = jnp.sum(tw_re * p_re - tw_im * p_im, axis=1)
    imag_part = jnp.sum(tw_re * p_im + tw_im * p_re, axis=1)
    return jnp.concatenate([real_part, imag_part], axis=-1)


def local(records, kept_bins, pair_offsets):
    ch_dev, win_dev, samples = records.shape
    bin_count = kept_bins.shape[0]
    band_span = pair_offsets.shape[0]
    spectra = forward_spectra(records.reshape(ch_dev * win_dev, samples), kept_bins)
    white = whiten(spectra).reshape(ch_dev, win_dev, 2, bin_count)
    gy_count = lax.axis_size("gy")
    shard_bins = bin_count // gy_count
    me = lax.axis_index("gy")
    slots = []
    for shift in range(gy_count):
        dest = lax.rem(me + shift, gy_count)
        piece = lax.dynamic_slice_in_dim(white, dest * shard_bins, shard_bins, 3)
        if shift:
            piece = lax.ppermute(piece, "gy", perm=[(src, (src + shift) % gy_count) for src in range(gy_count)])
        slots.append(piece)
    freq_white = jnp.concatenate(slots, axis=1)
    windows = freq_white.shape[1]
    rows_white = jnp.transpose(freq_white, (0, 2, 1, 3)).reshape(ch_dev, 2 * windows, shard_bins)
    gx_count = lax.axis_size("gx")
    needed = -(-band_span // ch_dev)
    blocks = [rows_white]
    for shift in range(1, min(needed, gx_count - 1) + 1):
        pairs = [(src, src - shift) for src in range(shift, gx_count)]
        blocks.append(lax.ppermute(rows_white, "gx", perm=pairs))
    missing = needed + 1 - len(blocks)
    if missing > 0:
        blocks.append(jnp.zeros((missing * ch_dev,) + rows_white.shape[1:], rows_white.dtype))
    padded = jnp.concatenate(blocks, axis=0).astype(jnp.float32)
    base = jnp.zeros((1,), jnp.int32)
    gy_count = lax.axis_size("gy")
    off_dev = band_span // gy_count
    me = lax.axis_index("gy")
    offsets = pair_offsets.astype(jnp.int32)
    inverse = inverse_table(kept_bins)
    norm_scale = 0.5 / math.sqrt(windows * bin_count)
    lagged = None
    for shift in list(range(1, gy_count)) + [0]:
        dest = lax.rem(me + shift, gy_count)
        part = cross_spectra(
            padded, lax.dynamic_slice_in_dim(offsets, dest * off_dev, off_dev), base, ch_dev
        ).astype(jnp.bfloat16)
        if shift:
            pairs = [(src, (src + shift) % gy_count) for src in range(gy_count)]
            part = lax.ppermute(part, "gy", perm=pairs)
        origin = lax.rem(me + gy_count - shift, gy_count)
        rows = lax.dynamic_slice_in_dim(inverse, origin * shard_bins, shard_bins, 1)
        term = jnp.einsum("opck,pkl->ocl", part, rows, preferred_element_type=jnp.float32)
        lagged = term if lagged is None else lagged + term
    lagged = lagged * norm_scale
    return lagged.astype(jnp.bfloat16)


def solution(mesh):
    return jax.shard_map(
        local,
        mesh=mesh,
        in_specs=(P("gx", "gy", None), P(), P()),
        out_specs=P("gy", "gx", None),
        check_vma=False,
    )
```

```python
import functools
import math

import jax
import jax.numpy as jnp
from jax import lax
from jax.experimental import pallas as pl
from jax.experimental.pallas import tpu as pltpu
from jax.sharding import PartitionSpec as P

SAMPLES = 8192
LAGS = 512


def inverse_table(kept_bins):
    fine_count = 32
    coarse_count = LAGS // fine_count

    def angles(index):
        return jnp.mod(kept_bins[:, None] * index[None, :], SAMPLES).astype(jnp.float32) * (
            2.0 * math.pi / SAMPLES
        )

    fine = angles(jnp.arange(fine_count, dtype=jnp.int32))[:, None, :]
    coarse = angles(fine_count * jnp.arange(coarse_count, dtype=jnp.int32) - LAGS // 2)[:, :, None]
    cos_f, sin_f, cos_c, sin_c = jnp.cos(fine), jnp.sin(fine), jnp.cos(coarse), jnp.sin(coarse)
    cos_t = (cos_f * cos_c - sin_f * sin_c).reshape(kept_bins.shape[0], LAGS)
    sin_t = (sin_f * cos_c + cos_f * sin_c).reshape(kept_bins.shape[0], LAGS)
    return jnp.stack([cos_t, -sin_t], axis=0).astype(jnp.bfloat16)


def whiten(spectra):
    mean_power = jnp.mean(spectra * spectra, axis=-1, keepdims=True)
    return (spectra * lax.rsqrt(mean_power + 1e-06)).astype(jnp.bfloat16)


def cross_kernel(offsets_ref, base_ref, white_ref, out_ref, *, group, own_count, half):
    step = pl.program_id(0)
    base = base_ref[0]
    own = [white_ref[base + c].astype(jnp.float32) for c in range(own_count)]

    def one_offset(i, carry):
        shift = offsets_ref[step * group + i]
        for c in range(own_count):
            a = own[c]
            b = white_ref[base + c + shift].astype(jnp.float32)
            ar, ai, br, bi = a[:half], a[half:], b[:half], b[half:]
            out_ref[i, 0, pl.ds(c, 1), :] = jnp.sum(ar * br + ai * bi, axis=0, keepdims=True)
            out_ref[i, 1, pl.ds(c, 1), :] = jnp.sum(ai * br - ar * bi, axis=0, keepdims=True)
        return carry

    lax.fori_loop(0, group, one_offset, 0)


def cross_spectra(white_all, pair_offsets, base, own_count):
    rows, bins = white_all.shape[1], white_all.shape[2]
    band_span = pair_offsets.shape[0]
    group = math.gcd(band_span, 8)
    kernel = functools.partial(cross_kernel, group=group, own_count=own_count, half=rows // 2)
    return pl.pallas_call(
        kernel,
        grid_spec=pltpu.PrefetchScalarGridSpec(
            num_scalar_prefetch=2,
            grid=(band_span // group,),
            in_specs=[pl.BlockSpec(white_all.shape, lambda g, offs, b: (0, 0, 0))],
            out_specs=pl.BlockSpec((group, 2, own_count, bins), lambda g, offs, b: (g, 0, 0, 0)),
        ),
        out_shape=jax.ShapeDtypeStruct((band_span, 2, own_count, bins), jnp.float32),
        compiler_params=pltpu.CompilerParams(vmem_limit_bytes=48 * 1024 * 1024),
        cost_estimate=pl.CostEstimate(
            flops=8 * band_span * own_count * rows * bins,
            transcendentals=0,
            bytes_accessed=white_all.size * 4 + band_span * 2 * own_count * bins * 4,
        ),
    )(pair_offsets, base, white_all)


def small_table(kept_bins, rows):
    fine_count = 1 << ((rows.bit_length() - 1) // 2)
    coarse_count = rows // fine_count

    def angles(step, count):
        index = step * jnp.arange(count, dtype=jnp.int32)
        return jnp.mod(index[:, None] * kept_bins[None, :], SAMPLES).astype(jnp.float32) * (
            2.0 * math.pi / SAMPLES
        )

    fine = angles(1, fine_count)[None, :, :]
    coarse = angles(fine_count, coarse_count)[:, None, :]
    cos_f, sin_f, cos_c, sin_c = jnp.cos(fine), jnp.sin(fine), jnp.cos(coarse), jnp.sin(coarse)
    cos_t = cos_f * cos_c - sin_f * sin_c
    sin_t = sin_f * cos_c + cos_f * sin_c
    table = jnp.concatenate([cos_t, -sin_t], axis=-1)
    return table.reshape(rows, 2 * kept_bins.shape[0]).astype(jnp.bfloat16)


def forward_spectra(record_rows, kept_bins):
    row_count, samples = record_rows.shape
    bin_count = kept_bins.shape[0]
    block_count = 4
    block_len = samples // block_count
    prod = jnp.dot(
        record_rows.reshape(row_count * block_count, block_len),
        small_table(kept_bins, block_len),
        preferred_element_type=jnp.float32,
    ).reshape(row_count, block_count, 2, bin_count)
    turns = jnp.mod(
        jnp.arange(block_count, dtype=jnp.int32)[:, None] * jnp.mod(kept_bins, block_count)[None, :],
        block_count,
    ).astype(jnp.float32) * (2.0 * math.pi / block_count)
    tw_re = jnp.round(jnp.cos(turns))[None]
    tw_im = jnp.round(-jnp.sin(turns))[None]
    p_re, p_im = prod[:, :, 0], prod[:, :, 1]
    real_part = jnp.sum(tw_re * p_re - tw_im * p_im, axis=1)
    imag_part = jnp.sum(tw_re * p_im + tw_im * p_re, axis=1)
    return jnp.concatenate([real_part, imag_part], axis=-1)


def local(records, kept_bins, pair_offsets):
    ch_dev, win_dev, samples = records.shape
    bin_count = kept_bins.shape[0]
    band_span = pair_offsets.shape[0]
    spectra = forward_spectra(records.reshape(ch_dev * win_dev, samples), kept_bins)
    white = whiten(spectra).reshape(ch_dev, win_dev, 2, bin_count)
    gy_count = lax.axis_size("gy")
    shard_bins = bin_count // gy_count
    me = lax.axis_index("gy")
    slots = []
    for shift in range(gy_count):
        dest = lax.rem(me + shift, gy_count)
        piece = lax.dynamic_slice_in_dim(white, dest * shard_bins, shard_bins, 3)
        if shift:
            piece = lax.ppermute(piece, "gy", perm=[(src, (src + shift) % gy_count) for src in range(gy_count)])
        slots.append(piece)
    freq_white = jnp.concatenate(slots, axis=1)
    windows = freq_white.shape[1]
    rows_white = jnp.transpose(freq_white, (0, 2, 1, 3)).reshape(ch_dev, 2 * windows, shard_bins)
    gx_count = lax.axis_size("gx")
    needed = -(-band_span // ch_dev)
    blocks = [rows_white]
    for shift in range(1, min(needed, gx_count - 1) + 1):
        pairs = [(src, src - shift) for src in range(shift, gx_count)]
        blocks.append(lax.ppermute(rows_white, "gx", perm=pairs))
    missing = needed + 1 - len(blocks)
    if missing > 0:
        blocks.append(jnp.zeros((missing * ch_dev,) + rows_white.shape[1:], rows_white.dtype))
    padded = jnp.concatenate(blocks, axis=0).astype(jnp.float32)
    base = jnp.zeros((1,), jnp.int32)
    gy_count = lax.axis_size("gy")
    off_dev = band_span // gy_count
    me = lax.axis_index("gy")
    offsets = pair_offsets.astype(jnp.int32)
    inverse, padded = lax.optimization_barrier((inverse_table(kept_bins), padded))
    norm_scale = 0.5 / math.sqrt(windows * bin_count)
    lagged = None
    for shift in list(range(1, gy_count)) + [0]:
        dest = lax.rem(me + shift, gy_count)
        part = cross_spectra(
            padded, lax.dynamic_slice_in_dim(offsets, dest * off_dev, off_dev), base, ch_dev
        ).astype(jnp.bfloat16)
        if shift:
            pairs = [(src, (src + shift) % gy_count) for src in range(gy_count)]
            part = lax.ppermute(part, "gy", perm=pairs)
        origin = lax.rem(me + gy_count - shift, gy_count)
        rows = lax.dynamic_slice_in_dim(inverse, origin * shard_bins, shard_bins, 1)
        term = jnp.einsum("opck,pkl->ocl", part, rows, preferred_element_type=jnp.float32)
        lagged = term if lagged is None else lagged + term
    lagged = lagged * norm_scale
    return lagged.astype(jnp.bfloat16)


def solution(mesh):
    return jax.shard_map(
        local,
        mesh=mesh,
        in_specs=(P("gx", "gy", None), P(), P()),
        out_specs=P("gy", "gx", None),
        check_vma=False,
    )
```

```python
import functools
import math

import jax
import jax.numpy as jnp
from jax import lax
from jax.experimental import pallas as pl
from jax.experimental.pallas import tpu as pltpu
from jax.sharding import PartitionSpec as P

SAMPLES = 8192
LAGS = 512


def inverse_table(kept_bins):
    fine_count = 32
    coarse_count = LAGS // fine_count

    def angles(index):
        return jnp.mod(kept_bins[:, None] * index[None, :], SAMPLES).astype(jnp.float32) * (
            2.0 * math.pi / SAMPLES
        )

    fine = angles(jnp.arange(fine_count, dtype=jnp.int32))[:, None, :]
    coarse = angles(fine_count * jnp.arange(coarse_count, dtype=jnp.int32) - LAGS // 2)[:, :, None]
    cos_f, sin_f, cos_c, sin_c = jnp.cos(fine), jnp.sin(fine), jnp.cos(coarse), jnp.sin(coarse)
    cos_t = (cos_f * cos_c - sin_f * sin_c).reshape(kept_bins.shape[0], LAGS)
    sin_t = (sin_f * cos_c + cos_f * sin_c).reshape(kept_bins.shape[0], LAGS)
    return jnp.stack([cos_t, -sin_t], axis=0).astype(jnp.bfloat16)


def whiten(spectra):
    mean_power = jnp.mean(spectra * spectra, axis=-1, keepdims=True)
    return (spectra * lax.rsqrt(mean_power + 1e-06)).astype(jnp.bfloat16)


def cross_kernel(offsets_ref, base_ref, white_ref, out_ref, *, group, own_count, half):
    step = pl.program_id(0)
    base = base_ref[0]
    own = [white_ref[base + c].astype(jnp.float32) for c in range(own_count)]

    def one_offset(i, carry):
        shift = offsets_ref[step * group + i]
        for c in range(own_count):
            a = own[c]
            b = white_ref[base + c + shift].astype(jnp.float32)
            ar, ai, br, bi = a[:half], a[half:], b[:half], b[half:]
            out_ref[i, 0, pl.ds(c, 1), :] = jnp.sum(ar * br + ai * bi, axis=0, keepdims=True)
            out_ref[i, 1, pl.ds(c, 1), :] = jnp.sum(ai * br - ar * bi, axis=0, keepdims=True)
        return carry

    lax.fori_loop(0, group, one_offset, 0)


def cross_spectra(white_all, pair_offsets, base, own_count):
    rows, bins = white_all.shape[1], white_all.shape[2]
    band_span = pair_offsets.shape[0]
    group = math.gcd(band_span, 32)
    kernel = functools.partial(cross_kernel, group=group, own_count=own_count, half=rows // 2)
    return pl.pallas_call(
        kernel,
        grid_spec=pltpu.PrefetchScalarGridSpec(
            num_scalar_prefetch=2,
            grid=(band_span // group,),
            in_specs=[pl.BlockSpec(white_all.shape, lambda g, offs, b: (0, 0, 0))],
            out_specs=pl.BlockSpec((group, 2, own_count, bins), lambda g, offs, b: (g, 0, 0, 0)),
        ),
        out_shape=jax.ShapeDtypeStruct((band_span, 2, own_count, bins), jnp.float32),
        compiler_params=pltpu.CompilerParams(vmem_limit_bytes=48 * 1024 * 1024),
        cost_estimate=pl.CostEstimate(
            flops=8 * band_span * own_count * rows * bins,
            transcendentals=0,
            bytes_accessed=white_all.size * 4 + band_span * 2 * own_count * bins * 4,
        ),
    )(pair_offsets, base, white_all)


def small_table(kept_bins, rows):
    fine_count = 1 << ((rows.bit_length() - 1) // 2)
    coarse_count = rows // fine_count

    def angles(step, count):
        index = step * jnp.arange(count, dtype=jnp.int32)
        return jnp.mod(index[:, None] * kept_bins[None, :], SAMPLES).astype(jnp.float32) * (
            2.0 * math.pi / SAMPLES
        )

    fine = angles(1, fine_count)[None, :, :]
    coarse = angles(fine_count, coarse_count)[:, None, :]
    cos_f, sin_f, cos_c, sin_c = jnp.cos(fine), jnp.sin(fine), jnp.cos(coarse), jnp.sin(coarse)
    cos_t = cos_f * cos_c - sin_f * sin_c
    sin_t = sin_f * cos_c + cos_f * sin_c
    table = jnp.concatenate([cos_t, -sin_t], axis=-1)
    return table.reshape(rows, 2 * kept_bins.shape[0]).astype(jnp.bfloat16)


def forward_spectra(record_rows, kept_bins):
    row_count, samples = record_rows.shape
    bin_count = kept_bins.shape[0]
    block_count = 4
    block_len = samples // block_count
    prod = jnp.dot(
        record_rows.reshape(row_count * block_count, block_len),
        small_table(kept_bins, block_len),
        preferred_element_type=jnp.float32,
    ).reshape(row_count, block_count, 2, bin_count)
    turns = jnp.mod(
        jnp.arange(block_count, dtype=jnp.int32)[:, None] * jnp.mod(kept_bins, block_count)[None, :],
        block_count,
    ).astype(jnp.float32) * (2.0 * math.pi / block_count)
    tw_re = jnp.round(jnp.cos(turns))[None]
    tw_im = jnp.round(-jnp.sin(turns))[None]
    p_re, p_im = prod[:, :, 0], prod[:, :, 1]
    real_part = jnp.sum(tw_re * p_re - tw_im * p_im, axis=1)
    imag_part = jnp.sum(tw_re * p_im + tw_im * p_re, axis=1)
    return jnp.concatenate([real_part, imag_part], axis=-1)


def local(records, kept_bins, pair_offsets):
    ch_dev, win_dev, samples = records.shape
    bin_count = kept_bins.shape[0]
    band_span = pair_offsets.shape[0]
    spectra = forward_spectra(records.reshape(ch_dev * win_dev, samples), kept_bins)
    white = whiten(spectra).reshape(ch_dev, win_dev, 2, bin_count)
    gy_count = lax.axis_size("gy")
    shard_bins = bin_count // gy_count
    me = lax.axis_index("gy")
    slots = []
    for shift in range(gy_count):
        dest = lax.rem(me + shift, gy_count)
        piece = lax.dynamic_slice_in_dim(white, dest * shard_bins, shard_bins, 3)
        if shift:
            piece = lax.ppermute(piece, "gy", perm=[(src, (src + shift) % gy_count) for src in range(gy_count)])
        slots.append(piece)
    freq_white = jnp.concatenate(slots, axis=1)
    windows = freq_white.shape[1]
    rows_white = jnp.transpose(freq_white, (0, 2, 1, 3)).reshape(ch_dev, 2 * windows, shard_bins)
    gx_count = lax.axis_size("gx")
    needed = -(-band_span // ch_dev)
    blocks = [rows_white]
    for shift in range(1, min(needed, gx_count - 1) + 1):
        pairs = [(src, src - shift) for src in range(shift, gx_count)]
        blocks.append(lax.ppermute(rows_white, "gx", perm=pairs))
    missing = needed + 1 - len(blocks)
    if missing > 0:
        blocks.append(jnp.zeros((missing * ch_dev,) + rows_white.shape[1:], rows_white.dtype))
    padded = jnp.concatenate(blocks, axis=0).astype(jnp.float32)
    base = jnp.zeros((1,), jnp.int32)
    gy_count = lax.axis_size("gy")
    off_dev = band_span // gy_count
    me = lax.axis_index("gy")
    offsets = pair_offsets.astype(jnp.int32)
    inverse = inverse_table(kept_bins)
    norm_scale = 0.5 / math.sqrt(windows * bin_count)
    lagged = None
    for shift in list(range(1, gy_count)) + [0]:
        dest = lax.rem(me + shift, gy_count)
        part = cross_spectra(
            padded, lax.dynamic_slice_in_dim(offsets, dest * off_dev, off_dev), base, ch_dev
        ).astype(jnp.bfloat16)
        if shift:
            pairs = [(src, (src + shift) % gy_count) for src in range(gy_count)]
            part = lax.ppermute(part, "gy", perm=pairs)
        origin = lax.rem(me + gy_count - shift, gy_count)
        rows = lax.dynamic_slice_in_dim(inverse, origin * shard_bins, shard_bins, 1)
        term = jnp.einsum("opck,pkl->ocl", part, rows, preferred_element_type=jnp.float32)
        lagged = term if lagged is None else lagged + term
    lagged = lagged * norm_scale
    return lagged.astype(jnp.bfloat16)


def solution(mesh):
    return jax.shard_map(
        local,
        mesh=mesh,
        in_specs=(P("gx", "gy", None), P(), P()),
        out_specs=P("gy", "gx", None),
        check_vma=False,
    )
```

```python
import functools
import math

import jax
import jax.numpy as jnp
from jax import lax
from jax.experimental import pallas as pl
from jax.experimental.pallas import tpu as pltpu
from jax.sharding import PartitionSpec as P

SAMPLES = 8192
LAGS = 512


def inverse_table(kept_bins):
    fine_count = 32
    coarse_count = LAGS // fine_count

    def angles(index):
        return jnp.mod(kept_bins[:, None] * index[None, :], SAMPLES).astype(jnp.float32) * (
            2.0 * math.pi / SAMPLES
        )

    fine = angles(jnp.arange(fine_count, dtype=jnp.int32))[:, None, :]
    coarse = angles(fine_count * jnp.arange(coarse_count, dtype=jnp.int32) - LAGS // 2)[:, :, None]
    cos_f, sin_f, cos_c, sin_c = jnp.cos(fine), jnp.sin(fine), jnp.cos(coarse), jnp.sin(coarse)
    cos_t = (cos_f * cos_c - sin_f * sin_c).reshape(kept_bins.shape[0], LAGS)
    sin_t = (sin_f * cos_c + cos_f * sin_c).reshape(kept_bins.shape[0], LAGS)
    return jnp.stack([cos_t, -sin_t], axis=0).astype(jnp.bfloat16)


def whiten(spectra):
    mean_power = jnp.mean(spectra * spectra, axis=-1, keepdims=True)
    return (spectra * lax.rsqrt(mean_power + 1e-06)).astype(jnp.bfloat16)


def cross_kernel(offsets_ref, base_ref, white_ref, out_ref, *, group, own_count, half):
    step = pl.program_id(0)
    base = base_ref[0]
    own = [white_ref[base + c].astype(jnp.float32) for c in range(own_count)]

    def one_offset(i, carry):
        shift = offsets_ref[step * group + i]
        for c in range(own_count):
            a = own[c]
            b = white_ref[base + c + shift].astype(jnp.float32)
            ar, ai, br, bi = a[:half], a[half:], b[:half], b[half:]
            out_ref[i, 0, pl.ds(c, 1), :] = jnp.sum(ar * br + ai * bi, axis=0, keepdims=True)
            out_ref[i, 1, pl.ds(c, 1), :] = jnp.sum(ai * br - ar * bi, axis=0, keepdims=True)
        return carry

    lax.fori_loop(0, group, one_offset, 0)


def cross_spectra(white_all, pair_offsets, base, own_count):
    rows, bins = white_all.shape[1], white_all.shape[2]
    band_span = pair_offsets.shape[0]
    group = math.gcd(band_span, 8)
    kernel = functools.partial(cross_kernel, group=group, own_count=own_count, half=rows // 2)
    return pl.pallas_call(
        kernel,
        grid_spec=pltpu.PrefetchScalarGridSpec(
            num_scalar_prefetch=2,
            grid=(band_span // group,),
            in_specs=[pl.BlockSpec(white_all.shape, lambda g, offs, b: (0, 0, 0))],
            out_specs=pl.BlockSpec((group, 2, own_count, bins), lambda g, offs, b: (g, 0, 0, 0)),
        ),
        out_shape=jax.ShapeDtypeStruct((band_span, 2, own_count, bins), jnp.float32),
        compiler_params=pltpu.CompilerParams(vmem_limit_bytes=48 * 1024 * 1024),
        cost_estimate=pl.CostEstimate(
            flops=8 * band_span * own_count * rows * bins,
            transcendentals=0,
            bytes_accessed=white_all.size * 4 + band_span * 2 * own_count * bins * 4,
        ),
    )(pair_offsets, base, white_all)


def small_table(kept_bins, rows):
    fine_count = 1 << ((rows.bit_length() - 1) // 2)
    coarse_count = rows // fine_count

    def angles(step, count):
        index = step * jnp.arange(count, dtype=jnp.int32)
        return jnp.mod(index[:, None] * kept_bins[None, :], SAMPLES).astype(jnp.float32) * (
            2.0 * math.pi / SAMPLES
        )

    fine = angles(1, fine_count)[None, :, :]
    coarse = angles(fine_count, coarse_count)[:, None, :]
    cos_f, sin_f, cos_c, sin_c = jnp.cos(fine), jnp.sin(fine), jnp.cos(coarse), jnp.sin(coarse)
    cos_t = cos_f * cos_c - sin_f * sin_c
    sin_t = sin_f * cos_c + cos_f * sin_c
    table = jnp.concatenate([cos_t, -sin_t], axis=-1)
    return table.reshape(rows, 2 * kept_bins.shape[0]).astype(jnp.bfloat16)


def forward_spectra(record_rows, kept_bins):
    row_count, samples = record_rows.shape
    bin_count = kept_bins.shape[0]
    block_count = 4
    block_len = samples // block_count
    prod = jnp.dot(
        record_rows.reshape(row_count * block_count, block_len),
        small_table(kept_bins, block_len),
        preferred_element_type=jnp.float32,
    ).reshape(row_count, block_count, 2, bin_count)
    turns = jnp.mod(
        jnp.arange(block_count, dtype=jnp.int32)[:, None] * jnp.mod(kept_bins, block_count)[None, :],
        block_count,
    ).astype(jnp.float32) * (2.0 * math.pi / block_count)
    tw_re = jnp.round(jnp.cos(turns))[None]
    tw_im = jnp.round(-jnp.sin(turns))[None]
    p_re, p_im = prod[:, :, 0], prod[:, :, 1]
    real_part = jnp.sum(tw_re * p_re - tw_im * p_im, axis=1)
    imag_part = jnp.sum(tw_re * p_im + tw_im * p_re, axis=1)
    return jnp.concatenate([real_part, imag_part], axis=-1)


def local(records, kept_bins, pair_offsets):
    ch_dev, win_dev, samples = records.shape
    bin_count = kept_bins.shape[0]
    band_span = pair_offsets.shape[0]
    spectra = forward_spectra(records.reshape(ch_dev * win_dev, samples), kept_bins)
    white = whiten(spectra).reshape(ch_dev, win_dev, 2, bin_count)
    gy_count = lax.axis_size("gy")
    shard_bins = bin_count // gy_count
    me = lax.axis_index("gy")
    slots = []
    for shift in range(gy_count):
        dest = lax.rem(me + shift, gy_count)
        piece = lax.dynamic_slice_in_dim(white, dest * shard_bins, shard_bins, 3)
        if shift:
            piece = lax.ppermute(piece, "gy", perm=[(src, (src + shift) % gy_count) for src in range(gy_count)])
        slots.append(piece)
    freq_white = jnp.concatenate(slots, axis=1)
    windows = freq_white.shape[1]
    rows_white = jnp.transpose(freq_white, (0, 2, 1, 3)).reshape(ch_dev, 2 * windows, shard_bins)
    gx_count = lax.axis_size("gx")
    needed = -(-band_span // ch_dev)
    blocks = [rows_white]
    for shift in range(1, min(needed, gx_count - 1) + 1):
        pairs = [(src, src - shift) for src in range(shift, gx_count)]
        blocks.append(lax.ppermute(rows_white, "gx", perm=pairs))
    missing = needed + 1 - len(blocks)
    if missing > 0:
        blocks.append(jnp.zeros((missing * ch_dev,) + rows_white.shape[1:], rows_white.dtype))
    padded = jnp.concatenate(blocks, axis=0).astype(jnp.float32)
    base = jnp.zeros((1,), jnp.int32)
    gy_count = lax.axis_size("gy")
    off_dev = band_span // gy_count
    me = lax.axis_index("gy")
    offsets = pair_offsets.astype(jnp.int32)
    inverse = inverse_table(kept_bins)
    norm_scale = 0.5 / math.sqrt(windows * bin_count)
    lagged = None
    far_shift = gy_count // 2
    for shift in [far_shift] + [s for s in range(1, gy_count) if s != far_shift] + [0]:
        dest = lax.rem(me + shift, gy_count)
        part = cross_spectra(
            padded, lax.dynamic_slice_in_dim(offsets, dest * off_dev, off_dev), base, ch_dev
        ).astype(jnp.bfloat16)
        if shift:
            pairs = [(src, (src + shift) % gy_count) for src in range(gy_count)]
            part = lax.ppermute(part, "gy", perm=pairs)
        origin = lax.rem(me + gy_count - shift, gy_count)
        rows = lax.dynamic_slice_in_dim(inverse, origin * shard_bins, shard_bins, 1)
        term = jnp.einsum("opck,pkl->ocl", part, rows, preferred_element_type=jnp.float32)
        lagged = term if lagged is None else lagged + term
    lagged = lagged * norm_scale
    return lagged.astype(jnp.bfloat16)


def solution(mesh):
    return jax.shard_map(
        local,
        mesh=mesh,
        in_specs=(P("gx", "gy", None), P(), P()),
        out_specs=P("gy", "gx", None),
        check_vma=False,
    )
```

```python
import functools
import math

import jax
import jax.numpy as jnp
from jax import lax
from jax.experimental import pallas as pl
from jax.experimental.pallas import tpu as pltpu
from jax.sharding import PartitionSpec as P

SAMPLES = 8192
LAGS = 512


def inverse_table(kept_bins):
    fine_count = 32
    coarse_count = LAGS // fine_count

    def angles(index):
        return jnp.mod(kept_bins[:, None] * index[None, :], SAMPLES).astype(jnp.float32) * (
            2.0 * math.pi / SAMPLES
        )

    fine = angles(jnp.arange(fine_count, dtype=jnp.int32))[:, None, :]
    coarse = angles(fine_count * jnp.arange(coarse_count, dtype=jnp.int32) - LAGS // 2)[:, :, None]
    cos_f, sin_f, cos_c, sin_c = jnp.cos(fine), jnp.sin(fine), jnp.cos(coarse), jnp.sin(coarse)
    cos_t = (cos_f * cos_c - sin_f * sin_c).reshape(kept_bins.shape[0], LAGS)
    sin_t = (sin_f * cos_c + cos_f * sin_c).reshape(kept_bins.shape[0], LAGS)
    return jnp.stack([cos_t, -sin_t], axis=0).astype(jnp.bfloat16)


def whiten(spectra):
    mean_power = jnp.mean(spectra * spectra, axis=-1, keepdims=True)
    return (spectra * lax.rsqrt(mean_power + 1e-06)).astype(jnp.bfloat16)


def cross_kernel(offsets_ref, base_ref, white_ref, out_ref, *, group, own_count, half):
    step = pl.program_id(0)
    base = base_ref[0]

    def one_offset(i, carry):
        shift = offsets_ref[step * group + i]
        for c in range(own_count):
            a = white_ref[base + c].astype(jnp.float32)
            b = white_ref[base + c + shift].astype(jnp.float32)
            ar, ai, br, bi = a[:half], a[half:], b[:half], b[half:]
            out_ref[i, 0, pl.ds(c, 1), :] = jnp.sum(ar * br + ai * bi, axis=0, keepdims=True)
            out_ref[i, 1, pl.ds(c, 1), :] = jnp.sum(ai * br - ar * bi, axis=0, keepdims=True)
        return carry

    lax.fori_loop(0, group, one_offset, 0)


def cross_spectra(white_all, pair_offsets, base, own_count):
    rows, bins = white_all.shape[1], white_all.shape[2]
    band_span = pair_offsets.shape[0]
    group = math.gcd(band_span, 8)
    kernel = functools.partial(cross_kernel, group=group, own_count=own_count, half=rows // 2)
    return pl.pallas_call(
        kernel,
        grid_spec=pltpu.PrefetchScalarGridSpec(
            num_scalar_prefetch=2,
            grid=(band_span // group,),
            in_specs=[pl.BlockSpec(white_all.shape, lambda g, offs, b: (0, 0, 0))],
            out_specs=pl.BlockSpec((group, 2, own_count, bins), lambda g, offs, b: (g, 0, 0, 0)),
        ),
        out_shape=jax.ShapeDtypeStruct((band_span, 2, own_count, bins), jnp.float32),
        compiler_params=pltpu.CompilerParams(vmem_limit_bytes=48 * 1024 * 1024),
        cost_estimate=pl.CostEstimate(
            flops=8 * band_span * own_count * rows * bins,
            transcendentals=0,
            bytes_accessed=white_all.size * 4 + band_span * 2 * own_count * bins * 4,
        ),
    )(pair_offsets, base, white_all)


def small_table(kept_bins, rows):
    fine_count = 1 << ((rows.bit_length() - 1) // 2)
    coarse_count = rows // fine_count

    def angles(step, count):
        index = step * jnp.arange(count, dtype=jnp.int32)
        return jnp.mod(index[:, None] * kept_bins[None, :], SAMPLES).astype(jnp.float32) * (
            2.0 * math.pi / SAMPLES
        )

    fine = angles(1, fine_count)[None, :, :]
    coarse = angles(fine_count, coarse_count)[:, None, :]
    cos_f, sin_f, cos_c, sin_c = jnp.cos(fine), jnp.sin(fine), jnp.cos(coarse), jnp.sin(coarse)
    cos_t = cos_f * cos_c - sin_f * sin_c
    sin_t = sin_f * cos_c + cos_f * sin_c
    table = jnp.concatenate([cos_t, -sin_t], axis=-1)
    return table.reshape(rows, 2 * kept_bins.shape[0]).astype(jnp.bfloat16)


def forward_spectra(record_rows, kept_bins):
    row_count, samples = record_rows.shape
    bin_count = kept_bins.shape[0]
    block_count = 4
    block_len = samples // block_count
    prod = jnp.dot(
        record_rows.reshape(row_count * block_count, block_len),
        small_table(kept_bins, block_len),
        preferred_element_type=jnp.float32,
    ).reshape(row_count, block_count, 2, bin_count)
    turns = jnp.mod(
        jnp.arange(block_count, dtype=jnp.int32)[:, None] * jnp.mod(kept_bins, block_count)[None, :],
        block_count,
    ).astype(jnp.float32) * (2.0 * math.pi / block_count)
    tw_re = jnp.round(jnp.cos(turns))[None]
    tw_im = jnp.round(-jnp.sin(turns))[None]
    p_re, p_im = prod[:, :, 0], prod[:, :, 1]
    real_part = jnp.sum(tw_re * p_re - tw_im * p_im, axis=1)
    imag_part = jnp.sum(tw_re * p_im + tw_im * p_re, axis=1)
    return jnp.concatenate([real_part, imag_part], axis=-1)


def local(records, kept_bins, pair_offsets):
    ch_dev, win_dev, samples = records.shape
    bin_count = kept_bins.shape[0]
    band_span = pair_offsets.shape[0]
    spectra = forward_spectra(records.reshape(ch_dev * win_dev, samples), kept_bins)
    white = whiten(spectra).reshape(ch_dev, win_dev, 2, bin_count)
    gy_count = lax.axis_size("gy")
    shard_bins = bin_count // gy_count
    me = lax.axis_index("gy")
    slots = []
    for shift in range(gy_count):
        dest = lax.rem(me + shift, gy_count)
        piece = lax.dynamic_slice_in_dim(white, dest * shard_bins, shard_bins, 3)
        if shift:
            piece = lax.ppermute(piece, "gy", perm=[(src, (src + shift) % gy_count) for src in range(gy_count)])
        slots.append(piece)
    freq_white = jnp.concatenate(slots, axis=1)
    windows = freq_white.shape[1]
    rows_white = jnp.transpose(freq_white, (0, 2, 1, 3)).reshape(ch_dev, 2 * windows, shard_bins)
    gx_count = lax.axis_size("gx")
    needed = -(-band_span // ch_dev)
    blocks = [rows_white]
    for shift in range(1, min(needed, gx_count - 1) + 1):
        pairs = [(src, src - shift) for src in range(shift, gx_count)]
        blocks.append(lax.ppermute(rows_white, "gx", perm=pairs))
    missing = needed + 1 - len(blocks)
    if missing > 0:
        blocks.append(jnp.zeros((missing * ch_dev,) + rows_white.shape[1:], rows_white.dtype))
    padded = jnp.concatenate(blocks, axis=0).astype(jnp.float32)
    base = jnp.zeros((1,), jnp.int32)
    gy_count = lax.axis_size("gy")
    off_dev = band_span // gy_count
    me = lax.axis_index("gy")
    offsets = pair_offsets.astype(jnp.int32)
    inverse = inverse_table(kept_bins)
    norm_scale = 0.5 / math.sqrt(windows * bin_count)
    lagged = None
    for shift in list(range(1, gy_count)) + [0]:
        dest = lax.rem(me + shift, gy_count)
        part = cross_spectra(
            padded, lax.dynamic_slice_in_dim(offsets, dest * off_dev, off_dev), base, ch_dev
        ).astype(jnp.bfloat16)
        if shift:
            pairs = [(src, (src + shift) % gy_count) for src in range(gy_count)]
            part = lax.ppermute(part, "gy", perm=pairs)
        origin = lax.rem(me + gy_count - shift, gy_count)
        rows = lax.dynamic_slice_in_dim(inverse, origin * shard_bins, shard_bins, 1)
        term = jnp.einsum("opck,pkl->ocl", part, rows, preferred_element_type=jnp.float32)
        lagged = term if lagged is None else lagged + term
    lagged = lagged * norm_scale
    return lagged.astype(jnp.bfloat16)


def solution(mesh):
    return jax.shard_map(
        local,
        mesh=mesh,
        in_specs=(P("gx", "gy", None), P(), P()),
        out_specs=P("gy", "gx", None),
        check_vma=False,
    )
```

```python
import functools
import math

import jax
import jax.numpy as jnp
from jax import lax
from jax.experimental import pallas as pl
from jax.experimental.pallas import tpu as pltpu
from jax.sharding import PartitionSpec as P

SAMPLES = 8192
LAGS = 512


def inverse_table(kept_bins):
    fine_count = 32
    coarse_count = LAGS // fine_count

    def angles(index):
        return jnp.mod(kept_bins[:, None] * index[None, :], SAMPLES).astype(jnp.float32) * (
            2.0 * math.pi / SAMPLES
        )

    fine = angles(jnp.arange(fine_count, dtype=jnp.int32))[:, None, :]
    coarse = angles(fine_count * jnp.arange(coarse_count, dtype=jnp.int32) - LAGS // 2)[:, :, None]
    cos_f, sin_f, cos_c, sin_c = jnp.cos(fine), jnp.sin(fine), jnp.cos(coarse), jnp.sin(coarse)
    cos_t = (cos_f * cos_c - sin_f * sin_c).reshape(kept_bins.shape[0], LAGS)
    sin_t = (sin_f * cos_c + cos_f * sin_c).reshape(kept_bins.shape[0], LAGS)
    return jnp.stack([cos_t, -sin_t], axis=0).astype(jnp.bfloat16)


def whiten(spectra):
    mean_power = jnp.mean(spectra * spectra, axis=-1, keepdims=True)
    return (spectra * lax.rsqrt(mean_power + 1e-06)).astype(jnp.bfloat16)


def cross_kernel(offsets_ref, base_ref, white_ref, out_ref, *, group, own_count, half):
    step = pl.program_id(0)
    base = base_ref[0]

    def one_offset(i, carry):
        shift = offsets_ref[step * group + i]
        real_rows, imag_rows = [], []
        for c in range(own_count):
            a = white_ref[base + c].astype(jnp.float32)
            b = white_ref[base + c + shift].astype(jnp.float32)
            ar, ai, br, bi = a[:half], a[half:], b[:half], b[half:]
            real_rows.append(jnp.sum(ar * br + ai * bi, axis=0, keepdims=True))
            imag_rows.append(jnp.sum(ai * br - ar * bi, axis=0, keepdims=True))
        out_ref[i, 0] = jnp.concatenate(real_rows, axis=0).astype(out_ref.dtype)
        out_ref[i, 1] = jnp.concatenate(imag_rows, axis=0).astype(out_ref.dtype)
        return carry

    lax.fori_loop(0, group, one_offset, 0)


def cross_spectra(white_all, pair_offsets, base, own_count):
    rows, bins = white_all.shape[1], white_all.shape[2]
    band_span = pair_offsets.shape[0]
    group = math.gcd(band_span, 8)
    kernel = functools.partial(cross_kernel, group=group, own_count=own_count, half=rows // 2)
    return pl.pallas_call(
        kernel,
        grid_spec=pltpu.PrefetchScalarGridSpec(
            num_scalar_prefetch=2,
            grid=(band_span // group,),
            in_specs=[pl.BlockSpec(white_all.shape, lambda g, offs, b: (0, 0, 0))],
            out_specs=pl.BlockSpec((group, 2, own_count, bins), lambda g, offs, b: (g, 0, 0, 0)),
        ),
        out_shape=jax.ShapeDtypeStruct((band_span, 2, own_count, bins), jnp.bfloat16),
        compiler_params=pltpu.CompilerParams(vmem_limit_bytes=48 * 1024 * 1024),
        cost_estimate=pl.CostEstimate(
            flops=8 * band_span * own_count * rows * bins,
            transcendentals=0,
            bytes_accessed=white_all.size * 4 + band_span * 2 * own_count * bins * 4,
        ),
    )(pair_offsets, base, white_all)


def small_table(kept_bins, rows):
    fine_count = 1 << ((rows.bit_length() - 1) // 2)
    coarse_count = rows // fine_count

    def angles(step, count):
        index = step * jnp.arange(count, dtype=jnp.int32)
        return jnp.mod(index[:, None] * kept_bins[None, :], SAMPLES).astype(jnp.float32) * (
            2.0 * math.pi / SAMPLES
        )

    fine = angles(1, fine_count)[None, :, :]
    coarse = angles(fine_count, coarse_count)[:, None, :]
    cos_f, sin_f, cos_c, sin_c = jnp.cos(fine), jnp.sin(fine), jnp.cos(coarse), jnp.sin(coarse)
    cos_t = cos_f * cos_c - sin_f * sin_c
    sin_t = sin_f * cos_c + cos_f * sin_c
    table = jnp.concatenate([cos_t, -sin_t], axis=-1)
    return table.reshape(rows, 2 * kept_bins.shape[0]).astype(jnp.bfloat16)


def forward_spectra(record_rows, kept_bins):
    row_count, samples = record_rows.shape
    bin_count = kept_bins.shape[0]
    block_count = 4
    block_len = samples // block_count
    prod = jnp.dot(
        record_rows.reshape(row_count * block_count, block_len),
        small_table(kept_bins, block_len),
        preferred_element_type=jnp.float32,
    ).reshape(row_count, block_count, 2, bin_count)
    turns = jnp.mod(
        jnp.arange(block_count, dtype=jnp.int32)[:, None] * jnp.mod(kept_bins, block_count)[None, :],
        block_count,
    ).astype(jnp.float32) * (2.0 * math.pi / block_count)
    tw_re = jnp.round(jnp.cos(turns))[None]
    tw_im = jnp.round(-jnp.sin(turns))[None]
    p_re, p_im = prod[:, :, 0], prod[:, :, 1]
    real_part = jnp.sum(tw_re * p_re - tw_im * p_im, axis=1)
    imag_part = jnp.sum(tw_re * p_im + tw_im * p_re, axis=1)
    return jnp.concatenate([real_part, imag_part], axis=-1)


def local(records, kept_bins, pair_offsets):
    ch_dev, win_dev, samples = records.shape
    bin_count = kept_bins.shape[0]
    band_span = pair_offsets.shape[0]
    spectra = forward_spectra(records.reshape(ch_dev * win_dev, samples), kept_bins)
    white = whiten(spectra).reshape(ch_dev, win_dev, 2, bin_count)
    gy_count = lax.axis_size("gy")
    shard_bins = bin_count // gy_count
    me = lax.axis_index("gy")
    slots = []
    for shift in range(gy_count):
        dest = lax.rem(me + shift, gy_count)
        piece = lax.dynamic_slice_in_dim(white, dest * shard_bins, shard_bins, 3)
        if shift:
            piece = lax.ppermute(piece, "gy", perm=[(src, (src + shift) % gy_count) for src in range(gy_count)])
        slots.append(piece)
    freq_white = jnp.concatenate(slots, axis=1)
    windows = freq_white.shape[1]
    rows_white = jnp.transpose(freq_white, (0, 2, 1, 3)).reshape(ch_dev, 2 * windows, shard_bins)
    gx_count = lax.axis_size("gx")
    needed = -(-band_span // ch_dev)
    blocks = [rows_white]
    for shift in range(1, min(needed, gx_count - 1) + 1):
        pairs = [(src, src - shift) for src in range(shift, gx_count)]
        blocks.append(lax.ppermute(rows_white, "gx", perm=pairs))
    missing = needed + 1 - len(blocks)
    if missing > 0:
        blocks.append(jnp.zeros((missing * ch_dev,) + rows_white.shape[1:], rows_white.dtype))
    padded = jnp.concatenate(blocks, axis=0).astype(jnp.float32)
    base = jnp.zeros((1,), jnp.int32)
    gy_count = lax.axis_size("gy")
    off_dev = band_span // gy_count
    me = lax.axis_index("gy")
    offsets = pair_offsets.astype(jnp.int32)
    inverse = inverse_table(kept_bins)
    norm_scale = 0.5 / math.sqrt(windows * bin_count)
    lagged = None
    for shift in list(range(1, gy_count)) + [0]:
        dest = lax.rem(me + shift, gy_count)
        part = cross_spectra(
            padded, lax.dynamic_slice_in_dim(offsets, dest * off_dev, off_dev), base, ch_dev
        ).astype(jnp.bfloat16)
        if shift:
            pairs = [(src, (src + shift) % gy_count) for src in range(gy_count)]
            part = lax.ppermute(part, "gy", perm=pairs)
        origin = lax.rem(me + gy_count - shift, gy_count)
        rows = lax.dynamic_slice_in_dim(inverse, origin * shard_bins, shard_bins, 1)
        term = jnp.einsum("opck,pkl->ocl", part, rows, preferred_element_type=jnp.float32)
        lagged = term if lagged is None else lagged + term
    lagged = lagged * norm_scale
    return lagged.astype(jnp.bfloat16)


def solution(mesh):
    return jax.shard_map(
        local,
        mesh=mesh,
        in_specs=(P("gx", "gy", None), P(), P()),
        out_specs=P("gy", "gx", None),
        check_vma=False,
    )
```

```python
import functools
import math

import jax
import jax.numpy as jnp
from jax import lax
from jax.experimental import pallas as pl
from jax.experimental.pallas import tpu as pltpu
from jax.sharding import PartitionSpec as P

SAMPLES = 8192
LAGS = 512


def inverse_table(kept_bins):
    fine_count = 32
    coarse_count = LAGS // fine_count

    def angles(index):
        return jnp.mod(kept_bins[:, None] * index[None, :], SAMPLES).astype(jnp.float32) * (
            2.0 * math.pi / SAMPLES
        )

    fine = angles(jnp.arange(fine_count, dtype=jnp.int32))[:, None, :]
    coarse = angles(fine_count * jnp.arange(coarse_count, dtype=jnp.int32) - LAGS // 2)[:, :, None]
    cos_f, sin_f, cos_c, sin_c = jnp.cos(fine), jnp.sin(fine), jnp.cos(coarse), jnp.sin(coarse)
    cos_t = (cos_f * cos_c - sin_f * sin_c).reshape(kept_bins.shape[0], LAGS)
    sin_t = (sin_f * cos_c + cos_f * sin_c).reshape(kept_bins.shape[0], LAGS)
    return jnp.stack([cos_t, -sin_t], axis=0).astype(jnp.bfloat16)


def whiten(spectra):
    mean_power = jnp.mean(spectra * spectra, axis=-1, keepdims=True)
    return (spectra * lax.rsqrt(mean_power + 1e-06)).astype(jnp.bfloat16)


def cross_kernel(offsets_ref, base_ref, white_ref, out_ref, *, group, own_count, half):
    step = pl.program_id(0)
    base = base_ref[0]

    def one_offset(i, carry):
        shift = offsets_ref[step * group + i]
        for c in range(own_count):
            a = white_ref[base + c].astype(jnp.float32)
            b = white_ref[base + c + shift].astype(jnp.float32)
            ar, ai, br, bi = a[:half], a[half:], b[:half], b[half:]
            out_ref[i, 0, pl.ds(c, 1), :] = jnp.sum(ar * br + ai * bi, axis=0, keepdims=True)
            out_ref[i, 1, pl.ds(c, 1), :] = jnp.sum(ai * br - ar * bi, axis=0, keepdims=True)
        return carry

    lax.fori_loop(0, group, one_offset, 0)


def cross_spectra(white_all, pair_offsets, base, own_count):
    rows, bins = white_all.shape[1], white_all.shape[2]
    band_span = pair_offsets.shape[0]
    group = math.gcd(band_span, 8)
    kernel = functools.partial(cross_kernel, group=group, own_count=own_count, half=rows // 2)
    return pl.pallas_call(
        kernel,
        grid_spec=pltpu.PrefetchScalarGridSpec(
            num_scalar_prefetch=2,
            grid=(band_span // group,),
            in_specs=[pl.BlockSpec(white_all.shape, lambda g, offs, b: (0, 0, 0))],
            out_specs=pl.BlockSpec((group, 2, own_count, bins), lambda g, offs, b: (g, 0, 0, 0)),
        ),
        out_shape=jax.ShapeDtypeStruct((band_span, 2, own_count, bins), jnp.float32),
        compiler_params=pltpu.CompilerParams(vmem_limit_bytes=48 * 1024 * 1024),
        cost_estimate=pl.CostEstimate(
            flops=8 * band_span * own_count * rows * bins,
            transcendentals=0,
            bytes_accessed=white_all.size * 4 + band_span * 2 * own_count * bins * 4,
        ),
    )(pair_offsets, base, white_all)


def small_table(kept_bins, rows):
    fine_count = 1 << ((rows.bit_length() - 1) // 2)
    coarse_count = rows // fine_count

    def angles(step, count):
        index = step * jnp.arange(count, dtype=jnp.int32)
        return jnp.mod(index[:, None] * kept_bins[None, :], SAMPLES).astype(jnp.float32) * (
            2.0 * math.pi / SAMPLES
        )

    fine = angles(1, fine_count)[None, :, :]
    coarse = angles(fine_count, coarse_count)[:, None, :]
    cos_f, sin_f, cos_c, sin_c = jnp.cos(fine), jnp.sin(fine), jnp.cos(coarse), jnp.sin(coarse)
    cos_t = cos_f * cos_c - sin_f * sin_c
    sin_t = sin_f * cos_c + cos_f * sin_c
    table = jnp.concatenate([cos_t, -sin_t], axis=-1)
    return table.reshape(rows, 2 * kept_bins.shape[0]).astype(jnp.bfloat16)


def forward_spectra(record_rows, kept_bins):
    row_count, samples = record_rows.shape
    bin_count = kept_bins.shape[0]
    block_count = 4
    block_len = samples // block_count
    prod = jnp.dot(
        record_rows.reshape(row_count * block_count, block_len),
        small_table(kept_bins, block_len),
        preferred_element_type=jnp.float32,
    ).reshape(row_count, block_count, 2, bin_count)
    turns = jnp.mod(
        jnp.arange(block_count, dtype=jnp.int32)[:, None] * jnp.mod(kept_bins, block_count)[None, :],
        block_count,
    ).astype(jnp.float32) * (2.0 * math.pi / block_count)
    tw_re = jnp.round(jnp.cos(turns))[None]
    tw_im = jnp.round(-jnp.sin(turns))[None]
    p_re, p_im = prod[:, :, 0], prod[:, :, 1]
    real_part = jnp.sum(tw_re * p_re - tw_im * p_im, axis=1)
    imag_part = jnp.sum(tw_re * p_im + tw_im * p_re, axis=1)
    return jnp.concatenate([real_part, imag_part], axis=-1)


def local(records, kept_bins, pair_offsets):
    ch_dev, win_dev, samples = records.shape
    bin_count = kept_bins.shape[0]
    band_span = pair_offsets.shape[0]
    spectra = forward_spectra(records.reshape(ch_dev * win_dev, samples), kept_bins)
    white = whiten(spectra).reshape(ch_dev, win_dev, 2, bin_count)
    gy_count = lax.axis_size("gy")
    shard_bins = bin_count // gy_count
    me = lax.axis_index("gy")
    slots = []
    for shift in range(gy_count):
        dest = lax.rem(me + shift, gy_count)
        piece = lax.dynamic_slice_in_dim(white, dest * shard_bins, shard_bins, 3)
        if shift:
            piece = lax.ppermute(piece, "gy", perm=[(src, (src + shift) % gy_count) for src in range(gy_count)])
        slots.append(piece)
    freq_white = jnp.concatenate(slots, axis=1)
    windows = freq_white.shape[1]
    rows_white = jnp.transpose(freq_white, (0, 2, 1, 3)).reshape(ch_dev, 2 * windows, shard_bins)
    gx_count = lax.axis_size("gx")
    needed = -(-band_span // ch_dev)
    blocks = [rows_white]
    for shift in range(1, min(needed, gx_count - 1) + 1):
        pairs = [(src, src - shift) for src in range(shift, gx_count)]
        blocks.append(lax.ppermute(rows_white, "gx", perm=pairs))
    missing = needed + 1 - len(blocks)
    if missing > 0:
        blocks.append(jnp.zeros((missing * ch_dev,) + rows_white.shape[1:], rows_white.dtype))
    padded = jnp.concatenate(blocks, axis=0).astype(jnp.float32)
    base = jnp.zeros((1,), jnp.int32)
    gy_count = lax.axis_size("gy")
    off_dev = band_span // gy_count
    me = lax.axis_index("gy")
    offsets = pair_offsets.astype(jnp.int32)
    inverse = inverse_table(kept_bins)
    norm_scale = 0.5 / math.sqrt(windows * bin_count)
    lagged = None
    far_shift = gy_count // 2
    for shift in [s for s in range(1, gy_count) if s != far_shift] + [far_shift, 0]:
        dest = lax.rem(me + shift, gy_count)
        part = cross_spectra(
            padded, lax.dynamic_slice_in_dim(offsets, dest * off_dev, off_dev), base, ch_dev
        ).astype(jnp.bfloat16)
        if shift:
            pairs = [(src, (src + shift) % gy_count) for src in range(gy_count)]
            part = lax.ppermute(part, "gy", perm=pairs)
        origin = lax.rem(me + gy_count - shift, gy_count)
        rows = lax.dynamic_slice_in_dim(inverse, origin * shard_bins, shard_bins, 1)
        term = jnp.einsum("opck,pkl->ocl", part, rows, preferred_element_type=jnp.float32)
        lagged = term if lagged is None else lagged + term
    lagged = lagged * norm_scale
    return lagged.astype(jnp.bfloat16)


def solution(mesh):
    return jax.shard_map(
        local,
        mesh=mesh,
        in_specs=(P("gx", "gy", None), P(), P()),
        out_specs=P("gy", "gx", None),
        check_vma=False,
    )
```

```python
import functools
import math

import jax
import jax.numpy as jnp
from jax import lax
from jax.experimental import pallas as pl
from jax.experimental.pallas import tpu as pltpu
from jax.sharding import PartitionSpec as P

SAMPLES = 8192
LAGS = 512


def inverse_table(kept_bins):
    fine_count = 32
    coarse_count = LAGS // fine_count

    def angles(index):
        return jnp.mod(kept_bins[:, None] * index[None, :], SAMPLES).astype(jnp.float32) * (
            2.0 * math.pi / SAMPLES
        )

    fine = angles(jnp.arange(fine_count, dtype=jnp.int32))[:, None, :]
    coarse = angles(fine_count * jnp.arange(coarse_count, dtype=jnp.int32) - LAGS // 2)[:, :, None]
    cos_f, sin_f, cos_c, sin_c = jnp.cos(fine), jnp.sin(fine), jnp.cos(coarse), jnp.sin(coarse)
    cos_t = (cos_f * cos_c - sin_f * sin_c).reshape(kept_bins.shape[0], LAGS)
    sin_t = (sin_f * cos_c + cos_f * sin_c).reshape(kept_bins.shape[0], LAGS)
    return jnp.stack([cos_t, -sin_t], axis=0).astype(jnp.bfloat16)


def whiten(spectra):
    mean_power = jnp.mean(spectra * spectra, axis=-1, keepdims=True)
    return (spectra * lax.rsqrt(mean_power + 1e-06)).astype(jnp.bfloat16)


def cross_kernel(offsets_ref, base_ref, white_ref, out_ref, *, group, own_count, half):
    step = pl.program_id(0)
    base = base_ref[0]

    def one_offset(i, carry):
        shift = offsets_ref[step * group + i]
        for c in range(own_count):
            a = white_ref[base + c].astype(jnp.float32)
            b = white_ref[base + c + shift].astype(jnp.float32)
            ar, ai, br, bi = a[:half], a[half:], b[:half], b[half:]
            out_ref[i, 0, pl.ds(c, 1), :] = jnp.sum(ar * br + ai * bi, axis=0, keepdims=True)
            out_ref[i, 1, pl.ds(c, 1), :] = jnp.sum(ai * br - ar * bi, axis=0, keepdims=True)
        return carry

    lax.fori_loop(0, group, one_offset, 0)


def cross_spectra(white_all, pair_offsets, base, own_count):
    rows, bins = white_all.shape[1], white_all.shape[2]
    band_span = pair_offsets.shape[0]
    group = math.gcd(band_span, 8)
    kernel = functools.partial(cross_kernel, group=group, own_count=own_count, half=rows // 2)
    return pl.pallas_call(
        kernel,
        grid_spec=pltpu.PrefetchScalarGridSpec(
            num_scalar_prefetch=2,
            grid=(band_span // group,),
            in_specs=[pl.BlockSpec(white_all.shape, lambda g, offs, b: (0, 0, 0))],
            out_specs=pl.BlockSpec((group, 2, own_count, bins), lambda g, offs, b: (g, 0, 0, 0)),
        ),
        out_shape=jax.ShapeDtypeStruct((band_span, 2, own_count, bins), jnp.float32),
        compiler_params=pltpu.CompilerParams(vmem_limit_bytes=48 * 1024 * 1024),
        cost_estimate=pl.CostEstimate(
            flops=8 * band_span * own_count * rows * bins,
            transcendentals=0,
            bytes_accessed=white_all.size * 4 + band_span * 2 * own_count * bins * 4,
        ),
    )(pair_offsets, base, white_all)


def small_table(kept_bins, rows):
    fine_count = 1 << ((rows.bit_length() - 1) // 2)
    coarse_count = rows // fine_count

    def angles(step, count):
        index = step * jnp.arange(count, dtype=jnp.int32)
        return jnp.mod(index[:, None] * kept_bins[None, :], SAMPLES).astype(jnp.float32) * (
            2.0 * math.pi / SAMPLES
        )

    fine = angles(1, fine_count)[None, :, :]
    coarse = angles(fine_count, coarse_count)[:, None, :]
    cos_f, sin_f, cos_c, sin_c = jnp.cos(fine), jnp.sin(fine), jnp.cos(coarse), jnp.sin(coarse)
    cos_t = cos_f * cos_c - sin_f * sin_c
    sin_t = sin_f * cos_c + cos_f * sin_c
    table = jnp.concatenate([cos_t, -sin_t], axis=-1)
    return table.reshape(rows, 2 * kept_bins.shape[0]).astype(jnp.bfloat16)


def forward_spectra(record_rows, kept_bins):
    row_count, samples = record_rows.shape
    bin_count = kept_bins.shape[0]
    block_count = 4
    block_len = samples // block_count
    prod = jnp.dot(
        record_rows.reshape(row_count * block_count, block_len),
        small_table(kept_bins, block_len),
        preferred_element_type=jnp.float32,
    ).reshape(row_count, block_count, 2, bin_count)
    turns = jnp.mod(
        jnp.arange(block_count, dtype=jnp.int32)[:, None] * jnp.mod(kept_bins, block_count)[None, :],
        block_count,
    ).astype(jnp.float32) * (2.0 * math.pi / block_count)
    tw_re = jnp.round(jnp.cos(turns))[None]
    tw_im = jnp.round(-jnp.sin(turns))[None]
    p_re, p_im = prod[:, :, 0], prod[:, :, 1]
    real_part = jnp.sum(tw_re * p_re - tw_im * p_im, axis=1)
    imag_part = jnp.sum(tw_re * p_im + tw_im * p_re, axis=1)
    return jnp.concatenate([real_part, imag_part], axis=-1)


def local(records, kept_bins, pair_offsets):
    ch_dev, win_dev, samples = records.shape
    bin_count = kept_bins.shape[0]
    band_span = pair_offsets.shape[0]
    spectra = forward_spectra(records.reshape(ch_dev * win_dev, samples), kept_bins)
    white = whiten(spectra).reshape(ch_dev, win_dev, 2, bin_count)
    gy_count = lax.axis_size("gy")
    shard_bins = bin_count // gy_count
    me = lax.axis_index("gy")
    slots = []
    for shift in range(gy_count):
        dest = lax.rem(me + shift, gy_count)
        piece = lax.dynamic_slice_in_dim(white, dest * shard_bins, shard_bins, 3)
        if shift:
            piece = lax.ppermute(piece, "gy", perm=[(src, (src + shift) % gy_count) for src in range(gy_count)])
        slots.append(piece)
    freq_white = jnp.concatenate(slots, axis=1)
    windows = freq_white.shape[1]
    rows_white = jnp.transpose(freq_white, (0, 2, 1, 3)).reshape(ch_dev, 2 * windows, shard_bins)
    gx_count = lax.axis_size("gx")
    needed = -(-band_span // ch_dev)
    blocks = [rows_white]
    for shift in range(1, min(needed, gx_count - 1) + 1):
        pairs = [(src, src - shift) for src in range(shift, gx_count)]
        blocks.append(lax.ppermute(rows_white, "gx", perm=pairs))
    missing = needed + 1 - len(blocks)
    if missing > 0:
        blocks.append(jnp.zeros((missing * ch_dev,) + rows_white.shape[1:], rows_white.dtype))
    padded = jnp.concatenate(blocks, axis=0).astype(jnp.float32)
    base = jnp.zeros((1,), jnp.int32)
    gy_count = lax.axis_size("gy")
    off_dev = band_span // gy_count
    me = lax.axis_index("gy")
    offsets = pair_offsets.astype(jnp.int32)
    inverse = jnp.transpose(inverse_table(kept_bins).reshape(2, gy_count, shard_bins, LAGS), (1, 0, 2, 3))
    norm_scale = 0.5 / math.sqrt(windows * bin_count)
    lagged = None
    for shift in list(range(1, gy_count)) + [0]:
        dest = lax.rem(me + shift, gy_count)
        part = cross_spectra(
            padded, lax.dynamic_slice_in_dim(offsets, dest * off_dev, off_dev), base, ch_dev
        ).astype(jnp.bfloat16)
        if shift:
            pairs = [(src, (src + shift) % gy_count) for src in range(gy_count)]
            part = lax.ppermute(part, "gy", perm=pairs)
        origin = lax.rem(me + gy_count - shift, gy_count)
        rows = lax.dynamic_index_in_dim(inverse, origin, 0, keepdims=False)
        term = jnp.einsum("opck,pkl->ocl", part, rows, preferred_element_type=jnp.float32)
        lagged = term if lagged is None else lagged + term
    lagged = lagged * norm_scale
    return lagged.astype(jnp.bfloat16)


def solution(mesh):
    return jax.shard_map(
        local,
        mesh=mesh,
        in_specs=(P("gx", "gy", None), P(), P()),
        out_specs=P("gy", "gx", None),
        check_vma=False,
    )
```

```python
import functools
import math

import jax
import jax.numpy as jnp
from jax import lax
from jax.experimental import pallas as pl
from jax.experimental.pallas import tpu as pltpu
from jax.sharding import PartitionSpec as P

SAMPLES = 8192
LAGS = 512


def inverse_table(kept_bins):
    fine_count = 32
    coarse_count = LAGS // fine_count

    def angles(index):
        return jnp.mod(kept_bins[:, None] * index[None, :], SAMPLES).astype(jnp.float32) * (
            2.0 * math.pi / SAMPLES
        )

    fine = angles(jnp.arange(fine_count, dtype=jnp.int32))[:, None, :]
    coarse = angles(fine_count * jnp.arange(coarse_count, dtype=jnp.int32) - LAGS // 2)[:, :, None]
    cos_f, sin_f, cos_c, sin_c = jnp.cos(fine), jnp.sin(fine), jnp.cos(coarse), jnp.sin(coarse)
    cos_t = (cos_f * cos_c - sin_f * sin_c).reshape(kept_bins.shape[0], LAGS)
    sin_t = (sin_f * cos_c + cos_f * sin_c).reshape(kept_bins.shape[0], LAGS)
    return jnp.stack([cos_t, -sin_t], axis=0).astype(jnp.bfloat16)


def whiten(spectra):
    mean_power = jnp.mean(spectra * spectra, axis=-1, keepdims=True)
    return (spectra * lax.rsqrt(mean_power + 1e-06)).astype(jnp.bfloat16)


def cross_kernel(offsets_ref, base_ref, white_ref, out_ref, *, group, own_count, half):
    step = pl.program_id(0)
    base = base_ref[0]

    def one_offset(i, carry):
        shift = offsets_ref[step * group + i]
        for c in range(own_count):
            a = white_ref[base + c].astype(jnp.float32)
            b = white_ref[base + c + shift].astype(jnp.float32)
            ar, ai, br, bi = a[:half], a[half:], b[:half], b[half:]
            out_ref[i, 0, pl.ds(c, 1), :] = jnp.sum(ar * br + ai * bi, axis=0, keepdims=True)
            out_ref[i, 1, pl.ds(c, 1), :] = jnp.sum(ai * br - ar * bi, axis=0, keepdims=True)
        return carry

    lax.fori_loop(0, group, one_offset, 0)


def cross_spectra(white_all, pair_offsets, base, own_count):
    rows, bins = white_all.shape[1], white_all.shape[2]
    band_span = pair_offsets.shape[0]
    group = math.gcd(band_span, 8)
    kernel = functools.partial(cross_kernel, group=group, own_count=own_count, half=rows // 2)
    return pl.pallas_call(
        kernel,
        grid_spec=pltpu.PrefetchScalarGridSpec(
            num_scalar_prefetch=2,
            grid=(band_span // group,),
            in_specs=[pl.BlockSpec(white_all.shape, lambda g, offs, b: (0, 0, 0))],
            out_specs=pl.BlockSpec((group, 2, own_count, bins), lambda g, offs, b: (g, 0, 0, 0)),
        ),
        out_shape=jax.ShapeDtypeStruct((band_span, 2, own_count, bins), jnp.float32),
        compiler_params=pltpu.CompilerParams(vmem_limit_bytes=48 * 1024 * 1024),
        cost_estimate=pl.CostEstimate(
            flops=1024 * band_span * own_count * rows * bins,
            transcendentals=0,
            bytes_accessed=white_all.size * 4 + band_span * 2 * own_count * bins * 4,
        ),
    )(pair_offsets, base, white_all)


def small_table(kept_bins, rows):
    fine_count = 1 << ((rows.bit_length() - 1) // 2)
    coarse_count = rows // fine_count

    def angles(step, count):
        index = step * jnp.arange(count, dtype=jnp.int32)
        return jnp.mod(index[:, None] * kept_bins[None, :], SAMPLES).astype(jnp.float32) * (
            2.0 * math.pi / SAMPLES
        )

    fine = angles(1, fine_count)[None, :, :]
    coarse = angles(fine_count, coarse_count)[:, None, :]
    cos_f, sin_f, cos_c, sin_c = jnp.cos(fine), jnp.sin(fine), jnp.cos(coarse), jnp.sin(coarse)
    cos_t = cos_f * cos_c - sin_f * sin_c
    sin_t = sin_f * cos_c + cos_f * sin_c
    table = jnp.concatenate([cos_t, -sin_t], axis=-1)
    return table.reshape(rows, 2 * kept_bins.shape[0]).astype(jnp.bfloat16)


def forward_spectra(record_rows, kept_bins):
    row_count, samples = record_rows.shape
    bin_count = kept_bins.shape[0]
    block_count = 4
    block_len = samples // block_count
    prod = jnp.dot(
        record_rows.reshape(row_count * block_count, block_len),
        small_table(kept_bins, block_len),
        preferred_element_type=jnp.float32,
    ).reshape(row_count, block_count, 2, bin_count)
    turns = jnp.mod(
        jnp.arange(block_count, dtype=jnp.int32)[:, None] * jnp.mod(kept_bins, block_count)[None, :],
        block_count,
    ).astype(jnp.float32) * (2.0 * math.pi / block_count)
    tw_re = jnp.round(jnp.cos(turns))[None]
    tw_im = jnp.round(-jnp.sin(turns))[None]
    p_re, p_im = prod[:, :, 0], prod[:, :, 1]
    real_part = jnp.sum(tw_re * p_re - tw_im * p_im, axis=1)
    imag_part = jnp.sum(tw_re * p_im + tw_im * p_re, axis=1)
    return jnp.concatenate([real_part, imag_part], axis=-1)


def local(records, kept_bins, pair_offsets):
    ch_dev, win_dev, samples = records.shape
    bin_count = kept_bins.shape[0]
    band_span = pair_offsets.shape[0]
    spectra = forward_spectra(records.reshape(ch_dev * win_dev, samples), kept_bins)
    white = whiten(spectra).reshape(ch_dev, win_dev, 2, bin_count)
    gy_count = lax.axis_size("gy")
    shard_bins = bin_count // gy_count
    me = lax.axis_index("gy")
    slots = []
    for shift in range(gy_count):
        dest = lax.rem(me + shift, gy_count)
        piece = lax.dynamic_slice_in_dim(white, dest * shard_bins, shard_bins, 3)
        if shift:
            piece = lax.ppermute(piece, "gy", perm=[(src, (src + shift) % gy_count) for src in range(gy_count)])
        slots.append(piece)
    freq_white = jnp.concatenate(slots, axis=1)
    windows = freq_white.shape[1]
    rows_white = jnp.transpose(freq_white, (0, 2, 1, 3)).reshape(ch_dev, 2 * windows, shard_bins)
    gx_count = lax.axis_size("gx")
    needed = -(-band_span // ch_dev)
    blocks = [rows_white]
    for shift in range(1, min(needed, gx_count - 1) + 1):
        pairs = [(src, src - shift) for src in range(shift, gx_count)]
        blocks.append(lax.ppermute(rows_white, "gx", perm=pairs))
    missing = needed + 1 - len(blocks)
    if missing > 0:
        blocks.append(jnp.zeros((missing * ch_dev,) + rows_white.shape[1:], rows_white.dtype))
    padded = jnp.concatenate(blocks, axis=0).astype(jnp.float32)
    base = jnp.zeros((1,), jnp.int32)
    gy_count = lax.axis_size("gy")
    off_dev = band_span // gy_count
    me = lax.axis_index("gy")
    offsets = pair_offsets.astype(jnp.int32)
    inverse = inverse_table(kept_bins)
    norm_scale = 0.5 / math.sqrt(windows * bin_count)
    lagged = None
    for shift in list(range(1, gy_count)) + [0]:
        dest = lax.rem(me + shift, gy_count)
        part = cross_spectra(
            padded, lax.dynamic_slice_in_dim(offsets, dest * off_dev, off_dev), base, ch_dev
        ).astype(jnp.bfloat16)
        if shift:
            pairs = [(src, (src + shift) % gy_count) for src in range(gy_count)]
            part = lax.ppermute(part, "gy", perm=pairs)
        origin = lax.rem(me + gy_count - shift, gy_count)
        rows = lax.dynamic_slice_in_dim(inverse, origin * shard_bins, shard_bins, 1)
        term = jnp.einsum("opck,pkl->ocl", part, rows, preferred_element_type=jnp.float32)
        lagged = term if lagged is None else lagged + term
    lagged = lagged * norm_scale
    return lagged.astype(jnp.bfloat16)


def solution(mesh):
    return jax.shard_map(
        local,
        mesh=mesh,
        in_specs=(P("gx", "gy", None), P(), P()),
        out_specs=P("gy", "gx", None),
        check_vma=False,
    )
```

```python
import functools
import math

import jax
import jax.numpy as jnp
from jax import lax
from jax.experimental import pallas as pl
from jax.experimental.pallas import tpu as pltpu
from jax.sharding import PartitionSpec as P

SAMPLES = 8192
LAGS = 512


def inverse_table(kept_bins):
    fine_count = 32
    coarse_count = LAGS // fine_count

    def angles(index):
        return jnp.mod(kept_bins[:, None] * index[None, :], SAMPLES).astype(jnp.float32) * (
            2.0 * math.pi / SAMPLES
        )

    fine = angles(jnp.arange(fine_count, dtype=jnp.int32))[:, None, :]
    coarse = angles(fine_count * jnp.arange(coarse_count, dtype=jnp.int32) - LAGS // 2)[:, :, None]
    cos_f, sin_f, cos_c, sin_c = jnp.cos(fine), jnp.sin(fine), jnp.cos(coarse), jnp.sin(coarse)
    cos_t = (cos_f * cos_c - sin_f * sin_c).reshape(kept_bins.shape[0], LAGS)
    sin_t = (sin_f * cos_c + cos_f * sin_c).reshape(kept_bins.shape[0], LAGS)
    return jnp.stack([cos_t, -sin_t], axis=0).astype(jnp.bfloat16)


def whiten(spectra):
    mean_power = jnp.mean(spectra * spectra, axis=-1, keepdims=True)
    return (spectra * lax.rsqrt(mean_power + 1e-06)).astype(jnp.bfloat16)


def cross_kernel(offsets_ref, base_ref, white_ref, out_ref, *, group, own_count, half):
    step = pl.program_id(0)
    base = base_ref[0]

    def one_offset(i, carry):
        shift = offsets_ref[step * group + i]
        for c in range(own_count):
            a = white_ref[base + c].astype(jnp.float32)
            b = white_ref[base + c + shift].astype(jnp.float32)
            ar, ai, br, bi = a[:half], a[half:], b[:half], b[half:]
            out_ref[i, 0, pl.ds(c, 1), :] = jnp.sum(ar * br + ai * bi, axis=0, keepdims=True)
            out_ref[i, 1, pl.ds(c, 1), :] = jnp.sum(ai * br - ar * bi, axis=0, keepdims=True)
        return carry

    lax.fori_loop(0, group, one_offset, 0)


def cross_spectra(white_all, pair_offsets, base, own_count):
    rows, bins = white_all.shape[1], white_all.shape[2]
    band_span = pair_offsets.shape[0]
    group = math.gcd(band_span, 8)
    kernel = functools.partial(cross_kernel, group=group, own_count=own_count, half=rows // 2)
    return pl.pallas_call(
        kernel,
        grid_spec=pltpu.PrefetchScalarGridSpec(
            num_scalar_prefetch=2,
            grid=(band_span // group,),
            in_specs=[pl.BlockSpec(white_all.shape, lambda g, offs, b: (0, 0, 0))],
            out_specs=pl.BlockSpec((group, 2, own_count, bins), lambda g, offs, b: (g, 0, 0, 0)),
        ),
        out_shape=jax.ShapeDtypeStruct((band_span, 2, own_count, bins), jnp.float32),
        compiler_params=pltpu.CompilerParams(vmem_limit_bytes=48 * 1024 * 1024),
        cost_estimate=pl.CostEstimate(
            flops=1024 * band_span * own_count * rows * bins,
            transcendentals=0,
            bytes_accessed=white_all.size * 4 + band_span * 2 * own_count * bins * 4,
        ),
    )(pair_offsets, base, white_all)


def small_table(kept_bins, rows):
    fine_count = 1 << ((rows.bit_length() - 1) // 2)
    coarse_count = rows // fine_count

    def angles(step, count):
        index = step * jnp.arange(count, dtype=jnp.int32)
        return jnp.mod(index[:, None] * kept_bins[None, :], SAMPLES).astype(jnp.float32) * (
            2.0 * math.pi / SAMPLES
        )

    fine = angles(1, fine_count)[None, :, :]
    coarse = angles(fine_count, coarse_count)[:, None, :]
    cos_f, sin_f, cos_c, sin_c = jnp.cos(fine), jnp.sin(fine), jnp.cos(coarse), jnp.sin(coarse)
    cos_t = cos_f * cos_c - sin_f * sin_c
    sin_t = sin_f * cos_c + cos_f * sin_c
    table = jnp.concatenate([cos_t, -sin_t], axis=-1)
    return table.reshape(rows, 2 * kept_bins.shape[0]).astype(jnp.bfloat16)


def forward_spectra(record_rows, kept_bins):
    row_count, samples = record_rows.shape
    bin_count = kept_bins.shape[0]
    block_count = 4
    block_len = samples // block_count
    prod = jnp.dot(
        record_rows.reshape(row_count * block_count, block_len),
        small_table(kept_bins, block_len),
        preferred_element_type=jnp.float32,
    ).reshape(row_count, block_count, 2, bin_count)
    turns = jnp.mod(
        jnp.arange(block_count, dtype=jnp.int32)[:, None] * jnp.mod(kept_bins, block_count)[None, :],
        block_count,
    ).astype(jnp.float32) * (2.0 * math.pi / block_count)
    tw_re = jnp.round(jnp.cos(turns))[None]
    tw_im = jnp.round(-jnp.sin(turns))[None]
    p_re, p_im = prod[:, :, 0], prod[:, :, 1]
    real_part = jnp.sum(tw_re * p_re - tw_im * p_im, axis=1)
    imag_part = jnp.sum(tw_re * p_im + tw_im * p_re, axis=1)
    return jnp.concatenate([real_part, imag_part], axis=-1)


def local(records, kept_bins, pair_offsets):
    ch_dev, win_dev, samples = records.shape
    bin_count = kept_bins.shape[0]
    band_span = pair_offsets.shape[0]
    spectra = forward_spectra(records.reshape(ch_dev * win_dev, samples), kept_bins)
    white = whiten(spectra).reshape(ch_dev, win_dev, 2, bin_count)
    gy_count = lax.axis_size("gy")
    shard_bins = bin_count // gy_count
    me = lax.axis_index("gy")
    slots = []
    for shift in range(gy_count):
        dest = lax.rem(me + shift, gy_count)
        piece = lax.dynamic_slice_in_dim(white, dest * shard_bins, shard_bins, 3)
        if shift:
            piece = lax.ppermute(piece, "gy", perm=[(src, (src + shift) % gy_count) for src in range(gy_count)])
        slots.append(piece)
    freq_white = jnp.concatenate(slots, axis=1)
    windows = freq_white.shape[1]
    rows_white = jnp.transpose(freq_white, (0, 2, 1, 3)).reshape(ch_dev, 2 * windows, shard_bins)
    gx_count = lax.axis_size("gx")
    needed = -(-band_span // ch_dev)
    blocks = [rows_white]
    for shift in range(1, min(needed, gx_count - 1) + 1):
        pairs = [(src, src - shift) for src in range(shift, gx_count)]
        blocks.append(lax.ppermute(rows_white, "gx", perm=pairs))
    missing = needed + 1 - len(blocks)
    if missing > 0:
        blocks.append(jnp.zeros((missing * ch_dev,) + rows_white.shape[1:], rows_white.dtype))
    padded = jnp.concatenate(blocks, axis=0).astype(jnp.float32)
    base = jnp.zeros((1,), jnp.int32)
    gy_count = lax.axis_size("gy")
    off_dev = band_span // gy_count
    me = lax.axis_index("gy")
    offsets = pair_offsets.astype(jnp.int32)
    inverse = inverse_table(kept_bins)
    norm_scale = 0.5 / math.sqrt(windows * bin_count)
    lagged = None
    far_shift = gy_count // 2
    for shift in [far_shift] + [s for s in range(1, gy_count) if s != far_shift] + [0]:
        dest = lax.rem(me + shift, gy_count)
        part = cross_spectra(
            padded, lax.dynamic_slice_in_dim(offsets, dest * off_dev, off_dev), base, ch_dev
        ).astype(jnp.bfloat16)
        if shift:
            pairs = [(src, (src + shift) % gy_count) for src in range(gy_count)]
            part = lax.ppermute(part, "gy", perm=pairs)
        origin = lax.rem(me + gy_count - shift, gy_count)
        rows = lax.dynamic_slice_in_dim(inverse, origin * shard_bins, shard_bins, 1)
        term = jnp.einsum("opck,pkl->ocl", part, rows, preferred_element_type=jnp.float32)
        lagged = term if lagged is None else lagged + term
    lagged = lagged * norm_scale
    return lagged.astype(jnp.bfloat16)


def solution(mesh):
    return jax.shard_map(
        local,
        mesh=mesh,
        in_specs=(P("gx", "gy", None), P(), P()),
        out_specs=P("gy", "gx", None),
        check_vma=False,
    )
```

```python
import functools
import math

import jax
import jax.numpy as jnp
from jax import lax
from jax.experimental import pallas as pl
from jax.experimental.pallas import tpu as pltpu
from jax.sharding import PartitionSpec as P

SAMPLES = 8192
LAGS = 512


def inverse_table(kept_bins):
    fine_count = 32
    coarse_count = LAGS // fine_count

    def angles(index):
        return jnp.mod(kept_bins[:, None] * index[None, :], SAMPLES).astype(jnp.float32) * (
            2.0 * math.pi / SAMPLES
        )

    fine = angles(jnp.arange(fine_count, dtype=jnp.int32))[:, None, :]
    coarse = angles(fine_count * jnp.arange(coarse_count, dtype=jnp.int32) - LAGS // 2)[:, :, None]
    cos_f, sin_f, cos_c, sin_c = jnp.cos(fine), jnp.sin(fine), jnp.cos(coarse), jnp.sin(coarse)
    cos_t = (cos_f * cos_c - sin_f * sin_c).reshape(kept_bins.shape[0], LAGS)
    sin_t = (sin_f * cos_c + cos_f * sin_c).reshape(kept_bins.shape[0], LAGS)
    return jnp.stack([cos_t, -sin_t], axis=0).astype(jnp.bfloat16)


def whiten(spectra):
    mean_power = jnp.mean(spectra * spectra, axis=-1, keepdims=True)
    return (spectra * lax.rsqrt(mean_power + 1e-06)).astype(jnp.bfloat16)


def cross_kernel(offsets_ref, base_ref, white_ref, out_ref, *, group, own_count, half):
    step = pl.program_id(0)
    base = base_ref[0]

    def one_offset(i, carry):
        shift = offsets_ref[step * group + i]
        real_rows, imag_rows = [], []
        for c in range(own_count):
            a = white_ref[base + c].astype(jnp.float32)
            b = white_ref[base + c + shift].astype(jnp.float32)
            ar, ai, br, bi = a[:half], a[half:], b[:half], b[half:]
            real_rows.append(jnp.sum(ar * br + ai * bi, axis=0, keepdims=True))
            imag_rows.append(jnp.sum(ai * br - ar * bi, axis=0, keepdims=True))
        out_ref[i, 0] = jnp.concatenate(real_rows, axis=0).astype(out_ref.dtype)
        out_ref[i, 1] = jnp.concatenate(imag_rows, axis=0).astype(out_ref.dtype)
        return carry

    lax.fori_loop(0, group, one_offset, 0)


def cross_spectra(white_all, pair_offsets, base, own_count):
    rows, bins = white_all.shape[1], white_all.shape[2]
    band_span = pair_offsets.shape[0]
    group = math.gcd(band_span, 8)
    kernel = functools.partial(cross_kernel, group=group, own_count=own_count, half=rows // 2)
    return pl.pallas_call(
        kernel,
        grid_spec=pltpu.PrefetchScalarGridSpec(
            num_scalar_prefetch=2,
            grid=(band_span // group,),
            in_specs=[pl.BlockSpec(white_all.shape, lambda g, offs, b: (0, 0, 0))],
            out_specs=pl.BlockSpec((group, 2, own_count, bins), lambda g, offs, b: (g, 0, 0, 0)),
        ),
        out_shape=jax.ShapeDtypeStruct((band_span, 2, own_count, bins), jnp.bfloat16),
        compiler_params=pltpu.CompilerParams(vmem_limit_bytes=48 * 1024 * 1024),
        cost_estimate=pl.CostEstimate(
            flops=1024 * band_span * own_count * rows * bins,
            transcendentals=0,
            bytes_accessed=white_all.size * 4 + band_span * 2 * own_count * bins * 4,
        ),
    )(pair_offsets, base, white_all)


def small_table(kept_bins, rows):
    fine_count = 1 << ((rows.bit_length() - 1) // 2)
    coarse_count = rows // fine_count

    def angles(step, count):
        index = step * jnp.arange(count, dtype=jnp.int32)
        return jnp.mod(index[:, None] * kept_bins[None, :], SAMPLES).astype(jnp.float32) * (
            2.0 * math.pi / SAMPLES
        )

    fine = angles(1, fine_count)[None, :, :]
    coarse = angles(fine_count, coarse_count)[:, None, :]
    cos_f, sin_f, cos_c, sin_c = jnp.cos(fine), jnp.sin(fine), jnp.cos(coarse), jnp.sin(coarse)
    cos_t = cos_f * cos_c - sin_f * sin_c
    sin_t = sin_f * cos_c + cos_f * sin_c
    table = jnp.concatenate([cos_t, -sin_t], axis=-1)
    return table.reshape(rows, 2 * kept_bins.shape[0]).astype(jnp.bfloat16)


def forward_spectra(record_rows, kept_bins):
    row_count, samples = record_rows.shape
    bin_count = kept_bins.shape[0]
    block_count = 4
    block_len = samples // block_count
    prod = jnp.dot(
        record_rows.reshape(row_count * block_count, block_len),
        small_table(kept_bins, block_len),
        preferred_element_type=jnp.float32,
    ).reshape(row_count, block_count, 2, bin_count)
    turns = jnp.mod(
        jnp.arange(block_count, dtype=jnp.int32)[:, None] * jnp.mod(kept_bins, block_count)[None, :],
        block_count,
    ).astype(jnp.float32) * (2.0 * math.pi / block_count)
    tw_re = jnp.round(jnp.cos(turns))[None]
    tw_im = jnp.round(-jnp.sin(turns))[None]
    p_re, p_im = prod[:, :, 0], prod[:, :, 1]
    real_part = jnp.sum(tw_re * p_re - tw_im * p_im, axis=1)
    imag_part = jnp.sum(tw_re * p_im + tw_im * p_re, axis=1)
    return jnp.concatenate([real_part, imag_part], axis=-1)


def local(records, kept_bins, pair_offsets):
    ch_dev, win_dev, samples = records.shape
    bin_count = kept_bins.shape[0]
    band_span = pair_offsets.shape[0]
    spectra = forward_spectra(records.reshape(ch_dev * win_dev, samples), kept_bins)
    white = whiten(spectra).reshape(ch_dev, win_dev, 2, bin_count)
    gy_count = lax.axis_size("gy")
    shard_bins = bin_count // gy_count
    me = lax.axis_index("gy")
    slots = []
    for shift in range(gy_count):
        dest = lax.rem(me + shift, gy_count)
        piece = lax.dynamic_slice_in_dim(white, dest * shard_bins, shard_bins, 3)
        if shift:
            piece = lax.ppermute(piece, "gy", perm=[(src, (src + shift) % gy_count) for src in range(gy_count)])
        slots.append(piece)
    freq_white = jnp.concatenate(slots, axis=1)
    windows = freq_white.shape[1]
    rows_white = jnp.transpose(freq_white, (0, 2, 1, 3)).reshape(ch_dev, 2 * windows, shard_bins)
    gx_count = lax.axis_size("gx")
    needed = -(-band_span // ch_dev)
    blocks = [rows_white]
    for shift in range(1, min(needed, gx_count - 1) + 1):
        pairs = [(src, src - shift) for src in range(shift, gx_count)]
        blocks.append(lax.ppermute(rows_white, "gx", perm=pairs))
    missing = needed + 1 - len(blocks)
    if missing > 0:
        blocks.append(jnp.zeros((missing * ch_dev,) + rows_white.shape[1:], rows_white.dtype))
    padded = jnp.concatenate(blocks, axis=0).astype(jnp.float32)
    base = jnp.zeros((1,), jnp.int32)
    gy_count = lax.axis_size("gy")
    off_dev = band_span // gy_count
    me = lax.axis_index("gy")
    offsets = pair_offsets.astype(jnp.int32)
    inverse = inverse_table(kept_bins)
    norm_scale = 0.5 / math.sqrt(windows * bin_count)
    lagged = None
    for shift in list(range(1, gy_count)) + [0]:
        dest = lax.rem(me + shift, gy_count)
        part = cross_spectra(
            padded, lax.dynamic_slice_in_dim(offsets, dest * off_dev, off_dev), base, ch_dev
        ).astype(jnp.bfloat16)
        if shift:
            pairs = [(src, (src + shift) % gy_count) for src in range(gy_count)]
            part = lax.ppermute(part, "gy", perm=pairs)
        origin = lax.rem(me + gy_count - shift, gy_count)
        rows = lax.dynamic_slice_in_dim(inverse, origin * shard_bins, shard_bins, 1)
        term = jnp.einsum("opck,pkl->ocl", part, rows, preferred_element_type=jnp.float32)
        lagged = term if lagged is None else lagged + term
    lagged = lagged * norm_scale
    return lagged.astype(jnp.bfloat16)


def solution(mesh):
    return jax.shard_map(
        local,
        mesh=mesh,
        in_specs=(P("gx", "gy", None), P(), P()),
        out_specs=P("gy", "gx", None),
        check_vma=False,
    )
```
